32 devices in a mesh: kv: 4 (over x, core), blk: 8 (over z, y).
Axes of the slice: x: 2, y: 2, z: 4, core: 2. Of those that a mesh axis runs over, the one named last changes fastest.
Arguments:
- patches: bfloat16 [24, 256, 1408], P('blk'), may hold values from -6 to 6
- merged_grid: int32 [24, 2], P('blk'), may hold values from 1 to 8, as said below
- picture_start: int32 [24], P('blk'), may hold values from 0 to 4095, as said below
- vis_gain: float32 [1408], replicated, may hold values from 0.5 to 2
- vis_qkv: bfloat16 [1408, 3, 1408], P(None, None, 'kv'), may hold values from -2 to 2
- vis_out: bfloat16 [1408, 1408], P('kv'), may hold values from -0.15625 to 0.15625
- merge_weight: bfloat16 [1408, 4096], P(None, 'kv'), may hold values from -0.15625 to 0.15625
- text_embed: bfloat16 [4096, 4096], P('blk', 'kv'), may hold values from -6 to 6
- dec_gain: float32 [4096], replicated, may hold values from 0.1 to 1.9
- w_query: bfloat16 [4096, 2048], P(None, 'kv'), may hold values from -2 to 2
- w_keyval: bfloat16 [4096, 2, 1024], P(None, None, 'kv'), may hold values from -2 to 2
- w_out: bfloat16 [2048, 4096], P('kv'), may hold values from -0.5 to 0.5
- req_lengths: int32 [8], replicated, may hold values from 1 to 2048, as said below
- final_gain: float32 [4096], P('kv'), may hold values from 0.1 to 1.9
- table: bfloat16 [8192, 4096], P('blk', 'kv'), may hold values from -0.25 to 0.25
Outputs:
- hidden: bfloat16 [4096, 4096], P('blk', 'kv')
- last_norm: bfloat16 [8, 4096], P(None, 'kv')
- max_logit: float32 [8], replicated
The draws below stay inside these ranges and needn't reach their ends.
Inputs may be any that keep to these rules, and one draw needn't show every extreme that they name: `merged_grid`: some picture has a grid of 8 x 8 merged cells. Picture p's merged rows go to consecutive positions from picture_start[p] on, all inside the block of 512 positions with block index p // 3; pictures never share a position. `req_lengths`: the first request ends inside positions 512 to 1023; the second request holds 2048 positions, more than any other.
All inputs are finite; a program needn't handle non-finite values.
Results may differ from the reference program's by a relative error of at most 0.017.
Values may be sent and summed in bfloat16 or wider, within the bound.
No kernel may reach another device: no remote copies, remote signals or barrier semaphores. Data moves between devices by JAX's collectives and lax.ppermute only.
A program may use at most 128 MiB of HBM per device.

```python
import math
import jax
import jax.numpy as jnp
from jax import lax

VD = 1408
VHEADS = 16
VHD = 88
D = 4096
QHEADS = 16
KVHEADS = 8
HD = 128
TOK_DEV = 512
PICS_DEV = 3
GRID_MAX = 8
REQS = 8
MERGED_MAX = 64
PATCH_MAX = 256
TOKENS = 4096
PICTURES = 24
VOCAB = 8192
N_KV = 4


def picture_grid(key):
    sides = jax.random.randint(jax.random.fold_in(key, 11), (PICTURES, 2), 1, GRID_MAX + 1)
    sides = sides.at[0].set(GRID_MAX)
    return sides.astype(jnp.int32)


def draw_merged_grid(key, part):
    return picture_grid(key)


def draw_picture_start(key, part):
    sides = picture_grid(key)
    cell_count = sides[:, 0] * sides[:, 1]
    slot_rows = TOK_DEV // PICS_DEV
    picture_index = jnp.arange(PICTURES, dtype=jnp.int32)
    offset = jax.random.randint(jax.random.fold_in(key, 23), (PICTURES,), 0, slot_rows - cell_count + 1)
    return (picture_index // PICS_DEV * TOK_DEV + picture_index % PICS_DEV * slot_rows + offset).astype(jnp.int32)


def draw_req_lengths(key, part):
    first_len = TOK_DEV + jax.random.randint(jax.random.fold_in(key, 401), (1,), TOK_DEV // 4, 3 * TOK_DEV // 4 + 1)
    second_len = jnp.full((1,), TOKENS // 2, jnp.int32)
    others = REQS - 2
    rest_total = TOKENS - TOKENS // 2 - first_len[0]
    extra = rest_total - others
    shares = jax.random.randint(jax.random.fold_in(key, 403), (others,), 1, 9)
    portion = extra * shares // jnp.sum(shares)
    portion = portion.at[others - 1].add(extra - jnp.sum(portion))
    return jnp.concatenate([first_len, second_len, 1 + portion]).astype(jnp.int32)


def draw_patches(key, part):
    noise = jax.random.normal(jax.random.fold_in(key, 207), (PICTURES, PATCH_MAX, VD), jnp.float32)
    values = noise
    return jnp.clip(values, -6.0, 6.0).astype(jnp.bfloat16)


def draw_vis_qkv(key, part):
    base = jnp.clip(jax.random.normal(jax.random.fold_in(key, 213), (VD, 3, VHEADS * VHD), jnp.float32), -6.0, 6.0) * VD ** (-0.5)
    return jnp.clip(base, -2.0, 2.0).astype(jnp.bfloat16)


def draw_text_embed(key, part):
    noise = jax.random.normal(jax.random.fold_in(key, 307), (TOKENS, D), jnp.float32)
    values = noise
    return jnp.clip(values, -6.0, 6.0).astype(jnp.bfloat16)


def draw_w_query(key, part):
    base = jnp.clip(jax.random.normal(jax.random.fold_in(key, 317), (D, QHEADS * HD), jnp.float32), -6.0, 6.0) * D ** (-0.5)
    return jnp.clip(base, -2.0, 2.0).astype(jnp.bfloat16)


def draw_w_keyval(key, part):
    base = jnp.clip(jax.random.normal(jax.random.fold_in(key, 319), (D, 2, KVHEADS * HD), jnp.float32), -6.0, 6.0) * D ** (-0.5)
    return jnp.clip(base, -2.0, 2.0).astype(jnp.bfloat16)


def levels(own_key, dims, split, least, top_value):
    loudness, own = 1.0, jax.random.fold_in(own_key, 6)
    for dim, shards_of in split:
        draws = jnp.exp(jax.random.uniform(jax.random.fold_in(own, dim), (shards_of,), jnp.float32, least / len(split), top_value / len(split)))
        loudness = loudness * jnp.repeat(draws, dims[dim] // shards_of).reshape([-1 if axis == dim else 1 for axis in range(len(dims))])
    return loudness


def scatter_about(own_key, extent, scale, bound, pieces=(), kind=jnp.bfloat16):
    values = scale * jax.random.normal(own_key, extent, jnp.float32)
    if pieces:
        values = values * levels(own_key, extent, pieces, -0.22, 0.18)
    return jnp.clip(values, -bound, bound).astype(kind)


def setup_inputs(seed: int = 0) -> dict:
    streams_of = jax.random.split(jax.random.key(seed), 16)
    return {
        "patches": draw_patches(jax.random.fold_in(streams_of[15], 71), 0),
        "merged_grid": draw_merged_grid(jax.random.fold_in(streams_of[15], 71), 0),
        "picture_start": draw_picture_start(jax.random.fold_in(streams_of[15], 71), 0),
        "vis_gain": jnp.clip(jnp.exp(jax.random.uniform(streams_of[3], (VD,), jnp.float32, math.log(0.5), math.log(2.0))), 0.5, 2.0),
        "vis_qkv": draw_vis_qkv(jax.random.fold_in(streams_of[15], 71), 0),
        "vis_out": scatter_about(streams_of[5], (VHEADS * VHD, VD), (VHEADS * VHD) ** -0.5, 0.15625, ((0, 4),)),
        "merge_weight": scatter_about(streams_of[6], (VD, D), VD ** -0.5, 0.15625, ((1, 4),)),
        "text_embed": draw_text_embed(jax.random.fold_in(streams_of[15], 71), 0),
        "dec_gain": jnp.clip(1.0 + 0.18 * jax.random.normal(streams_of[8], (D,), jnp.float32), 0.1, 1.9),
        "w_query": draw_w_query(jax.random.fold_in(streams_of[15], 71), 0),
        "w_keyval": draw_w_keyval(jax.random.fold_in(streams_of[15], 71), 0),
        "w_out": scatter_about(streams_of[11], (QHEADS * HD, D), (QHEADS * HD // 16) ** -0.5, 0.5, ((0, 4),)),
        "req_lengths": draw_req_lengths(jax.random.fold_in(streams_of[15], 71), 0),
        "final_gain": jnp.clip(1.0 + 0.18 * jax.random.normal(streams_of[13], (D,), jnp.float32), 0.1, 1.9),
        "table": scatter_about(streams_of[14], (VOCAB, D), (D // 9) ** -0.5, 0.25, ((0, 8), (1, 4))),
    }


def layer_norm(inputs, gain):
    centre = lax.optimization_barrier(jnp.mean(inputs, axis=-1, keepdims=True))
    centred = inputs - centre
    spread = lax.optimization_barrier(jnp.mean(centred * centred, axis=-1, keepdims=True))
    return centred * lax.rsqrt(spread + 1e-06) * gain

def rounded(values):
    return lax.optimization_barrier(values.astype(jnp.bfloat16)).astype(jnp.float32)

def rotate(inputs, position):
    half_width = inputs.shape[-1] // 2
    inverse = 500000.0 ** (-jnp.arange(half_width, dtype=jnp.float32) * 2.0 / inputs.shape[-1])
    angles = position.astype(jnp.float32)[:, None] * inverse[None, :]
    cosine = jnp.cos(angles)[:, None, :]
    sine = jnp.sin(angles)[:, None, :]
    first = inputs[..., :half_width]
    second = inputs[..., half_width:]
    return jnp.concatenate([first * cosine - second * sine, second * cosine + first * sine], axis=-1)

def request_info(row_index, req_lengths):
    ends_at = jnp.cumsum(req_lengths).astype(jnp.int32)
    starts_at = ends_at - req_lengths
    request_id = lax.optimization_barrier(jnp.sum((row_index[:, None] >= ends_at[None, :]).astype(jnp.int32), axis=1))
    choose = request_id[:, None] == jnp.arange(req_lengths.shape[0], dtype=jnp.int32)[None, :]
    request_begin = lax.optimization_barrier(jnp.sum(jnp.where(choose, starts_at[None, :], 0), axis=1)).astype(jnp.int32)
    return (request_id, request_begin)

def vision_picture(patch_rows, cell_count, vis_gain, vis_qkv, vis_out):
    inputs = patch_rows.astype(jnp.float32)
    normed = layer_norm(inputs, vis_gain).astype(jnp.bfloat16)
    packed = jnp.dot(normed, vis_qkv.reshape(VD, 3 * VHEADS * VHD), preferred_element_type=jnp.float32)
    packed = rounded(packed).reshape(PATCH_MAX, 3, VHEADS, VHD)
    scores = jnp.einsum('qhd,khd->hqk', packed[:, 0], packed[:, 1]) / math.sqrt(VHD)
    valid_cols = jnp.arange(PATCH_MAX, dtype=jnp.int32) < 4 * cell_count
    scores = jnp.where(valid_cols[None, None, :], scores, -1e+30)
    weights = jnp.exp(scores - lax.optimization_barrier(jnp.max(scores, axis=-1, keepdims=True)))
    weight_sum = lax.optimization_barrier(jnp.sum(weights, axis=-1))
    mixed_rows = jnp.einsum('hqk,khd->qhd', rounded(weights), packed[:, 2]) / jnp.transpose(weight_sum)[:, :, None]
    mixed_rows = mixed_rows.astype(jnp.bfloat16).reshape(PATCH_MAX, VHEADS * VHD)
    summed = inputs + jnp.dot(mixed_rows, vis_out, preferred_element_type=jnp.float32)
    return lax.optimization_barrier(jnp.mean(summed.reshape(MERGED_MAX, 4, VD), axis=1)).astype(jnp.bfloat16)

def reference(patches, merged_grid, picture_start, vis_gain, vis_qkv, vis_out, merge_weight, text_embed, dec_gain, w_query, w_keyval, w_out, req_lengths, final_gain, table):
    cell_count = merged_grid[:, 0] * merged_grid[:, 1]
    pooled = lax.map(lambda item: vision_picture(item[0], item[1], vis_gain, vis_qkv, vis_out), (patches, cell_count))
    merged = jnp.dot(pooled.reshape(PICTURES * MERGED_MAX, VD), merge_weight, preferred_element_type=jnp.float32).astype(jnp.bfloat16)
    slot_index = jnp.arange(MERGED_MAX, dtype=jnp.int32)
    target = picture_start[:, None] + slot_index[None, :]
    target = jnp.where(slot_index[None, :] < cell_count[:, None], target, TOKENS).reshape(-1)
    seq_in = text_embed.at[target].set(merged, mode='drop')
    row_ids = jnp.arange(TOKENS, dtype=jnp.int32)
    request_id, request_begin = request_info(row_ids, req_lengths)
    position = row_ids - request_begin
    full_float = seq_in.astype(jnp.float32)
    dec_normed = (full_float * lax.rsqrt(lax.optimization_barrier(jnp.mean(full_float * full_float, axis=-1, keepdims=True)) + 1e-05) * dec_gain).astype(jnp.bfloat16)
    queries = jnp.dot(dec_normed, w_query, preferred_element_type=jnp.float32).reshape(TOKENS, QHEADS, HD)
    queries = rotate(queries, position).astype(jnp.bfloat16)
    key_value = jnp.dot(dec_normed, w_keyval.reshape(D, 2 * KVHEADS * HD), preferred_element_type=jnp.float32).reshape(TOKENS, 2, KVHEADS, HD)
    key_rows = rotate(key_value[:, 0], position).astype(jnp.bfloat16)
    value_rows = key_value[:, 1].astype(jnp.bfloat16)
    per_group = QHEADS // KVHEADS

    def one_head(head_index):
        query_head = lax.dynamic_index_in_dim(queries, head_index, 1, keepdims=False)
        key_head = lax.dynamic_index_in_dim(key_rows, head_index // per_group, 1, keepdims=False)
        value_head = lax.dynamic_index_in_dim(value_rows, head_index // per_group, 1, keepdims=False)

        def one_block(block_index):
            first_row = block_index * TOK_DEV
            query_part = lax.dynamic_slice_in_dim(query_head, first_row, TOK_DEV, 0)
            query_req = lax.dynamic_slice_in_dim(request_id, first_row, TOK_DEV, 0)
            query_ids = first_row + jnp.arange(TOK_DEV, dtype=jnp.int32)
            scores = jnp.dot(query_part, key_head.T, preferred_element_type=jnp.float32) / math.sqrt(HD)
            allowed = (row_ids[None, :] <= query_ids[:, None]) & (request_id[None, :] == query_req[:, None])
            scores = jnp.where(allowed, scores, -1e+30)
            weights = jnp.exp(scores - lax.optimization_barrier(jnp.max(scores, axis=-1, keepdims=True)))
            weight_sum = lax.optimization_barrier(jnp.sum(weights, axis=-1))
            mixed_rows = jnp.dot(weights.astype(jnp.bfloat16), value_head, preferred_element_type=jnp.float32) / weight_sum[:, None]
            return mixed_rows.astype(jnp.bfloat16)
        return lax.map(one_block, jnp.arange(TOKENS // TOK_DEV, dtype=jnp.int32))
    context = lax.map(one_head, jnp.arange(QHEADS, dtype=jnp.int32))
    context = jnp.transpose(context.reshape(QHEADS, TOKENS, HD), (1, 0, 2)).reshape(TOKENS, QHEADS * HD)
    group_width = QHEADS * HD // N_KV

    def add_group(running, group_index):
        part_sum = jnp.dot(lax.dynamic_slice_in_dim(context, group_index * group_width, group_width, 1), lax.dynamic_slice_in_dim(w_out, group_index * group_width, group_width, 0), preferred_element_type=jnp.float32)
        return (running + rounded(part_sum), None)
    head_total, unused_out = lax.scan(add_group, jnp.zeros((TOKENS, D), jnp.float32), jnp.arange(N_KV, dtype=jnp.int32))
    hidden = (full_float + head_total).astype(jnp.bfloat16)
    last_ids = (jnp.cumsum(req_lengths) - 1).astype(jnp.int32)
    last_row = jnp.take(hidden, last_ids, axis=0).astype(jnp.float32)
    inv_rms = lax.rsqrt(lax.optimization_barrier(jnp.mean(last_row * last_row, axis=-1)) + 1e-05)
    last_norm = (last_row * inv_rms[:, None] * final_gain).astype(jnp.bfloat16)
    scaled = (last_row * final_gain).astype(jnp.bfloat16)
    logits = inv_rms[:, None] * jnp.dot(scaled, table.T, preferred_element_type=jnp.float32)
    max_logit = lax.optimization_barrier(jnp.max(logits, axis=-1))
    return (hidden, last_norm, max_logit)
```

```python
import math

import jax
import jax.numpy as jnp
from jax import lax
from jax.sharding import PartitionSpec as P

VHD = 88
D = 4096
QHEADS = 16
KVHEADS = 8
HD = 128


def layer_norm(inputs, gain):
    centre = jnp.mean(inputs, axis=-1, keepdims=True)
    centred = inputs - centre
    spread = jnp.mean(centred * centred, axis=-1, keepdims=True)
    return centred * lax.rsqrt(spread + 1e-06) * gain


def rotate(inputs, position):
    half_width = inputs.shape[-1] // 2
    inverse = 500000.0 ** (-jnp.arange(half_width, dtype=jnp.float32) * 2.0 / inputs.shape[-1])
    angles = position.astype(jnp.float32)[:, None] * inverse[None, :]
    cosine = jnp.cos(angles)[:, None, :]
    sine = jnp.sin(angles)[:, None, :]
    first = inputs[..., :half_width]
    second = inputs[..., half_width:]
    return jnp.concatenate(
        [first * cosine - second * sine, second * cosine + first * sine], axis=-1
    )


def request_info(row_index, req_lengths):
    ends_at = jnp.cumsum(req_lengths)
    starts_at = ends_at - req_lengths
    request_id = jnp.sum((row_index[:, None] >= ends_at[None, :]).astype(jnp.int32), axis=1)
    choose = request_id[:, None] == jnp.arange(req_lengths.shape[0], dtype=jnp.int32)[None, :]
    request_begin = jnp.sum(jnp.where(choose, starts_at[None, :], 0), axis=1)
    return (request_id, request_begin)


def attend(state, queries, query_ids, query_req, key_part, value_part, key_ids, key_req, root):
    run_max, weight_sum, running = state
    scores = (
        jnp.einsum("tgqd,kgd->tgqk", queries, key_part, preferred_element_type=jnp.float32) / root
    )
    allowed = (key_ids[None, :] <= query_ids[:, None]) & (key_req[None, :] == query_req[:, None])
    allowed = allowed[:, None, None, :]
    scores = jnp.where(allowed, scores, -1e30)
    new_max = jnp.maximum(run_max, jnp.max(scores, axis=-1))
    weights = jnp.where(allowed, jnp.exp(scores - new_max[..., None]), 0.0)
    weight_sum = jnp.sum(weights, axis=-1)
    running = jnp.einsum(
        "tgqk,kgd->tgqd",
        weights.astype(jnp.bfloat16),
        value_part,
        preferred_element_type=jnp.float32,
    )
    return (new_max, weight_sum, running)


def on_device(
    patches,
    merged_grid,
    picture_start,
    vis_gain,
    vis_qkv,
    vis_out,
    merge_weight,
    text_embed,
    dec_gain,
    w_query,
    w_keyval,
    w_out,
    req_lengths,
    final_gain,
    table,
):
    pictures, patch_max, vis_width = patches.shape
    merged_max = patch_max // 4
    vis_cols = vis_qkv.shape[2]
    vis_heads = vis_cols // VHD
    tok_rows, feat_dev = text_embed.shape
    inputs = patches.astype(jnp.float32)
    normed = layer_norm(inputs, vis_gain).astype(jnp.bfloat16)
    packed = jnp.einsum(
        "pnd,dce->pnce", normed, vis_qkv, preferred_element_type=jnp.float32
    ).astype(jnp.bfloat16)
    packed = packed.reshape(pictures, patch_max, 3, vis_heads, VHD)
    scores = jnp.einsum(
        "pqhd,pkhd->phqk", packed[:, :, 0], packed[:, :, 1], preferred_element_type=jnp.float32
    ) / math.sqrt(VHD)
    cell_count = merged_grid[:, 0] * merged_grid[:, 1]
    valid_cols = jnp.arange(patch_max, dtype=jnp.int32)[None, :] < 4 * cell_count[:, None]
    scores = jnp.where(valid_cols[:, None, None, :], scores, -1e30)
    weights = jnp.exp(scores - jnp.max(scores, axis=-1, keepdims=True))
    weight_sum = jnp.sum(weights, axis=-1)
    mixed_rows = jnp.einsum(
        "phqk,pkhd->pqhd",
        weights.astype(jnp.bfloat16),
        packed[:, :, 2],
        preferred_element_type=jnp.float32,
    )
    mixed_rows = (
        (mixed_rows / jnp.transpose(weight_sum, (0, 2, 1))[..., None])
        .astype(jnp.bfloat16)
        .reshape(pictures, patch_max, vis_cols)
    )
    head_part = jnp.einsum("pnc,cd->pnd", mixed_rows, vis_out, preferred_element_type=jnp.float32)
    head_pooled = jnp.mean(head_part.reshape(pictures, merged_max, 4, vis_width), axis=2)
    head_total = lax.psum(head_pooled.astype(jnp.bfloat16), "kv").astype(jnp.float32)
    input_pooled = jnp.mean(inputs.reshape(pictures, merged_max, 4, vis_width), axis=2)
    pooled = (input_pooled + head_total).astype(jnp.bfloat16)
    merged = jnp.einsum(
        "pmd,de->pme", pooled, merge_weight, preferred_element_type=jnp.float32
    ).astype(jnp.bfloat16)
    block_base = lax.axis_index("blk") * tok_rows
    slot_index = jnp.arange(merged_max, dtype=jnp.int32)
    target = picture_start[:, None] + slot_index[None, :] - block_base
    target = jnp.where(slot_index[None, :] < cell_count[:, None], target, -1).reshape(-1)
    local_rows = jnp.arange(tok_rows, dtype=jnp.int32)
    one_hot = local_rows[:, None] == target[None, :]
    placed = jnp.dot(
        one_hot.astype(jnp.bfloat16),
        merged.reshape(pictures * merged_max, feat_dev),
        preferred_element_type=jnp.float32,
    )
    is_vision = jnp.any(one_hot, axis=1)
    seq_in = jnp.where(is_vision[:, None], placed.astype(jnp.bfloat16), text_embed)
    full_rows = lax.all_gather(seq_in, "kv", axis=1, tiled=True)
    full_float = full_rows.astype(jnp.float32)
    dec_normed = (
        full_float
        * lax.rsqrt(jnp.mean(full_float * full_float, axis=-1, keepdims=True) + 1e-05)
        * dec_gain
    ).astype(jnp.bfloat16)
    per_group = QHEADS // KVHEADS
    kv_heads = w_keyval.shape[2] // HD
    row_ids = block_base + local_rows
    request_id, request_begin = request_info(row_ids, req_lengths)
    position = row_ids - request_begin
    query_proj = jnp.dot(dec_normed, w_query, preferred_element_type=jnp.float32).reshape(
        tok_rows, kv_heads * per_group, HD
    )
    query_proj = (
        rotate(query_proj, position)
        .astype(jnp.bfloat16)
        .reshape(tok_rows, kv_heads * per_group * HD)
    )
    key_value = jnp.einsum("td,dce->tce", dec_normed, w_keyval, preferred_element_type=jnp.float32)
    key_rows = (
        rotate(key_value[:, 0].reshape(tok_rows, kv_heads, HD), position)
        .astype(jnp.bfloat16)
        .reshape(tok_rows, kv_heads * HD)
    )
    value_rows = key_value[:, 1].astype(jnp.bfloat16)
    queries = query_proj
    query_req, query_begin = request_info(row_ids, req_lengths)
    queries = queries.reshape(tok_rows, kv_heads, per_group, HD)
    half_rows = tok_rows // 2
    root = math.sqrt(HD)

    def empty_state():
        return (
            jnp.full((half_rows, kv_heads, per_group), -1e30, jnp.float32),
            jnp.zeros((half_rows, kv_heads, per_group), jnp.float32),
            jnp.zeros((half_rows, kv_heads, per_group, HD), jnp.float32),
        )

    carry = (empty_state(), empty_state())
    first_row = jnp.int32(0)
    reqs = req_lengths.shape[0]
    ends_at = jnp.cumsum(req_lengths)
    last_ids = ends_at - 1
    picker = (local_rows[None, :] == (last_ids - block_base)[:, None]).astype(jnp.bfloat16)
    query_last = jnp.dot(picker, query_proj, preferred_element_type=jnp.float32)
    seq_last = jnp.dot(picker, seq_in, preferred_element_type=jnp.float32)
    extras = jnp.concatenate([query_last, seq_last], axis=1).astype(jnp.bfloat16).reshape(-1)
    kv_width = 2 * key_rows.shape[1]
    extra_rows = -(-extras.shape[0] // kv_width)
    extras = jnp.pad(extras, (0, extra_rows * kv_width - extras.shape[0]))
    shipped = jnp.concatenate(
        [key_rows, value_rows, ], axis=1
    )
    shipped = jnp.concatenate([shipped, extras.reshape(extra_rows, kv_width)], axis=0)
    gathered = lax.all_gather(shipped, "blk", axis=0, tiled=False)
    blocks = gathered.shape[0]
    key_part = gathered[:, :tok_rows, : kv_width // 2].reshape(blocks * tok_rows, kv_width // 2)
    value_part = gathered[:, :tok_rows, kv_width // 2 :].reshape(blocks * tok_rows, kv_width // 2)
    extras_all = gathered[:, tok_rows:].reshape(blocks, -1)[:, : reqs * (query_last.shape[1] + feat_dev)]
    extras_all = jnp.sum(extras_all.astype(jnp.float32).reshape(blocks, reqs, -1), axis=0)
    query_last = extras_all[:, : query_last.shape[1]].astype(jnp.bfloat16)
    seq_last = extras_all[:, query_last.shape[1] :]
    piece_rows = key_part.shape[0]
    key_ids = jnp.arange(piece_rows, dtype=jnp.int32)
    key_req, unused_begin = request_info(key_ids, req_lengths)
    key_part = key_part.reshape(piece_rows, kv_heads, HD)
    value_part = value_part.reshape(piece_rows, kv_heads, HD)
    result = []
    for part_index in range(2):
        lower = part_index * half_rows
        sub_ids = row_ids[lower : lower + half_rows]
        sub_req = query_req[lower : lower + half_rows]
        sub_queries = queries[lower : lower + half_rows]
        needed = (jnp.max(sub_ids) >= first_row) & (
            first_row + piece_rows - 1 >= jnp.min(query_begin[lower : lower + half_rows])
        )

        def compute(state):
            return attend(
                state, sub_queries, sub_ids, sub_req, key_part, value_part, key_ids, key_req, root
            )

        def keep_state(state):
            return state

        result.append(lax.cond(needed, compute, keep_state, carry[part_index]))
    states = tuple(result)
    context = jnp.concatenate(
        [states[0][2] / states[0][1][..., None], states[1][2] / states[1][1][..., None]], axis=0
    )
    context = context.astype(jnp.bfloat16).reshape(tok_rows, kv_heads * per_group * HD)
    last_begin = ends_at - req_lengths
    last_allowed = (key_ids[None, :] >= last_begin[:, None]) & (key_ids[None, :] <= last_ids[:, None])
    last_allowed = last_allowed[:, None, None, :]
    last_q = query_last.reshape(reqs, kv_heads, per_group, HD)
    last_scores = (
        jnp.einsum("tgqd,kgd->tgqk", last_q, key_part, preferred_element_type=jnp.float32) / root
    )
    last_scores = jnp.where(last_allowed, last_scores, -1e30)
    last_max = jnp.max(last_scores, axis=-1)
    last_weights = jnp.where(last_allowed, jnp.exp(last_scores - last_max[..., None]), 0.0)
    last_sum = jnp.sum(last_weights, axis=-1)
    last_mix = jnp.einsum(
        "tgqk,kgd->tgqd",
        last_weights.astype(jnp.bfloat16),
        value_part,
        preferred_element_type=jnp.float32,
    )
    last_context = (last_mix / last_sum[..., None]).astype(jnp.bfloat16).reshape(reqs, -1)
    out_rows = jnp.concatenate([context, last_context], axis=0)
    head_sum = lax.psum_scatter(
        jnp.dot(out_rows, w_out, preferred_element_type=jnp.float32).astype(jnp.bfloat16),
        "kv",
        scatter_dimension=1,
        tiled=True,
    ).astype(jnp.float32)
    hidden = (seq_in.astype(jnp.float32) + head_sum[:tok_rows]).astype(jnp.bfloat16)
    chosen = (seq_last + head_sum[tok_rows:]).astype(jnp.bfloat16).astype(jnp.float32)
    square_part = jnp.sum(chosen * chosen, axis=-1)
    scaled = (chosen * final_gain).astype(jnp.bfloat16)
    logit_part = lax.dot_general(
        scaled, table, (((1,), (1,)), ((), ())), preferred_element_type=jnp.float32
    )
    logit_sum, square_sum = (
        lax.psum(logit_part.astype(jnp.bfloat16), "kv").astype(jnp.float32),
        lax.psum(square_part.astype(jnp.bfloat16), "kv").astype(jnp.float32),
    )
    inv_rms = lax.rsqrt(square_sum / D + 1e-05)
    last_norm = (chosen * inv_rms[:, None] * final_gain).astype(jnp.bfloat16)
    local_max = jnp.max(inv_rms[:, None] * logit_sum, axis=-1)
    max_logit = lax.pmax(local_max, "blk")
    return (hidden, last_norm, max_logit)


def solution(mesh):
    placed = (
        P("blk", None, None),
        P("blk", None),
        P("blk"),
        P(),
        P(None, None, "kv"),
        P("kv", None),
        P(None, "kv"),
        P("blk", "kv"),
        P(),
        P(None, "kv"),
        P(None, None, "kv"),
        P("kv", None),
        P(),
        P("kv"),
        P("blk", "kv"),
    )
    return jax.shard_map(
        on_device,
        mesh=mesh,
        in_specs=placed,
        out_specs=(P("blk", "kv"), P(None, "kv"), P()),
        check_vma=False,
    )
```

```python
import math

import jax
import jax.numpy as jnp
from jax import lax
from jax.sharding import PartitionSpec as P

VHD = 88
D = 4096
QHEADS = 16
KVHEADS = 8
HD = 128


def layer_norm(inputs, gain):
    centre = jnp.mean(inputs, axis=-1, keepdims=True)
    centred = inputs - centre
    spread = jnp.mean(centred * centred, axis=-1, keepdims=True)
    return centred * lax.rsqrt(spread + 1e-06) * gain


def rotate(inputs, position):
    half_width = inputs.shape[-1] // 2
    inverse = 500000.0 ** (-jnp.arange(half_width, dtype=jnp.float32) * 2.0 / inputs.shape[-1])
    angles = position.astype(jnp.float32)[:, None] * inverse[None, :]
    cosine = jnp.cos(angles)[:, None, :]
    sine = jnp.sin(angles)[:, None, :]
    first = inputs[..., :half_width]
    second = inputs[..., half_width:]
    return jnp.concatenate(
        [first * cosine - second * sine, second * cosine + first * sine], axis=-1
    )


def request_info(row_index, req_lengths):
    ends_at = jnp.cumsum(req_lengths)
    starts_at = ends_at - req_lengths
    request_id = jnp.sum((row_index[:, None] >= ends_at[None, :]).astype(jnp.int32), axis=1)
    choose = request_id[:, None] == jnp.arange(req_lengths.shape[0], dtype=jnp.int32)[None, :]
    request_begin = jnp.sum(jnp.where(choose, starts_at[None, :], 0), axis=1)
    return (request_id, request_begin)


def on_device(
    patches,
    merged_grid,
    picture_start,
    vis_gain,
    vis_qkv,
    vis_out,
    merge_weight,
    text_embed,
    dec_gain,
    w_query,
    w_keyval,
    w_out,
    req_lengths,
    final_gain,
    table,
):
    pictures, patch_max, vis_width = patches.shape
    merged_max = patch_max // 4
    vis_cols = vis_qkv.shape[2]
    vis_heads = vis_cols // VHD
    tok_rows, feat_dev = text_embed.shape
    text_rows = lax.all_gather(text_embed, "kv", axis=1, tiled=True)
    inputs = patches.astype(jnp.float32)
    normed = layer_norm(inputs, vis_gain).astype(jnp.bfloat16)
    packed = jnp.einsum(
        "pnd,dce->pnce", normed, vis_qkv, preferred_element_type=jnp.float32
    ).astype(jnp.bfloat16)
    packed = packed.reshape(pictures, patch_max, 3, vis_heads, VHD)
    scores = jnp.einsum(
        "pqhd,pkhd->phqk", packed[:, :, 0], packed[:, :, 1], preferred_element_type=jnp.float32
    ) / math.sqrt(VHD)
    cell_count = merged_grid[:, 0] * merged_grid[:, 1]
    valid_cols = jnp.arange(patch_max, dtype=jnp.int32)[None, :] < 4 * cell_count[:, None]
    scores = jnp.where(valid_cols[:, None, None, :], scores, -1e30)
    weights = jnp.exp(scores - jnp.max(scores, axis=-1, keepdims=True))
    weight_sum = jnp.sum(weights, axis=-1)
    mixed_rows = jnp.einsum(
        "phqk,pkhd->pqhd",
        weights.astype(jnp.bfloat16),
        packed[:, :, 2],
        preferred_element_type=jnp.float32,
    )
    mixed_rows = (
        (mixed_rows / jnp.transpose(weight_sum, (0, 2, 1))[..., None])
        .astype(jnp.bfloat16)
        .reshape(pictures, patch_max, vis_cols)
    )
    head_part = jnp.einsum("pnc,cd->pnd", mixed_rows, vis_out, preferred_element_type=jnp.float32)
    head_pooled = jnp.mean(head_part.reshape(pictures, merged_max, 4, vis_width), axis=2)
    head_total = lax.psum(head_pooled.astype(jnp.bfloat16), "kv").astype(jnp.float32)
    input_pooled = jnp.mean(inputs.reshape(pictures, merged_max, 4, vis_width), axis=2)
    pooled = (input_pooled + head_total).astype(jnp.bfloat16)
    merged = jnp.einsum(
        "pmd,de->pme", pooled, merge_weight, preferred_element_type=jnp.float32
    ).astype(jnp.bfloat16)
    block_base = lax.axis_index("blk") * tok_rows
    slot_index = jnp.arange(merged_max, dtype=jnp.int32)
    target = picture_start[:, None] + slot_index[None, :] - block_base
    target = jnp.where(slot_index[None, :] < cell_count[:, None], target, -1).reshape(-1)
    local_rows = jnp.arange(tok_rows, dtype=jnp.int32)
    one_hot = local_rows[:, None] == target[None, :]
    placed = jnp.dot(
        one_hot.astype(jnp.bfloat16),
        merged.reshape(pictures * merged_max, feat_dev),
        preferred_element_type=jnp.float32,
    )
    is_vision = jnp.any(one_hot, axis=1)
    seq_in = jnp.where(is_vision[:, None], placed.astype(jnp.bfloat16), text_embed)
    merged_rows = lax.all_gather(
        merged.reshape(pictures * merged_max, feat_dev), "kv", axis=1, tiled=True
    )
    placed_rows = jnp.dot(one_hot.astype(jnp.bfloat16), merged_rows, preferred_element_type=jnp.float32)
    full_rows = jnp.where(is_vision[:, None], placed_rows.astype(jnp.bfloat16), text_rows)
    full_float = full_rows.astype(jnp.float32)
    dec_normed = (
        full_float
        * lax.rsqrt(jnp.mean(full_float * full_float, axis=-1, keepdims=True) + 1e-05)
        * dec_gain
    ).astype(jnp.bfloat16)
    per_group = QHEADS // KVHEADS
    kv_heads = w_keyval.shape[2] // HD
    row_ids = block_base + local_rows
    request_id, request_begin = request_info(row_ids, req_lengths)
    position = row_ids - request_begin
    query_proj = jnp.dot(dec_normed, w_query, preferred_element_type=jnp.float32).reshape(
        tok_rows, kv_heads * per_group, HD
    )
    query_proj = (
        rotate(query_proj, position)
        .astype(jnp.bfloat16)
        .reshape(tok_rows, kv_heads * per_group * HD)
    )
    key_value = jnp.einsum("td,dce->tce", dec_normed, w_keyval, preferred_element_type=jnp.float32)
    key_rows = (
        rotate(key_value[:, 0].reshape(tok_rows, kv_heads, HD), position)
        .astype(jnp.bfloat16)
        .reshape(tok_rows, kv_heads * HD)
    )
    value_rows = key_value[:, 1].astype(jnp.bfloat16)
    query_req, query_begin = request_info(row_ids, req_lengths)
    root = math.sqrt(HD)
    reqs = req_lengths.shape[0]
    ends_at = jnp.cumsum(req_lengths)
    last_ids = ends_at - 1
    picker = (local_rows[None, :] == (last_ids - block_base)[:, None]).astype(jnp.bfloat16)
    query_last = jnp.dot(picker, query_proj, preferred_element_type=jnp.float32)
    seq_last = jnp.dot(picker, seq_in, preferred_element_type=jnp.float32)
    extras = jnp.concatenate([query_last, seq_last], axis=1).astype(jnp.bfloat16).reshape(-1)
    kv_width = key_rows.shape[1]
    ship_width = 2 * kv_width
    extra_rows = -(-extras.shape[0] // ship_width)
    extras = jnp.pad(extras, (0, extra_rows * ship_width - extras.shape[0]))
    shipped = jnp.concatenate([key_rows, value_rows], axis=1)
    shipped = jnp.concatenate([shipped, extras.reshape(extra_rows, ship_width)], axis=0)
    gathered = lax.all_gather(shipped, "blk", axis=0, tiled=False)
    blocks = gathered.shape[0]
    q_cols = query_proj.shape[1]
    extras_all = gathered[:, tok_rows:].reshape(blocks, -1)[:, : reqs * (q_cols + feat_dev)]
    extras_all = jnp.sum(extras_all.astype(jnp.float32).reshape(blocks, reqs, -1), axis=0)
    query_last = extras_all[:, :q_cols].astype(jnp.bfloat16)
    seq_last = extras_all[:, q_cols:]
    group_queries = [
        query_proj[:, g * per_group * HD : (g + 1) * per_group * HD].reshape(tok_rows, per_group, HD)
        for g in range(kv_heads)
    ]
    block_index = lax.axis_index("blk")
    first_begin = query_begin[0]

    def block_step(kb, state):
        key_first = kb * tok_rows
        needed = (kb <= block_index) & (key_first + tok_rows - 1 >= first_begin)

        def compute(state):
            piece = lax.dynamic_index_in_dim(gathered, kb, 0, keepdims=False)
            key_ids = key_first + local_rows
            key_req, unused = request_info(key_ids, req_lengths)
            allowed = (key_ids[None, :] <= row_ids[:, None]) & (key_req[None, :] == query_req[:, None])
            allowed = allowed[:, None, :]
            new_state = []
            for g in range(kv_heads):
                run_max, run_sum, run_acc = state[g]
                keys_g = piece[:tok_rows, g * HD : (g + 1) * HD]
                values_g = piece[:tok_rows, kv_width + g * HD : kv_width + (g + 1) * HD]
                scores = (
                    jnp.einsum(
                        "tqd,kd->tqk", group_queries[g], keys_g, preferred_element_type=jnp.float32
                    )
                    / root
                )
                scores = jnp.where(allowed, scores, -1e30)
                new_max = jnp.maximum(run_max, jnp.max(scores, axis=-1))
                weights = jnp.where(allowed, jnp.exp(scores - new_max[..., None]), 0.0)
                scale = jnp.exp(run_max - new_max)
                new_sum = run_sum * scale + jnp.sum(weights, axis=-1)
                new_acc = run_acc * scale[..., None] + jnp.einsum(
                    "tqk,kd->tqd",
                    weights.astype(jnp.bfloat16),
                    values_g,
                    preferred_element_type=jnp.float32,
                )
                new_state.append((new_max, new_sum, new_acc))
            return tuple(new_state)

        return lax.cond(needed, compute, lambda s: s, state)

    init = tuple(
        (
            jnp.full((tok_rows, per_group), -1e30, jnp.float32),
            jnp.zeros((tok_rows, per_group), jnp.float32),
            jnp.zeros((tok_rows, per_group, HD), jnp.float32),
        )
        for g in range(kv_heads)
    )
    final = lax.fori_loop(0, blocks, block_step, init)
    context = jnp.concatenate(
        [(acc / total[..., None]).reshape(tok_rows, per_group * HD) for unused, total, acc in final],
        axis=1,
    ).astype(jnp.bfloat16)
    all_ids = jnp.arange(blocks * tok_rows, dtype=jnp.int32)
    last_begin = ends_at - req_lengths
    last_allowed = (all_ids[None, :] >= last_begin[:, None]) & (all_ids[None, :] <= last_ids[:, None])
    last_allowed = last_allowed[:, None, :]
    last_parts = []
    for g in range(kv_heads):
        keys_g = gathered[:, :tok_rows, g * HD : (g + 1) * HD].reshape(blocks * tok_rows, HD)
        values_g = gathered[:, :tok_rows, kv_width + g * HD : kv_width + (g + 1) * HD].reshape(
            blocks * tok_rows, HD
        )
        last_q = query_last[:, g * per_group * HD : (g + 1) * per_group * HD].reshape(
            reqs, per_group, HD
        )
        last_scores = (
            jnp.einsum("tqd,kd->tqk", last_q, keys_g, preferred_element_type=jnp.float32) / root
        )
        last_scores = jnp.where(last_allowed, last_scores, -1e30)
        last_max = jnp.max(last_scores, axis=-1)
        last_weights = jnp.where(last_allowed, jnp.exp(last_scores - last_max[..., None]), 0.0)
        last_sum = jnp.sum(last_weights, axis=-1)
        last_mix = jnp.einsum(
            "tqk,kd->tqd",
            last_weights.astype(jnp.bfloat16),
            values_g,
            preferred_element_type=jnp.float32,
        )
        last_parts.append((last_mix / last_sum[..., None]).reshape(reqs, per_group * HD))
    last_context = jnp.concatenate(last_parts, axis=1).astype(jnp.bfloat16)
    out_rows = jnp.concatenate([context, last_context], axis=0)
    head_sum = lax.psum_scatter(
        jnp.dot(out_rows, w_out, preferred_element_type=jnp.float32).astype(jnp.bfloat16),
        "kv",
        scatter_dimension=1,
        tiled=True,
    ).astype(jnp.float32)
    hidden = (seq_in.astype(jnp.float32) + head_sum[:tok_rows]).astype(jnp.bfloat16)
    chosen = (seq_last + head_sum[tok_rows:]).astype(jnp.bfloat16).astype(jnp.float32)
    square_part = jnp.sum(chosen * chosen, axis=-1)
    scaled = (chosen * final_gain).astype(jnp.bfloat16)
    logit_part = lax.dot_general(
        scaled, table, (((1,), (1,)), ((), ())), preferred_element_type=jnp.float32
    )
    logit_sum, square_sum = (
        lax.psum(logit_part.astype(jnp.bfloat16), "kv").astype(jnp.float32),
        lax.psum(square_part.astype(jnp.bfloat16), "kv").astype(jnp.float32),
    )
    inv_rms = lax.rsqrt(square_sum / D + 1e-05)
    last_norm = (chosen * inv_rms[:, None] * final_gain).astype(jnp.bfloat16)
    local_max = jnp.max(inv_rms[:, None] * logit_sum, axis=-1)
    max_logit = lax.pmax(local_max, "blk")
    return (hidden, last_norm, max_logit)


def solution(mesh):
    placed = (
        P("blk", None, None),
        P("blk", None),
        P("blk"),
        P(),
        P(None, None, "kv"),
        P("kv", None),
        P(None, "kv"),
        P("blk", "kv"),
        P(),
        P(None, "kv"),
        P(None, None, "kv"),
        P("kv", None),
        P(),
        P("kv"),
        P("blk", "kv"),
    )
    return jax.shard_map(
        on_device,
        mesh=mesh,
        in_specs=placed,
        out_specs=(P("blk", "kv"), P(None, "kv"), P()),
        check_vma=False,
    )
```

```python
import functools
import math

import jax
import jax.numpy as jnp
from jax import lax
from jax.experimental import pallas as pl
from jax.experimental.pallas import tpu as pltpu
from jax.sharding import PartitionSpec as P

VHD = 88
D = 4096
QHEADS = 16
KVHEADS = 8
HD = 128


def layer_norm(inputs, gain):
    centre = jnp.mean(inputs, axis=-1, keepdims=True)
    centred = inputs - centre
    spread = jnp.mean(centred * centred, axis=-1, keepdims=True)
    return centred * lax.rsqrt(spread + 1e-06) * gain


def rotate(inputs, position):
    half_width = inputs.shape[-1] // 2
    inverse = 500000.0 ** (-jnp.arange(half_width, dtype=jnp.float32) * 2.0 / inputs.shape[-1])
    angles = position.astype(jnp.float32)[:, None] * inverse[None, :]
    cosine = jnp.cos(angles)[:, None, :]
    sine = jnp.sin(angles)[:, None, :]
    first = inputs[..., :half_width]
    second = inputs[..., half_width:]
    return jnp.concatenate(
        [first * cosine - second * sine, second * cosine + first * sine], axis=-1
    )


def request_info(row_index, req_lengths):
    ends_at = jnp.cumsum(req_lengths)
    starts_at = ends_at - req_lengths
    request_id = jnp.sum((row_index[:, None] >= ends_at[None, :]).astype(jnp.int32), axis=1)
    choose = request_id[:, None] == jnp.arange(req_lengths.shape[0], dtype=jnp.int32)[None, :]
    request_begin = jnp.sum(jnp.where(choose, starts_at[None, :], 0), axis=1)
    return (request_id, request_begin)


def flash_kernel(needed_ref, q_ref, k_ref, v_ref, qid_ref, qreq_ref, kid_ref, kreq_ref, o_ref,
                 max_ref, sum_ref, acc_ref, *, root):
    kb = pl.program_id(1)

    @pl.when(kb == 0)
    def _():
        max_ref[...] = jnp.full(max_ref.shape, -1e30, jnp.float32)
        sum_ref[...] = jnp.zeros(sum_ref.shape, jnp.float32)
        acc_ref[...] = jnp.zeros(acc_ref.shape, jnp.float32)

    @pl.when(needed_ref[kb] != 0)
    def _():
        scores = lax.dot_general(
            q_ref[...], k_ref[...], (((1,), (1,)), ((), ())), preferred_element_type=jnp.float32
        ) / root
        allowed = (kid_ref[...] <= qid_ref[...]) & (kreq_ref[...] == qreq_ref[...])
        scores = jnp.where(allowed, scores, -1e30)
        old_max = max_ref[...]
        new_max = jnp.maximum(old_max, jnp.max(scores, axis=1, keepdims=True))
        weights = jnp.where(allowed, jnp.exp(scores - new_max), 0.0)
        scale = jnp.exp(old_max - new_max)
        sum_ref[...] = sum_ref[...] * scale + jnp.sum(weights, axis=1, keepdims=True)
        acc_ref[...] = acc_ref[...] * scale + jnp.dot(
            weights.astype(jnp.bfloat16), v_ref[...], preferred_element_type=jnp.float32
        )
        max_ref[...] = new_max

    @pl.when(kb == pl.num_programs(1) - 1)
    def _():
        o_ref[...] = (acc_ref[...] / sum_ref[...]).astype(o_ref.dtype)


def flash_attention(needed, grouped_q, gathered, q_ids, q_req, k_ids, k_req, groups, tok_rows, root):
    blocks = gathered.shape[0]
    group_rows = grouped_q.shape[1]
    grid_spec = pltpu.PrefetchScalarGridSpec(
        num_scalar_prefetch=1,
        grid=(groups, blocks),
        in_specs=[
            pl.BlockSpec((None, group_rows, HD), lambda g, kb, n: (g, 0, 0)),
            pl.BlockSpec((None, tok_rows, HD), lambda g, kb, n: (kb, 0, g)),
            pl.BlockSpec((None, tok_rows, HD), lambda g, kb, n: (kb, 0, groups + g)),
            pl.BlockSpec((group_rows, 1), lambda g, kb, n: (0, 0)),
            pl.BlockSpec((group_rows, 1), lambda g, kb, n: (0, 0)),
            pl.BlockSpec((None, 1, tok_rows), lambda g, kb, n: (kb, 0, 0)),
            pl.BlockSpec((None, 1, tok_rows), lambda g, kb, n: (kb, 0, 0)),
        ],
        out_specs=pl.BlockSpec((None, group_rows, HD), lambda g, kb, n: (g, 0, 0)),
        scratch_shapes=[
            pltpu.VMEM((group_rows, 1), jnp.float32),
            pltpu.VMEM((group_rows, 1), jnp.float32),
            pltpu.VMEM((group_rows, HD), jnp.float32),
        ],
    )
    flops = 4 * groups * blocks * group_rows * tok_rows * HD
    return pl.pallas_call(
        functools.partial(flash_kernel, root=root),
        grid_spec=grid_spec,
        out_shape=jax.ShapeDtypeStruct((groups, group_rows, HD), jnp.bfloat16),
        compiler_params=pltpu.CompilerParams(dimension_semantics=("arbitrary", "arbitrary")),
        cost_estimate=pl.CostEstimate(
            flops=flops,
            transcendentals=groups * blocks * group_rows * tok_rows,
            bytes_accessed=2 * groups * blocks * tok_rows * HD * 2 + 4 * groups * group_rows * HD,
        ),
    )(needed, grouped_q, gathered, gathered, q_ids, q_req, k_ids, k_req)


def on_device(
    patches,
    merged_grid,
    picture_start,
    vis_gain,
    vis_qkv,
    vis_out,
    merge_weight,
    text_embed,
    dec_gain,
    w_query,
    w_keyval,
    w_out,
    req_lengths,
    final_gain,
    table,
):
    pictures, patch_max, vis_width = patches.shape
    merged_max = patch_max // 4
    vis_cols = vis_qkv.shape[2]
    vis_heads = vis_cols // VHD
    tok_rows, feat_dev = text_embed.shape
    text_rows = lax.all_gather(text_embed, "kv", axis=1, tiled=True)
    inputs = patches.astype(jnp.float32)
    normed = layer_norm(inputs, vis_gain).astype(jnp.bfloat16)
    packed = jnp.einsum(
        "pnd,dce->pnce", normed, vis_qkv, preferred_element_type=jnp.float32
    ).astype(jnp.bfloat16)
    packed = packed.reshape(pictures, patch_max, 3, vis_heads, VHD)
    scores = jnp.einsum(
        "pqhd,pkhd->phqk", packed[:, :, 0], packed[:, :, 1], preferred_element_type=jnp.float32
    ) / math.sqrt(VHD)
    cell_count = merged_grid[:, 0] * merged_grid[:, 1]
    valid_cols = jnp.arange(patch_max, dtype=jnp.int32)[None, :] < 4 * cell_count[:, None]
    scores = jnp.where(valid_cols[:, None, None, :], scores, -1e30)
    weights = jnp.exp(scores - jnp.max(scores, axis=-1, keepdims=True))
    weight_sum = jnp.sum(weights, axis=-1)
    mixed_rows = jnp.einsum(
        "phqk,pkhd->pqhd",
        weights.astype(jnp.bfloat16),
        packed[:, :, 2],
        preferred_element_type=jnp.float32,
    )
    mixed_rows = (
        (mixed_rows / jnp.transpose(weight_sum, (0, 2, 1))[..., None])
        .astype(jnp.bfloat16)
        .reshape(pictures, patch_max, vis_cols)
    )
    head_part = jnp.einsum("pnc,cd->pnd", mixed_rows, vis_out, preferred_element_type=jnp.float32)
    head_pooled = jnp.mean(head_part.reshape(pictures, merged_max, 4, vis_width), axis=2)
    head_total = lax.psum(head_pooled.astype(jnp.bfloat16), "kv").astype(jnp.float32)
    input_pooled = jnp.mean(inputs.reshape(pictures, merged_max, 4, vis_width), axis=2)
    pooled = (input_pooled + head_total).astype(jnp.bfloat16)
    merged = jnp.einsum(
        "pmd,de->pme", pooled, merge_weight, preferred_element_type=jnp.float32
    ).astype(jnp.bfloat16)
    block_base = lax.axis_index("blk") * tok_rows
    slot_index = jnp.arange(merged_max, dtype=jnp.int32)
    target = picture_start[:, None] + slot_index[None, :] - block_base
    target = jnp.where(slot_index[None, :] < cell_count[:, None], target, -1).reshape(-1)
    local_rows = jnp.arange(tok_rows, dtype=jnp.int32)
    one_hot = local_rows[:, None] == target[None, :]
    placed = jnp.dot(
        one_hot.astype(jnp.bfloat16),
        merged.reshape(pictures * merged_max, feat_dev),
        preferred_element_type=jnp.float32,
    )
    is_vision = jnp.any(one_hot, axis=1)
    seq_in = jnp.where(is_vision[:, None], placed.astype(jnp.bfloat16), text_embed)
    merged_rows = lax.all_gather(
        merged.reshape(pictures * merged_max, feat_dev), "kv", axis=1, tiled=True
    )
    placed_rows = jnp.dot(one_hot.astype(jnp.bfloat16), merged_rows, preferred_element_type=jnp.float32)
    full_rows = jnp.where(is_vision[:, None], placed_rows.astype(jnp.bfloat16), text_rows)
    full_float = full_rows.astype(jnp.float32)
    dec_normed = (
        full_float
        * lax.rsqrt(jnp.mean(full_float * full_float, axis=-1, keepdims=True) + 1e-05)
        * dec_gain
    ).astype(jnp.bfloat16)
    per_group = QHEADS // KVHEADS
    kv_heads = w_keyval.shape[2] // HD
    row_ids = block_base + local_rows
    request_id, request_begin = request_info(row_ids, req_lengths)
    position = row_ids - request_begin
    query_proj = jnp.dot(dec_normed, w_query, preferred_element_type=jnp.float32).reshape(
        tok_rows, kv_heads * per_group, HD
    )
    query_proj = (
        rotate(query_proj, position)
        .astype(jnp.bfloat16)
        .reshape(tok_rows, kv_heads * per_group * HD)
    )
    key_value = jnp.einsum("td,dce->tce", dec_normed, w_keyval, preferred_element_type=jnp.float32)
    key_rows = (
        rotate(key_value[:, 0].reshape(tok_rows, kv_heads, HD), position)
        .astype(jnp.bfloat16)
        .reshape(tok_rows, kv_heads * HD)
    )
    value_rows = key_value[:, 1].astype(jnp.bfloat16)
    query_req, query_begin = request_info(row_ids, req_lengths)
    root = math.sqrt(HD)
    reqs = req_lengths.shape[0]
    ends_at = jnp.cumsum(req_lengths)
    last_ids = ends_at - 1
    picker = (local_rows[None, :] == (last_ids - block_base)[:, None]).astype(jnp.bfloat16)
    query_last = jnp.dot(picker, query_proj, preferred_element_type=jnp.float32)
    seq_last = jnp.dot(picker, seq_in, preferred_element_type=jnp.float32)
    extras = jnp.concatenate([query_last, seq_last], axis=1).astype(jnp.bfloat16).reshape(-1)
    kv_width = key_rows.shape[1]
    ship_width = 2 * kv_width
    extra_rows = -(-extras.shape[0] // ship_width)
    extras = jnp.pad(extras, (0, extra_rows * ship_width - extras.shape[0]))
    shipped = jnp.concatenate([key_rows, value_rows], axis=1)
    shipped = jnp.concatenate([shipped, extras.reshape(extra_rows, ship_width)], axis=0)
    gathered = lax.all_gather(shipped, "blk", axis=0, tiled=False)
    blocks = gathered.shape[0]
    q_cols = query_proj.shape[1]
    extras_all = gathered[:, tok_rows:].reshape(blocks, -1)[:, : reqs * (q_cols + feat_dev)]
    extras_all = jnp.sum(extras_all.astype(jnp.float32).reshape(blocks, reqs, -1), axis=0)
    query_last = extras_all[:, :q_cols].astype(jnp.bfloat16)
    seq_last = extras_all[:, q_cols:]
    block_index = lax.axis_index("blk")
    first_begin = query_begin[0]
    block_ids = jnp.arange(blocks, dtype=jnp.int32)
    needed = (
        (block_ids <= block_index) & (block_ids * tok_rows + tok_rows - 1 >= first_begin)
    ).astype(jnp.int32)
    group_rows = tok_rows * per_group
    grouped_q = jnp.transpose(
        query_proj.reshape(tok_rows, kv_heads, per_group, HD), (1, 0, 2, 3)
    ).reshape(kv_heads, group_rows, HD)
    q_ids = jnp.repeat(row_ids, per_group)[:, None]
    q_req = jnp.repeat(query_req, per_group)[:, None]
    all_ids = jnp.arange(blocks * tok_rows, dtype=jnp.int32)
    all_req, unused = request_info(all_ids, req_lengths)
    k_ids = all_ids.reshape(blocks, 1, tok_rows)
    k_req = all_req.reshape(blocks, 1, tok_rows)
    context = flash_attention(
        needed, grouped_q, gathered, q_ids, q_req, k_ids, k_req, kv_heads, tok_rows, root
    )
    context = jnp.transpose(
        context.reshape(kv_heads, tok_rows, per_group, HD), (1, 0, 2, 3)
    ).reshape(tok_rows, kv_heads * per_group * HD)
    all_ids = jnp.arange(blocks * tok_rows, dtype=jnp.int32)
    last_begin = ends_at - req_lengths
    last_allowed = (all_ids[None, :] >= last_begin[:, None]) & (all_ids[None, :] <= last_ids[:, None])
    last_allowed = last_allowed[:, None, :]
    last_parts = []
    for g in range(kv_heads):
        keys_g = gathered[:, :tok_rows, g * HD : (g + 1) * HD].reshape(blocks * tok_rows, HD)
        values_g = gathered[:, :tok_rows, kv_width + g * HD : kv_width + (g + 1) * HD].reshape(
            blocks * tok_rows, HD
        )
        last_q = query_last[:, g * per_group * HD : (g + 1) * per_group * HD].reshape(
            reqs, per_group, HD
        )
        last_scores = (
            jnp.einsum("tqd,kd->tqk", last_q, keys_g, preferred_element_type=jnp.float32) / root
        )
        last_scores = jnp.where(last_allowed, last_scores, -1e30)
        last_max = jnp.max(last_scores, axis=-1)
        last_weights = jnp.where(last_allowed, jnp.exp(last_scores - last_max[..., None]), 0.0)
        last_sum = jnp.sum(last_weights, axis=-1)
        last_mix = jnp.einsum(
            "tqk,kd->tqd",
            last_weights.astype(jnp.bfloat16),
            values_g,
            preferred_element_type=jnp.float32,
        )
        last_parts.append((last_mix / last_sum[..., None]).reshape(reqs, per_group * HD))
    last_context = jnp.concatenate(last_parts, axis=1).astype(jnp.bfloat16)
    out_rows = jnp.concatenate([context, last_context], axis=0)
    head_sum = lax.psum_scatter(
        jnp.dot(out_rows, w_out, preferred_element_type=jnp.float32).astype(jnp.bfloat16),
        "kv",
        scatter_dimension=1,
        tiled=True,
    ).astype(jnp.float32)
    hidden = (seq_in.astype(jnp.float32) + head_sum[:tok_rows]).astype(jnp.bfloat16)
    chosen = (seq_last + head_sum[tok_rows:]).astype(jnp.bfloat16).astype(jnp.float32)
    square_part = jnp.sum(chosen * chosen, axis=-1)
    scaled = (chosen * final_gain).astype(jnp.bfloat16)
    logit_part = lax.dot_general(
        scaled, table, (((1,), (1,)), ((), ())), preferred_element_type=jnp.float32
    )
    logit_sum, square_sum = (
        lax.psum(logit_part.astype(jnp.bfloat16), "kv").astype(jnp.float32),
        lax.psum(square_part.astype(jnp.bfloat16), "kv").astype(jnp.float32),
    )
    inv_rms = lax.rsqrt(square_sum / D + 1e-05)
    last_norm = (chosen * inv_rms[:, None] * final_gain).astype(jnp.bfloat16)
    local_max = jnp.max(inv_rms[:, None] * logit_sum, axis=-1)
    max_logit = lax.pmax(local_max, "blk")
    return (hidden, last_norm, max_logit)


def solution(mesh):
    placed = (
        P("blk", None, None),
        P("blk", None),
        P("blk"),
        P(),
        P(None, None, "kv"),
        P("kv", None),
        P(None, "kv"),
        P("blk", "kv"),
        P(),
        P(None, "kv"),
        P(None, None, "kv"),
        P("kv", None),
        P(),
        P("kv"),
        P("blk", "kv"),
    )
    return jax.shard_map(
        on_device,
        mesh=mesh,
        in_specs=placed,
        out_specs=(P("blk", "kv"), P(None, "kv"), P()),
        check_vma=False,
    )
```

```python
import functools
import math

import jax
import jax.numpy as jnp
from jax import lax
from jax.experimental import pallas as pl
from jax.experimental.pallas import tpu as pltpu
from jax.sharding import PartitionSpec as P

VHD = 88
D = 4096
QHEADS = 16
KVHEADS = 8
HD = 128


def layer_norm(inputs, gain):
    centre = jnp.mean(inputs, axis=-1, keepdims=True)
    centred = inputs - centre
    spread = jnp.mean(centred * centred, axis=-1, keepdims=True)
    return centred * lax.rsqrt(spread + 1e-06) * gain


def rotate(inputs, position):
    half_width = inputs.shape[-1] // 2
    inverse = 500000.0 ** (-jnp.arange(half_width, dtype=jnp.float32) * 2.0 / inputs.shape[-1])
    angles = position.astype(jnp.float32)[:, None] * inverse[None, :]
    cosine = jnp.cos(angles)[:, None, :]
    sine = jnp.sin(angles)[:, None, :]
    first = inputs[..., :half_width]
    second = inputs[..., half_width:]
    return jnp.concatenate(
        [first * cosine - second * sine, second * cosine + first * sine], axis=-1
    )


def request_info(row_index, req_lengths):
    ends_at = jnp.cumsum(req_lengths)
    starts_at = ends_at - req_lengths
    request_id = jnp.sum((row_index[:, None] >= ends_at[None, :]).astype(jnp.int32), axis=1)
    choose = request_id[:, None] == jnp.arange(req_lengths.shape[0], dtype=jnp.int32)[None, :]
    request_begin = jnp.sum(jnp.where(choose, starts_at[None, :], 0), axis=1)
    return (request_id, request_begin)


def flash_kernel(needed_ref, q_ref, k_ref, v_ref, qid_ref, qreq_ref, kid_ref, kreq_ref, o_ref,
                 max_ref, sum_ref, acc_ref, *, root):
    kb = pl.program_id(1)

    @pl.when(kb == 0)
    def _():
        max_ref[...] = jnp.full(max_ref.shape, -1e30, jnp.float32)
        sum_ref[...] = jnp.zeros(sum_ref.shape, jnp.float32)
        acc_ref[...] = jnp.zeros(acc_ref.shape, jnp.float32)

    @pl.when(needed_ref[kb] != 0)
    def _():
        scores = lax.dot_general(
            q_ref[...], k_ref[...], (((1,), (1,)), ((), ())), preferred_element_type=jnp.float32
        ) / root
        allowed = (kid_ref[...] <= qid_ref[...]) & (kreq_ref[...] == qreq_ref[...])
        scores = jnp.where(allowed, scores, -1e30)
        old_max = max_ref[...]
        new_max = jnp.maximum(old_max, jnp.max(scores, axis=1, keepdims=True))
        weights = jnp.where(allowed, jnp.exp(scores - new_max), 0.0)
        scale = jnp.exp(old_max - new_max)
        sum_ref[...] = sum_ref[...] * scale + jnp.sum(weights, axis=1, keepdims=True)
        acc_ref[...] = acc_ref[...] * scale + jnp.dot(
            weights.astype(jnp.bfloat16), v_ref[...], preferred_element_type=jnp.float32
        )
        max_ref[...] = new_max

    @pl.when(kb == pl.num_programs(1) - 1)
    def _():
        o_ref[...] = (acc_ref[...] / sum_ref[...]).astype(o_ref.dtype)


def flash_attention(needed, grouped_q, gathered, q_ids, q_req, k_ids, k_req, groups, tok_rows, root):
    blocks = gathered.shape[0]
    group_rows = grouped_q.shape[1]
    grid_spec = pltpu.PrefetchScalarGridSpec(
        num_scalar_prefetch=1,
        grid=(groups, blocks),
        in_specs=[
            pl.BlockSpec((None, group_rows, HD), lambda g, kb, n: (g, 0, 0)),
            pl.BlockSpec((None, tok_rows, HD), lambda g, kb, n: (kb, 0, g)),
            pl.BlockSpec((None, tok_rows, HD), lambda g, kb, n: (kb, 0, groups + g)),
            pl.BlockSpec((group_rows, 1), lambda g, kb, n: (0, 0)),
            pl.BlockSpec((group_rows, 1), lambda g, kb, n: (0, 0)),
            pl.BlockSpec((None, 1, tok_rows), lambda g, kb, n: (kb, 0, 0)),
            pl.BlockSpec((None, 1, tok_rows), lambda g, kb, n: (kb, 0, 0)),
        ],
        out_specs=pl.BlockSpec((None, group_rows, HD), lambda g, kb, n: (g, 0, 0)),
        scratch_shapes=[
            pltpu.VMEM((group_rows, 1), jnp.float32),
            pltpu.VMEM((group_rows, 1), jnp.float32),
            pltpu.VMEM((group_rows, HD), jnp.float32),
        ],
    )
    flops = 4 * groups * blocks * group_rows * tok_rows * HD
    return pl.pallas_call(
        functools.partial(flash_kernel, root=root),
        grid_spec=grid_spec,
        out_shape=jax.ShapeDtypeStruct((groups, group_rows, HD), jnp.bfloat16),
        compiler_params=pltpu.CompilerParams(dimension_semantics=("arbitrary", "arbitrary")),
        cost_estimate=pl.CostEstimate(
            flops=flops,
            transcendentals=groups * blocks * group_rows * tok_rows,
            bytes_accessed=2 * groups * blocks * tok_rows * HD * 2 + 4 * groups * group_rows * HD,
        ),
    )(needed, grouped_q, gathered, gathered, q_ids, q_req, k_ids, k_req)


def gather_by_permutes(local, count):
    me = lax.axis_index("kv")
    pieces = [local]
    for shift in range(1, count):
        pieces.append(
            lax.ppermute(local, "kv", perm=[(i, (i + shift) % count) for i in range(count)])
        )
    stacked = jnp.stack(pieces)
    order = (me - jnp.arange(count, dtype=jnp.int32)) % count
    ordered = jnp.take(stacked, order, axis=0)
    return jnp.concatenate([ordered[j] for j in range(count)], axis=1)


def on_device(
    patches,
    merged_grid,
    picture_start,
    vis_gain,
    vis_qkv,
    vis_out,
    merge_weight,
    text_embed,
    dec_gain,
    w_query,
    w_keyval,
    w_out,
    req_lengths,
    final_gain,
    table,
):
    pictures, patch_max, vis_width = patches.shape
    merged_max = patch_max // 4
    vis_cols = vis_qkv.shape[2]
    vis_heads = vis_cols // VHD
    tok_rows, feat_dev = text_embed.shape
    kv_count = D // text_embed.shape[1]
    text_rows = gather_by_permutes(text_embed, kv_count)
    inputs = patches.astype(jnp.float32)
    normed = layer_norm(inputs, vis_gain).astype(jnp.bfloat16)
    packed = jnp.einsum(
        "pnd,dce->pnce", normed, vis_qkv, preferred_element_type=jnp.float32
    ).astype(jnp.bfloat16)
    packed = packed.reshape(pictures, patch_max, 3, vis_heads, VHD)
    scores = jnp.einsum(
        "pqhd,pkhd->phqk", packed[:, :, 0], packed[:, :, 1], preferred_element_type=jnp.float32
    ) / math.sqrt(VHD)
    cell_count = merged_grid[:, 0] * merged_grid[:, 1]
    valid_cols = jnp.arange(patch_max, dtype=jnp.int32)[None, :] < 4 * cell_count[:, None]
    scores = jnp.where(valid_cols[:, None, None, :], scores, -1e30)
    weights = jnp.exp(scores - jnp.max(scores, axis=-1, keepdims=True))
    weight_sum = jnp.sum(weights, axis=-1)
    mixed_rows = jnp.einsum(
        "phqk,pkhd->pqhd",
        weights.astype(jnp.bfloat16),
        packed[:, :, 2],
        preferred_element_type=jnp.float32,
    )
    mixed_rows = (
        (mixed_rows / jnp.transpose(weight_sum, (0, 2, 1))[..., None])
        .astype(jnp.bfloat16)
        .reshape(pictures, patch_max, vis_cols)
    )
    head_part = jnp.einsum("pnc,cd->pnd", mixed_rows, vis_out, preferred_element_type=jnp.float32)
    head_pooled = jnp.mean(head_part.reshape(pictures, merged_max, 4, vis_width), axis=2)
    head_total = lax.psum(head_pooled.astype(jnp.bfloat16), "kv").astype(jnp.float32)
    input_pooled = jnp.mean(inputs.reshape(pictures, merged_max, 4, vis_width), axis=2)
    pooled = (input_pooled + head_total).astype(jnp.bfloat16)
    merged = jnp.einsum(
        "pmd,de->pme", pooled, merge_weight, preferred_element_type=jnp.float32
    ).astype(jnp.bfloat16)
    block_base = lax.axis_index("blk") * tok_rows
    slot_index = jnp.arange(merged_max, dtype=jnp.int32)
    target = picture_start[:, None] + slot_index[None, :] - block_base
    target = jnp.where(slot_index[None, :] < cell_count[:, None], target, -1).reshape(-1)
    local_rows = jnp.arange(tok_rows, dtype=jnp.int32)
    one_hot = local_rows[:, None] == target[None, :]
    placed = jnp.dot(
        one_hot.astype(jnp.bfloat16),
        merged.reshape(pictures * merged_max, feat_dev),
        preferred_element_type=jnp.float32,
    )
    is_vision = jnp.any(one_hot, axis=1)
    seq_in = jnp.where(is_vision[:, None], placed.astype(jnp.bfloat16), text_embed)
    merged_rows = lax.all_gather(
        merged.reshape(pictures * merged_max, feat_dev), "kv", axis=1, tiled=True
    )
    placed_rows = jnp.dot(one_hot.astype(jnp.bfloat16), merged_rows, preferred_element_type=jnp.float32)
    full_rows = jnp.where(is_vision[:, None], placed_rows.astype(jnp.bfloat16), text_rows)
    full_float = full_rows.astype(jnp.float32)
    dec_normed = (
        full_float
        * lax.rsqrt(jnp.mean(full_float * full_float, axis=-1, keepdims=True) + 1e-05)
        * dec_gain
    ).astype(jnp.bfloat16)
    per_group = QHEADS // KVHEADS
    kv_heads = w_keyval.shape[2] // HD
    row_ids = block_base + local_rows
    request_id, request_begin = request_info(row_ids, req_lengths)
    position = row_ids - request_begin
    query_proj = jnp.dot(dec_normed, w_query, preferred_element_type=jnp.float32).reshape(
        tok_rows, kv_heads * per_group, HD
    )
    query_proj = (
        rotate(query_proj, position)
        .astype(jnp.bfloat16)
        .reshape(tok_rows, kv_heads * per_group * HD)
    )
    key_value = jnp.einsum("td,dce->tce", dec_normed, w_keyval, preferred_element_type=jnp.float32)
    key_rows = (
        rotate(key_value[:, 0].reshape(tok_rows, kv_heads, HD), position)
        .astype(jnp.bfloat16)
        .reshape(tok_rows, kv_heads * HD)
    )
    value_rows = key_value[:, 1].astype(jnp.bfloat16)
    query_req, query_begin = request_info(row_ids, req_lengths)
    root = math.sqrt(HD)
    reqs = req_lengths.shape[0]
    ends_at = jnp.cumsum(req_lengths)
    last_ids = ends_at - 1
    picker = (local_rows[None, :] == (last_ids - block_base)[:, None]).astype(jnp.bfloat16)
    query_last = jnp.dot(picker, query_proj, preferred_element_type=jnp.float32)
    seq_last = jnp.dot(picker, seq_in, preferred_element_type=jnp.float32)
    extras = jnp.concatenate([query_last, seq_last], axis=1).astype(jnp.bfloat16).reshape(-1)
    kv_width = key_rows.shape[1]
    ship_width = 2 * kv_width
    extra_rows = -(-extras.shape[0] // ship_width)
    extras = jnp.pad(extras, (0, extra_rows * ship_width - extras.shape[0]))
    shipped = jnp.concatenate([key_rows, value_rows], axis=1)
    shipped = jnp.concatenate([shipped, extras.reshape(extra_rows, ship_width)], axis=0)
    gathered = lax.all_gather(shipped, "blk", axis=0, tiled=False)
    blocks = gathered.shape[0]
    q_cols = query_proj.shape[1]
    extras_all = gathered[:, tok_rows:].reshape(blocks, -1)[:, : reqs * (q_cols + feat_dev)]
    extras_all = jnp.sum(extras_all.astype(jnp.float32).reshape(blocks, reqs, -1), axis=0)
    query_last = extras_all[:, :q_cols].astype(jnp.bfloat16)
    seq_last = extras_all[:, q_cols:]
    block_index = lax.axis_index("blk")
    first_begin = query_begin[0]
    block_ids = jnp.arange(blocks, dtype=jnp.int32)
    needed = (
        (block_ids <= block_index) & (block_ids * tok_rows + tok_rows - 1 >= first_begin)
    ).astype(jnp.int32)
    group_rows = tok_rows * per_group
    grouped_q = jnp.transpose(
        query_proj.reshape(tok_rows, kv_heads, per_group, HD), (1, 0, 2, 3)
    ).reshape(kv_heads, group_rows, HD)
    q_ids = jnp.repeat(row_ids, per_group)[:, None]
    q_req = jnp.repeat(query_req, per_group)[:, None]
    all_ids = jnp.arange(blocks * tok_rows, dtype=jnp.int32)
    all_req, unused = request_info(all_ids, req_lengths)
    k_ids = all_ids.reshape(blocks, 1, tok_rows)
    k_req = all_req.reshape(blocks, 1, tok_rows)
    context = flash_attention(
        needed, grouped_q, gathered, q_ids, q_req, k_ids, k_req, kv_heads, tok_rows, root
    )
    context = jnp.transpose(
        context.reshape(kv_heads, tok_rows, per_group, HD), (1, 0, 2, 3)
    ).reshape(tok_rows, kv_heads * per_group * HD)
    all_ids = jnp.arange(blocks * tok_rows, dtype=jnp.int32)
    last_begin = ends_at - req_lengths
    last_allowed = (all_ids[None, :] >= last_begin[:, None]) & (all_ids[None, :] <= last_ids[:, None])
    last_allowed = last_allowed[:, None, :]
    last_parts = []
    for g in range(kv_heads):
        keys_g = gathered[:, :tok_rows, g * HD : (g + 1) * HD].reshape(blocks * tok_rows, HD)
        values_g = gathered[:, :tok_rows, kv_width + g * HD : kv_width + (g + 1) * HD].reshape(
            blocks * tok_rows, HD
        )
        last_q = query_last[:, g * per_group * HD : (g + 1) * per_group * HD].reshape(
            reqs, per_group, HD
        )
        last_scores = (
            jnp.einsum("tqd,kd->tqk", last_q, keys_g, preferred_element_type=jnp.float32) / root
        )
        last_scores = jnp.where(last_allowed, last_scores, -1e30)
        last_max = jnp.max(last_scores, axis=-1)
        last_weights = jnp.where(last_allowed, jnp.exp(last_scores - last_max[..., None]), 0.0)
        last_sum = jnp.sum(last_weights, axis=-1)
        last_mix = jnp.einsum(
            "tqk,kd->tqd",
            last_weights.astype(jnp.bfloat16),
            values_g,
            preferred_element_type=jnp.float32,
        )
        last_parts.append((last_mix / last_sum[..., None]).reshape(reqs, per_group * HD))
    last_context = jnp.concatenate(last_parts, axis=1).astype(jnp.bfloat16)
    out_rows = jnp.concatenate([context, last_context], axis=0)
    head_sum = lax.psum_scatter(
        jnp.dot(out_rows, w_out, preferred_element_type=jnp.float32).astype(jnp.bfloat16),
        "kv",
        scatter_dimension=1,
        tiled=True,
    ).astype(jnp.float32)
    hidden = (seq_in.astype(jnp.float32) + head_sum[:tok_rows]).astype(jnp.bfloat16)
    chosen = (seq_last + head_sum[tok_rows:]).astype(jnp.bfloat16).astype(jnp.float32)
    square_part = jnp.sum(chosen * chosen, axis=-1)
    scaled = (chosen * final_gain).astype(jnp.bfloat16)
    logit_part = lax.dot_general(
        scaled, table, (((1,), (1,)), ((), ())), preferred_element_type=jnp.float32
    )
    logit_sum, square_sum = (
        lax.psum(logit_part.astype(jnp.bfloat16), "kv").astype(jnp.float32),
        lax.psum(square_part.astype(jnp.bfloat16), "kv").astype(jnp.float32),
    )
    inv_rms = lax.rsqrt(square_sum / D + 1e-05)
    last_norm = (chosen * inv_rms[:, None] * final_gain).astype(jnp.bfloat16)
    local_max = jnp.max(inv_rms[:, None] * logit_sum, axis=-1)
    max_logit = lax.pmax(local_max, "blk")
    return (hidden, last_norm, max_logit)


def solution(mesh):
    placed = (
        P("blk", None, None),
        P("blk", None),
        P("blk"),
        P(),
        P(None, None, "kv"),
        P("kv", None),
        P(None, "kv"),
        P("blk", "kv"),
        P(),
        P(None, "kv"),
        P(None, None, "kv"),
        P("kv", None),
        P(),
        P("kv"),
        P("blk", "kv"),
    )
    return jax.shard_map(
        on_device,
        mesh=mesh,
        in_specs=placed,
        out_specs=(P("blk", "kv"), P(None, "kv"), P()),
        check_vma=False,
    )
```

```python
import functools
import math

import jax
import jax.numpy as jnp
from jax import lax
from jax.experimental import pallas as pl
from jax.experimental.pallas import tpu as pltpu
from jax.sharding import PartitionSpec as P

VHD = 88
D = 4096
QHEADS = 16
KVHEADS = 8
HD = 128


def layer_norm(inputs, gain):
    centre = jnp.mean(inputs, axis=-1, keepdims=True)
    centred = inputs - centre
    spread = jnp.mean(centred * centred, axis=-1, keepdims=True)
    return centred * lax.rsqrt(spread + 1e-06) * gain


def rotate(inputs, position):
    half_width = inputs.shape[-1] // 2
    inverse = 500000.0 ** (-jnp.arange(half_width, dtype=jnp.float32) * 2.0 / inputs.shape[-1])
    angles = position.astype(jnp.float32)[:, None] * inverse[None, :]
    cosine = jnp.cos(angles)[:, None, :]
    sine = jnp.sin(angles)[:, None, :]
    first = inputs[..., :half_width]
    second = inputs[..., half_width:]
    return jnp.concatenate(
        [first * cosine - second * sine, second * cosine + first * sine], axis=-1
    )


def request_info(row_index, req_lengths):
    ends_at = jnp.cumsum(req_lengths)
    starts_at = ends_at - req_lengths
    request_id = jnp.sum((row_index[:, None] >= ends_at[None, :]).astype(jnp.int32), axis=1)
    choose = request_id[:, None] == jnp.arange(req_lengths.shape[0], dtype=jnp.int32)[None, :]
    request_begin = jnp.sum(jnp.where(choose, starts_at[None, :], 0), axis=1)
    return (request_id, request_begin)


def flash_kernel(needed_ref, q_ref, k_ref, v_ref, qid_ref, qreq_ref, kid_ref, kreq_ref, o_ref,
                 max_ref, sum_ref, acc_ref, *, root):
    kb = pl.program_id(1)

    @pl.when(kb == 0)
    def _():
        max_ref[...] = jnp.full(max_ref.shape, -1e30, jnp.float32)
        sum_ref[...] = jnp.zeros(sum_ref.shape, jnp.float32)
        acc_ref[...] = jnp.zeros(acc_ref.shape, jnp.float32)

    @pl.when(needed_ref[kb] != 0)
    def _():
        scores = lax.dot_general(
            q_ref[...], k_ref[...], (((1,), (1,)), ((), ())), preferred_element_type=jnp.float32
        ) / root
        allowed = (kid_ref[...] <= qid_ref[...]) & (kreq_ref[...] == qreq_ref[...])
        scores = jnp.where(allowed, scores, -1e30)
        old_max = max_ref[...]
        new_max = jnp.maximum(old_max, jnp.max(scores, axis=1, keepdims=True))
        weights = jnp.where(allowed, jnp.exp(scores - new_max), 0.0)
        scale = jnp.exp(old_max - new_max)
        sum_ref[...] = sum_ref[...] * scale + jnp.sum(weights, axis=1, keepdims=True)
        acc_ref[...] = acc_ref[...] * scale + jnp.dot(
            weights.astype(jnp.bfloat16), v_ref[...], preferred_element_type=jnp.float32
        )
        max_ref[...] = new_max

    @pl.when(kb == pl.num_programs(1) - 1)
    def _():
        o_ref[...] = (acc_ref[...] / sum_ref[...]).astype(o_ref.dtype)


def flash_attention(needed, grouped_q, gathered, q_ids, q_req, k_ids, k_req, groups, tok_rows, root):
    blocks = gathered.shape[0]
    group_rows = grouped_q.shape[1]
    grid_spec = pltpu.PrefetchScalarGridSpec(
        num_scalar_prefetch=1,
        grid=(groups, blocks),
        in_specs=[
            pl.BlockSpec((None, group_rows, HD), lambda g, kb, n: (g, 0, 0)),
            pl.BlockSpec((None, tok_rows, HD), lambda g, kb, n: (kb, 0, g)),
            pl.BlockSpec((None, tok_rows, HD), lambda g, kb, n: (kb, 0, groups + g)),
            pl.BlockSpec((group_rows, 1), lambda g, kb, n: (0, 0)),
            pl.BlockSpec((group_rows, 1), lambda g, kb, n: (0, 0)),
            pl.BlockSpec((None, 1, tok_rows), lambda g, kb, n: (kb, 0, 0)),
            pl.BlockSpec((None, 1, tok_rows), lambda g, kb, n: (kb, 0, 0)),
        ],
        out_specs=pl.BlockSpec((None, group_rows, HD), lambda g, kb, n: (g, 0, 0)),
        scratch_shapes=[
            pltpu.VMEM((group_rows, 1), jnp.float32),
            pltpu.VMEM((group_rows, 1), jnp.float32),
            pltpu.VMEM((group_rows, HD), jnp.float32),
        ],
    )
    flops = 4 * groups * blocks * group_rows * tok_rows * HD
    return pl.pallas_call(
        functools.partial(flash_kernel, root=root),
        grid_spec=grid_spec,
        out_shape=jax.ShapeDtypeStruct((groups, group_rows, HD), jnp.bfloat16),
        compiler_params=pltpu.CompilerParams(dimension_semantics=("arbitrary", "arbitrary")),
        cost_estimate=pl.CostEstimate(
            flops=flops,
            transcendentals=groups * blocks * group_rows * tok_rows,
            bytes_accessed=2 * groups * blocks * tok_rows * HD * 2 + 4 * groups * group_rows * HD,
        ),
    )(needed, grouped_q, gathered, gathered, q_ids, q_req, k_ids, k_req)


def permute_pieces(local, count):
    pieces = [local]
    for shift in range(1, count):
        pieces.append(
            lax.ppermute(local, "kv", perm=[(i, (i + shift) % count) for i in range(count)])
        )
    return pieces


def ordered_sum(pieces, count):
    me = lax.axis_index("kv")
    stacked = jnp.stack([piece.astype(jnp.float32) for piece in pieces])
    order = (me - jnp.arange(count, dtype=jnp.int32)) % count
    return jnp.sum(jnp.take(stacked, order, axis=0), axis=0)


def tree_max(values, axis, count):
    if count & (count - 1):
        return lax.pmax(values, axis)
    step = 1
    while step < count:
        other = lax.ppermute(values, axis, perm=[(i, i ^ step) for i in range(count)])
        values = jnp.maximum(values, other)
        step *= 2
    return values


def on_device(
    patches,
    merged_grid,
    picture_start,
    vis_gain,
    vis_qkv,
    vis_out,
    merge_weight,
    text_embed,
    dec_gain,
    w_query,
    w_keyval,
    w_out,
    req_lengths,
    final_gain,
    table,
):
    pictures, patch_max, vis_width = patches.shape
    merged_max = patch_max // 4
    vis_cols = vis_qkv.shape[2]
    vis_heads = vis_cols // VHD
    tok_rows, feat_dev = text_embed.shape
    kv_count = D // text_embed.shape[1]
    text_pieces = permute_pieces(text_embed, kv_count)
    inputs = patches.astype(jnp.float32)
    normed = layer_norm(inputs, vis_gain).astype(jnp.bfloat16)
    packed = jnp.einsum(
        "pnd,dce->pnce", normed, vis_qkv, preferred_element_type=jnp.float32
    ).astype(jnp.bfloat16)
    packed = packed.reshape(pictures, patch_max, 3, vis_heads, VHD)
    scores = jnp.einsum(
        "pqhd,pkhd->phqk", packed[:, :, 0], packed[:, :, 1], preferred_element_type=jnp.float32
    ) / math.sqrt(VHD)
    cell_count = merged_grid[:, 0] * merged_grid[:, 1]
    valid_cols = jnp.arange(patch_max, dtype=jnp.int32)[None, :] < 4 * cell_count[:, None]
    scores = jnp.where(valid_cols[:, None, None, :], scores, -1e30)
    weights = jnp.exp(scores - jnp.max(scores, axis=-1, keepdims=True))
    weight_sum = jnp.sum(weights, axis=-1)
    mixed_rows = jnp.einsum(
        "phqk,pkhd->pqhd",
        weights.astype(jnp.bfloat16),
        packed[:, :, 2],
        preferred_element_type=jnp.float32,
    )
    mixed_rows = (
        (mixed_rows / jnp.transpose(weight_sum, (0, 2, 1))[..., None])
        .astype(jnp.bfloat16)
        .reshape(pictures, patch_max, vis_cols)
    )
    head_part = jnp.einsum("pnc,cd->pnd", mixed_rows, vis_out, preferred_element_type=jnp.float32)
    head_pooled = jnp.mean(head_part.reshape(pictures, merged_max, 4, vis_width), axis=2)
    head_total = ordered_sum(permute_pieces(head_pooled.astype(jnp.bfloat16), kv_count), kv_count)
    input_pooled = jnp.mean(inputs.reshape(pictures, merged_max, 4, vis_width), axis=2)
    pooled = (input_pooled + head_total).astype(jnp.bfloat16)
    merged = jnp.einsum(
        "pmd,de->pme", pooled, merge_weight, preferred_element_type=jnp.float32
    ).astype(jnp.bfloat16)
    block_base = lax.axis_index("blk") * tok_rows
    slot_index = jnp.arange(merged_max, dtype=jnp.int32)
    target = picture_start[:, None] + slot_index[None, :] - block_base
    target = jnp.where(slot_index[None, :] < cell_count[:, None], target, -1).reshape(-1)
    local_rows = jnp.arange(tok_rows, dtype=jnp.int32)
    one_hot = local_rows[:, None] == target[None, :]
    placed = jnp.dot(
        one_hot.astype(jnp.bfloat16),
        merged.reshape(pictures * merged_max, feat_dev),
        preferred_element_type=jnp.float32,
    )
    is_vision = jnp.any(one_hot, axis=1)
    seq_in = jnp.where(is_vision[:, None], placed.astype(jnp.bfloat16), text_embed)
    per_group = QHEADS // KVHEADS
    kv_heads = w_keyval.shape[2] // HD
    row_ids = block_base + local_rows
    request_id, request_begin = request_info(row_ids, req_lengths)
    position = row_ids - request_begin
    merged_pieces = permute_pieces(merged.reshape(pictures * merged_max, feat_dev), kv_count)
    one_hot_rows = one_hot.astype(jnp.bfloat16)
    full_pieces = [
        jnp.where(
            is_vision[:, None],
            jnp.dot(one_hot_rows, merged_piece, preferred_element_type=jnp.float32).astype(
                jnp.bfloat16
            ),
            text_piece,
        ).astype(jnp.float32)
        for merged_piece, text_piece in zip(merged_pieces, text_pieces)
    ]
    square_sum_rows = sum(jnp.sum(piece * piece, axis=1) for piece in full_pieces)
    row_scale = lax.rsqrt(square_sum_rows / (kv_count * feat_dev) + 1e-05)[:, None]
    me_kv = lax.axis_index("kv")
    query_proj = None
    key_value = None
    for shift, piece in enumerate(full_pieces):
        chunk = ((me_kv - shift) % kv_count) * feat_dev
        normed_piece = (
            piece * row_scale * lax.dynamic_slice_in_dim(dec_gain, chunk, feat_dev)
        ).astype(jnp.bfloat16)
        q_term = jnp.dot(
            normed_piece,
            lax.dynamic_slice_in_dim(w_query, chunk, feat_dev, 0),
            preferred_element_type=jnp.float32,
        )
        kv_term = jnp.einsum(
            "td,dce->tce",
            normed_piece,
            lax.dynamic_slice_in_dim(w_keyval, chunk, feat_dev, 0),
            preferred_element_type=jnp.float32,
        )
        query_proj = q_term if query_proj is None else query_proj + q_term
        key_value = kv_term if key_value is None else key_value + kv_term
    query_proj = query_proj.reshape(tok_rows, kv_heads * per_group, HD)
    query_proj = (
        rotate(query_proj, position)
        .astype(jnp.bfloat16)
        .reshape(tok_rows, kv_heads * per_group * HD)
    )
    key_rows = (
        rotate(key_value[:, 0].reshape(tok_rows, kv_heads, HD), position)
        .astype(jnp.bfloat16)
        .reshape(tok_rows, kv_heads * HD)
    )
    value_rows = key_value[:, 1].astype(jnp.bfloat16)
    query_req, query_begin = request_info(row_ids, req_lengths)
    root = math.sqrt(HD)
    reqs = req_lengths.shape[0]
    ends_at = jnp.cumsum(req_lengths)
    last_ids = ends_at - 1
    picker = (local_rows[None, :] == (last_ids - block_base)[:, None]).astype(jnp.bfloat16)
    query_last = jnp.dot(picker, query_proj, preferred_element_type=jnp.float32)
    seq_last = jnp.dot(picker, seq_in, preferred_element_type=jnp.float32)
    extras = jnp.concatenate([query_last, seq_last], axis=1).astype(jnp.bfloat16).reshape(-1)
    kv_width = key_rows.shape[1]
    ship_width = 2 * kv_width
    extra_rows = -(-extras.shape[0] // ship_width)
    extras = jnp.pad(extras, (0, extra_rows * ship_width - extras.shape[0]))
    shipped = jnp.concatenate([key_rows, value_rows], axis=1)
    shipped = jnp.concatenate([shipped, extras.reshape(extra_rows, ship_width)], axis=0)
    gathered = lax.all_gather(shipped, "blk", axis=0, tiled=False)
    blocks = gathered.shape[0]
    q_cols = query_proj.shape[1]
    extras_all = gathered[:, tok_rows:].reshape(blocks, -1)[:, : reqs * (q_cols + feat_dev)]
    extras_all = jnp.sum(extras_all.astype(jnp.float32).reshape(blocks, reqs, -1), axis=0)
    query_last = extras_all[:, :q_cols].astype(jnp.bfloat16)
    seq_last = extras_all[:, q_cols:]
    block_index = lax.axis_index("blk")
    first_begin = query_begin[0]
    block_ids = jnp.arange(blocks, dtype=jnp.int32)
    needed = (
        (block_ids <= block_index) & (block_ids * tok_rows + tok_rows - 1 >= first_begin)
    ).astype(jnp.int32)
    group_rows = tok_rows * per_group
    grouped_q = jnp.transpose(
        query_proj.reshape(tok_rows, kv_heads, per_group, HD), (1, 0, 2, 3)
    ).reshape(kv_heads, group_rows, HD)
    q_ids = jnp.repeat(row_ids, per_group)[:, None]
    q_req = jnp.repeat(query_req, per_group)[:, None]
    all_ids = jnp.arange(blocks * tok_rows, dtype=jnp.int32)
    all_req, unused = request_info(all_ids, req_lengths)
    k_ids = all_ids.reshape(blocks, 1, tok_rows)
    k_req = all_req.reshape(blocks, 1, tok_rows)
    context = flash_attention(
        needed, grouped_q, gathered, q_ids, q_req, k_ids, k_req, kv_heads, tok_rows, root
    )
    context = jnp.transpose(
        context.reshape(kv_heads, tok_rows, per_group, HD), (1, 0, 2, 3)
    ).reshape(tok_rows, kv_heads * per_group * HD)
    all_ids = jnp.arange(blocks * tok_rows, dtype=jnp.int32)
    last_begin = ends_at - req_lengths
    last_allowed = (all_ids[None, :] >= last_begin[:, None]) & (all_ids[None, :] <= last_ids[:, None])
    last_allowed = last_allowed[:, None, :]
    last_parts = []
    for g in range(kv_heads):
        keys_g = gathered[:, :tok_rows, g * HD : (g + 1) * HD].reshape(blocks * tok_rows, HD)
        values_g = gathered[:, :tok_rows, kv_width + g * HD : kv_width + (g + 1) * HD].reshape(
            blocks * tok_rows, HD
        )
        last_q = query_last[:, g * per_group * HD : (g + 1) * per_group * HD].reshape(
            reqs, per_group, HD
        )
        last_scores = (
            jnp.einsum("tqd,kd->tqk", last_q, keys_g, preferred_element_type=jnp.float32) / root
        )
        last_scores = jnp.where(last_allowed, last_scores, -1e30)
        last_max = jnp.max(last_scores, axis=-1)
        last_weights = jnp.where(last_allowed, jnp.exp(last_scores - last_max[..., None]), 0.0)
        last_sum = jnp.sum(last_weights, axis=-1)
        last_mix = jnp.einsum(
            "tqk,kd->tqd",
            last_weights.astype(jnp.bfloat16),
            values_g,
            preferred_element_type=jnp.float32,
        )
        last_parts.append((last_mix / last_sum[..., None]).reshape(reqs, per_group * HD))
    last_context = jnp.concatenate(last_parts, axis=1).astype(jnp.bfloat16)
    out_rows = jnp.concatenate([context, last_context], axis=0)
    head_sum = lax.psum_scatter(
        jnp.dot(out_rows, w_out, preferred_element_type=jnp.float32).astype(jnp.bfloat16),
        "kv",
        scatter_dimension=1,
        tiled=True,
    ).astype(jnp.float32)
    hidden = (seq_in.astype(jnp.float32) + head_sum[:tok_rows]).astype(jnp.bfloat16)
    chosen = (seq_last + head_sum[tok_rows:]).astype(jnp.bfloat16).astype(jnp.float32)
    square_part = jnp.sum(chosen * chosen, axis=-1)
    scaled = (chosen * final_gain).astype(jnp.bfloat16)
    logit_part = lax.dot_general(
        scaled, table, (((1,), (1,)), ((), ())), preferred_element_type=jnp.float32
    )
    packed_sums = ordered_sum(
        permute_pieces(jnp.concatenate([logit_part, square_part[:, None]], axis=1), kv_count),
        kv_count,
    )
    logit_sum = packed_sums[:, :-1]
    square_sum = packed_sums[:, -1]
    inv_rms = lax.rsqrt(square_sum / D + 1e-05)
    last_norm = (chosen * inv_rms[:, None] * final_gain).astype(jnp.bfloat16)
    local_max = jnp.max(inv_rms[:, None] * logit_sum, axis=-1)
    max_logit = tree_max(local_max, "blk", blocks)
    return (hidden, last_norm, max_logit)


def solution(mesh):
    placed = (
        P("blk", None, None),
        P("blk", None),
        P("blk"),
        P(),
        P(None, None, "kv"),
        P("kv", None),
        P(None, "kv"),
        P("blk", "kv"),
        P(),
        P(None, "kv"),
        P(None, None, "kv"),
        P("kv", None),
        P(),
        P("kv"),
        P("blk", "kv"),
    )
    return jax.shard_map(
        on_device,
        mesh=mesh,
        in_specs=placed,
        out_specs=(P("blk", "kv"), P(None, "kv"), P()),
        check_vma=False,
    )
```

```python
import functools
import math

import jax
import jax.numpy as jnp
from jax import lax
from jax.experimental import pallas as pl
from jax.experimental.pallas import tpu as pltpu
from jax.sharding import PartitionSpec as P

VHD = 88
D = 4096
QHEADS = 16
KVHEADS = 8
HD = 128


def layer_norm(inputs, gain):
    centre = jnp.mean(inputs, axis=-1, keepdims=True)
    centred = inputs - centre
    spread = jnp.mean(centred * centred, axis=-1, keepdims=True)
    return centred * lax.rsqrt(spread + 1e-06) * gain


def rotate(inputs, position):
    half_width = inputs.shape[-1] // 2
    inverse = 500000.0 ** (-jnp.arange(half_width, dtype=jnp.float32) * 2.0 / inputs.shape[-1])
    angles = position.astype(jnp.float32)[:, None] * inverse[None, :]
    cosine = jnp.cos(angles)[:, None, :]
    sine = jnp.sin(angles)[:, None, :]
    first = inputs[..., :half_width]
    second = inputs[..., half_width:]
    return jnp.concatenate(
        [first * cosine - second * sine, second * cosine + first * sine], axis=-1
    )


def request_info(row_index, req_lengths):
    ends_at = jnp.cumsum(req_lengths)
    starts_at = ends_at - req_lengths
    request_id = jnp.sum((row_index[:, None] >= ends_at[None, :]).astype(jnp.int32), axis=1)
    choose = request_id[:, None] == jnp.arange(req_lengths.shape[0], dtype=jnp.int32)[None, :]
    request_begin = jnp.sum(jnp.where(choose, starts_at[None, :], 0), axis=1)
    return (request_id, request_begin)


def flash_kernel(needed_ref, q_ref, k_ref, v_ref, qid_ref, qreq_ref, kid_ref, kreq_ref, o_ref,
                 max_ref, sum_ref, acc_ref, *, root):
    kb = pl.program_id(1)

    @pl.when(kb == 0)
    def _():
        max_ref[...] = jnp.full(max_ref.shape, -1e30, jnp.float32)
        sum_ref[...] = jnp.zeros(sum_ref.shape, jnp.float32)
        acc_ref[...] = jnp.zeros(acc_ref.shape, jnp.float32)

    @pl.when(needed_ref[kb] != 0)
    def _():
        scores = lax.dot_general(
            q_ref[...], k_ref[...], (((1,), (1,)), ((), ())), preferred_element_type=jnp.float32
        ) / root
        allowed = (kid_ref[...] <= qid_ref[...]) & (kreq_ref[...] == qreq_ref[...])
        scores = jnp.where(allowed, scores, -1e30)
        old_max = max_ref[...]
        new_max = jnp.maximum(old_max, jnp.max(scores, axis=1, keepdims=True))
        weights = jnp.where(allowed, jnp.exp(scores - new_max), 0.0)
        scale = jnp.exp(old_max - new_max)
        sum_ref[...] = sum_ref[...] * scale + jnp.sum(weights, axis=1, keepdims=True)
        acc_ref[...] = acc_ref[...] * scale + jnp.dot(
            weights.astype(jnp.bfloat16), v_ref[...], preferred_element_type=jnp.float32
        )
        max_ref[...] = new_max

    @pl.when(kb == pl.num_programs(1) - 1)
    def _():
        o_ref[...] = (acc_ref[...] / sum_ref[...]).astype(o_ref.dtype)


def flash_attention(needed, grouped_q, gathered, q_ids, q_req, k_ids, k_req, groups, tok_rows, root):
    blocks = gathered.shape[0]
    group_rows = grouped_q.shape[1]
    grid_spec = pltpu.PrefetchScalarGridSpec(
        num_scalar_prefetch=1,
        grid=(groups, blocks),
        in_specs=[
            pl.BlockSpec((None, group_rows, HD), lambda g, kb, n: (g, 0, 0)),
            pl.BlockSpec((None, tok_rows, HD), lambda g, kb, n: (kb, 0, g)),
            pl.BlockSpec((None, tok_rows, HD), lambda g, kb, n: (kb, 0, groups + g)),
            pl.BlockSpec((group_rows, 1), lambda g, kb, n: (0, 0)),
            pl.BlockSpec((group_rows, 1), lambda g, kb, n: (0, 0)),
            pl.BlockSpec((None, 1, tok_rows), lambda g, kb, n: (kb, 0, 0)),
            pl.BlockSpec((None, 1, tok_rows), lambda g, kb, n: (kb, 0, 0)),
        ],
        out_specs=pl.BlockSpec((None, group_rows, HD), lambda g, kb, n: (g, 0, 0)),
        scratch_shapes=[
            pltpu.VMEM((group_rows, 1), jnp.float32),
            pltpu.VMEM((group_rows, 1), jnp.float32),
            pltpu.VMEM((group_rows, HD), jnp.float32),
        ],
    )
    flops = 4 * groups * blocks * group_rows * tok_rows * HD
    return pl.pallas_call(
        functools.partial(flash_kernel, root=root),
        grid_spec=grid_spec,
        out_shape=jax.ShapeDtypeStruct((groups, group_rows, HD), jnp.bfloat16),
        compiler_params=pltpu.CompilerParams(dimension_semantics=("arbitrary", "arbitrary")),
        cost_estimate=pl.CostEstimate(
            flops=flops,
            transcendentals=groups * blocks * group_rows * tok_rows,
            bytes_accessed=2 * groups * blocks * tok_rows * HD * 2 + 4 * groups * group_rows * HD,
        ),
    )(needed, grouped_q, gathered, gathered, q_ids, q_req, k_ids, k_req)


def gather_by_permutes(local, count):
    me = lax.axis_index("kv")
    pieces = [local]
    for shift in range(1, count):
        pieces.append(
            lax.ppermute(local, "kv", perm=[(i, (i + shift) % count) for i in range(count)])
        )
    stacked = jnp.stack(pieces)
    order = (me - jnp.arange(count, dtype=jnp.int32)) % count
    ordered = jnp.take(stacked, order, axis=0)
    return jnp.concatenate([ordered[j] for j in range(count)], axis=1)


def permute_pieces(local, count):
    pieces = [local]
    for shift in range(1, count):
        pieces.append(
            lax.ppermute(local, "kv", perm=[(i, (i + shift) % count) for i in range(count)])
        )
    return pieces


def ordered_sum(pieces, count):
    me = lax.axis_index("kv")
    stacked = jnp.stack([piece.astype(jnp.float32) for piece in pieces])
    order = (me - jnp.arange(count, dtype=jnp.int32)) % count
    return jnp.sum(jnp.take(stacked, order, axis=0), axis=0)


def tree_max(values, axis, count):
    if count & (count - 1):
        return lax.pmax(values, axis)
    step = 1
    while step < count:
        other = lax.ppermute(values, axis, perm=[(i, i ^ step) for i in range(count)])
        values = jnp.maximum(values, other)
        step *= 2
    return values


def on_device(
    patches,
    merged_grid,
    picture_start,
    vis_gain,
    vis_qkv,
    vis_out,
    merge_weight,
    text_embed,
    dec_gain,
    w_query,
    w_keyval,
    w_out,
    req_lengths,
    final_gain,
    table,
):
    pictures, patch_max, vis_width = patches.shape
    merged_max = patch_max // 4
    vis_cols = vis_qkv.shape[2]
    vis_heads = vis_cols // VHD
    tok_rows, feat_dev = text_embed.shape
    kv_count = D // text_embed.shape[1]
    text_rows = gather_by_permutes(text_embed, kv_count)
    inputs = patches.astype(jnp.float32)
    normed = layer_norm(inputs, vis_gain).astype(jnp.bfloat16)
    packed = jnp.einsum(
        "pnd,dce->pnce", normed, vis_qkv, preferred_element_type=jnp.float32
    ).astype(jnp.bfloat16)
    packed = packed.reshape(pictures, patch_max, 3, vis_heads, VHD)
    scores = jnp.einsum(
        "pqhd,pkhd->phqk", packed[:, :, 0], packed[:, :, 1], preferred_element_type=jnp.float32
    ) / math.sqrt(VHD)
    cell_count = merged_grid[:, 0] * merged_grid[:, 1]
    valid_cols = jnp.arange(patch_max, dtype=jnp.int32)[None, :] < 4 * cell_count[:, None]
    scores = jnp.where(valid_cols[:, None, None, :], scores, -1e30)
    weights = jnp.exp(scores - jnp.max(scores, axis=-1, keepdims=True))
    weight_sum = jnp.sum(weights, axis=-1)
    mixed_rows = jnp.einsum(
        "phqk,pkhd->pqhd",
        weights.astype(jnp.bfloat16),
        packed[:, :, 2],
        preferred_element_type=jnp.float32,
    )
    mixed_rows = (
        (mixed_rows / jnp.transpose(weight_sum, (0, 2, 1))[..., None])
        .astype(jnp.bfloat16)
        .reshape(pictures, patch_max, vis_cols)
    )
    head_part = jnp.einsum("pnc,cd->pnd", mixed_rows, vis_out, preferred_element_type=jnp.float32)
    head_pooled = jnp.mean(head_part.reshape(pictures, merged_max, 4, vis_width), axis=2)
    head_total = lax.psum(head_pooled.astype(jnp.bfloat16), "kv").astype(jnp.float32)
    input_pooled = jnp.mean(inputs.reshape(pictures, merged_max, 4, vis_width), axis=2)
    pooled = (input_pooled + head_total).astype(jnp.bfloat16)
    merged = jnp.einsum(
        "pmd,de->pme", pooled, merge_weight, preferred_element_type=jnp.float32
    ).astype(jnp.bfloat16)
    block_base = lax.axis_index("blk") * tok_rows
    slot_index = jnp.arange(merged_max, dtype=jnp.int32)
    target = picture_start[:, None] + slot_index[None, :] - block_base
    target = jnp.where(slot_index[None, :] < cell_count[:, None], target, -1).reshape(-1)
    local_rows = jnp.arange(tok_rows, dtype=jnp.int32)
    one_hot = local_rows[:, None] == target[None, :]
    placed = jnp.dot(
        one_hot.astype(jnp.bfloat16),
        merged.reshape(pictures * merged_max, feat_dev),
        preferred_element_type=jnp.float32,
    )
    is_vision = jnp.any(one_hot, axis=1)
    seq_in = jnp.where(is_vision[:, None], placed.astype(jnp.bfloat16), text_embed)
    merged_rows = lax.all_gather(
        merged.reshape(pictures * merged_max, feat_dev), "kv", axis=1, tiled=True
    )
    placed_rows = jnp.dot(one_hot.astype(jnp.bfloat16), merged_rows, preferred_element_type=jnp.float32)
    full_rows = jnp.where(is_vision[:, None], placed_rows.astype(jnp.bfloat16), text_rows)
    full_float = full_rows.astype(jnp.float32)
    dec_normed = (
        full_float
        * lax.rsqrt(jnp.mean(full_float * full_float, axis=-1, keepdims=True) + 1e-05)
        * dec_gain
    ).astype(jnp.bfloat16)
    per_group = QHEADS // KVHEADS
    kv_heads = w_keyval.shape[2] // HD
    row_ids = block_base + local_rows
    request_id, request_begin = request_info(row_ids, req_lengths)
    position = row_ids - request_begin
    query_proj = jnp.dot(dec_normed, w_query, preferred_element_type=jnp.float32).reshape(
        tok_rows, kv_heads * per_group, HD
    )
    query_proj = (
        rotate(query_proj, position)
        .astype(jnp.bfloat16)
        .reshape(tok_rows, kv_heads * per_group * HD)
    )
    key_value = jnp.einsum("td,dce->tce", dec_normed, w_keyval, preferred_element_type=jnp.float32)
    key_rows = (
        rotate(key_value[:, 0].reshape(tok_rows, kv_heads, HD), position)
        .astype(jnp.bfloat16)
        .reshape(tok_rows, kv_heads * HD)
    )
    value_rows = key_value[:, 1].astype(jnp.bfloat16)
    query_req, query_begin = request_info(row_ids, req_lengths)
    root = math.sqrt(HD)
    reqs = req_lengths.shape[0]
    ends_at = jnp.cumsum(req_lengths)
    last_ids = ends_at - 1
    picker = (local_rows[None, :] == (last_ids - block_base)[:, None]).astype(jnp.bfloat16)
    query_last = jnp.dot(picker, query_proj, preferred_element_type=jnp.float32)
    seq_last = jnp.dot(picker, seq_in, preferred_element_type=jnp.float32)
    extras = jnp.concatenate([query_last, seq_last], axis=1).astype(jnp.bfloat16).reshape(-1)
    kv_width = key_rows.shape[1]
    ship_width = 2 * kv_width
    extra_rows = -(-extras.shape[0] // ship_width)
    extras = jnp.pad(extras, (0, extra_rows * ship_width - extras.shape[0]))
    shipped = jnp.concatenate([key_rows, value_rows], axis=1)
    shipped = jnp.concatenate([shipped, extras.reshape(extra_rows, ship_width)], axis=0)
    gathered = lax.all_gather(shipped, "blk", axis=0, tiled=False)
    blocks = gathered.shape[0]
    q_cols = query_proj.shape[1]
    extras_all = gathered[:, tok_rows:].reshape(blocks, -1)[:, : reqs * (q_cols + feat_dev)]
    extras_all = jnp.sum(extras_all.astype(jnp.float32).reshape(blocks, reqs, -1), axis=0)
    query_last = extras_all[:, :q_cols].astype(jnp.bfloat16)
    seq_last = extras_all[:, q_cols:]
    block_index = lax.axis_index("blk")
    first_begin = query_begin[0]
    block_ids = jnp.arange(blocks, dtype=jnp.int32)
    needed = (
        (block_ids <= block_index) & (block_ids * tok_rows + tok_rows - 1 >= first_begin)
    ).astype(jnp.int32)
    group_rows = tok_rows * per_group
    grouped_q = jnp.transpose(
        query_proj.reshape(tok_rows, kv_heads, per_group, HD), (1, 0, 2, 3)
    ).reshape(kv_heads, group_rows, HD)
    q_ids = jnp.repeat(row_ids, per_group)[:, None]
    q_req = jnp.repeat(query_req, per_group)[:, None]
    all_ids = jnp.arange(blocks * tok_rows, dtype=jnp.int32)
    all_req, unused = request_info(all_ids, req_lengths)
    k_ids = all_ids.reshape(blocks, 1, tok_rows)
    k_req = all_req.reshape(blocks, 1, tok_rows)
    context = flash_attention(
        needed, grouped_q, gathered, q_ids, q_req, k_ids, k_req, kv_heads, tok_rows, root
    )
    context = jnp.transpose(
        context.reshape(kv_heads, tok_rows, per_group, HD), (1, 0, 2, 3)
    ).reshape(tok_rows, kv_heads * per_group * HD)
    all_ids = jnp.arange(blocks * tok_rows, dtype=jnp.int32)
    last_begin = ends_at - req_lengths
    last_allowed = (all_ids[None, :] >= last_begin[:, None]) & (all_ids[None, :] <= last_ids[:, None])
    last_allowed = last_allowed[:, None, :]
    last_parts = []
    for g in range(kv_heads):
        keys_g = gathered[:, :tok_rows, g * HD : (g + 1) * HD].reshape(blocks * tok_rows, HD)
        values_g = gathered[:, :tok_rows, kv_width + g * HD : kv_width + (g + 1) * HD].reshape(
            blocks * tok_rows, HD
        )
        last_q = query_last[:, g * per_group * HD : (g + 1) * per_group * HD].reshape(
            reqs, per_group, HD
        )
        last_scores = (
            jnp.einsum("tqd,kd->tqk", last_q, keys_g, preferred_element_type=jnp.float32) / root
        )
        last_scores = jnp.where(last_allowed, last_scores, -1e30)
        last_max = jnp.max(last_scores, axis=-1)
        last_weights = jnp.where(last_allowed, jnp.exp(last_scores - last_max[..., None]), 0.0)
        last_sum = jnp.sum(last_weights, axis=-1)
        last_mix = jnp.einsum(
            "tqk,kd->tqd",
            last_weights.astype(jnp.bfloat16),
            values_g,
            preferred_element_type=jnp.float32,
        )
        last_parts.append((last_mix / last_sum[..., None]).reshape(reqs, per_group * HD))
    last_context = jnp.concatenate(last_parts, axis=1).astype(jnp.bfloat16)
    out_rows = jnp.concatenate([context, last_context], axis=0)
    head_sum = lax.psum_scatter(
        jnp.dot(out_rows, w_out, preferred_element_type=jnp.float32).astype(jnp.bfloat16),
        "kv",
        scatter_dimension=1,
        tiled=True,
    ).astype(jnp.float32)
    hidden = (seq_in.astype(jnp.float32) + head_sum[:tok_rows]).astype(jnp.bfloat16)
    chosen = (seq_last + head_sum[tok_rows:]).astype(jnp.bfloat16).astype(jnp.float32)
    square_part = jnp.sum(chosen * chosen, axis=-1)
    scaled = (chosen * final_gain).astype(jnp.bfloat16)
    logit_part = lax.dot_general(
        scaled, table, (((1,), (1,)), ((), ())), preferred_element_type=jnp.float32
    )
    packed_sums = ordered_sum(
        permute_pieces(jnp.concatenate([logit_part, square_part[:, None]], axis=1), kv_count),
        kv_count,
    )
    logit_sum = packed_sums[:, :-1]
    square_sum = packed_sums[:, -1]
    inv_rms = lax.rsqrt(square_sum / D + 1e-05)
    last_norm = (chosen * inv_rms[:, None] * final_gain).astype(jnp.bfloat16)
    local_max = jnp.max(inv_rms[:, None] * logit_sum, axis=-1)
    max_logit = tree_max(local_max, "blk", blocks)
    return (hidden, last_norm, max_logit)


def solution(mesh):
    placed = (
        P("blk", None, None),
        P("blk", None),
        P("blk"),
        P(),
        P(None, None, "kv"),
        P("kv", None),
        P(None, "kv"),
        P("blk", "kv"),
        P(),
        P(None, "kv"),
        P(None, None, "kv"),
        P("kv", None),
        P(),
        P("kv"),
        P("blk", "kv"),
    )
    return jax.shard_map(
        on_device,
        mesh=mesh,
        in_specs=placed,
        out_specs=(P("blk", "kv"), P(None, "kv"), P()),
        check_vma=False,
    )
```

```python
import functools
import math

import jax
import jax.numpy as jnp
from jax import lax
from jax.experimental import pallas as pl
from jax.experimental.pallas import tpu as pltpu
from jax.sharding import PartitionSpec as P

VHD = 88
D = 4096
QHEADS = 16
KVHEADS = 8
HD = 128


def layer_norm(inputs, gain):
    centre = jnp.mean(inputs, axis=-1, keepdims=True)
    centred = inputs - centre
    spread = jnp.mean(centred * centred, axis=-1, keepdims=True)
    return centred * lax.rsqrt(spread + 1e-06) * gain


def rotate(inputs, position):
    half_width = inputs.shape[-1] // 2
    inverse = 500000.0 ** (-jnp.arange(half_width, dtype=jnp.float32) * 2.0 / inputs.shape[-1])
    angles = position.astype(jnp.float32)[:, None] * inverse[None, :]
    cosine = jnp.cos(angles)[:, None, :]
    sine = jnp.sin(angles)[:, None, :]
    first = inputs[..., :half_width]
    second = inputs[..., half_width:]
    return jnp.concatenate(
        [first * cosine - second * sine, second * cosine + first * sine], axis=-1
    )


def request_info(row_index, req_lengths):
    ends_at = jnp.cumsum(req_lengths)
    starts_at = ends_at - req_lengths
    request_id = jnp.sum((row_index[:, None] >= ends_at[None, :]).astype(jnp.int32), axis=1)
    choose = request_id[:, None] == jnp.arange(req_lengths.shape[0], dtype=jnp.int32)[None, :]
    request_begin = jnp.sum(jnp.where(choose, starts_at[None, :], 0), axis=1)
    return (request_id, request_begin)


def flash_kernel(needed_ref, q_ref, k_ref, v_ref, qid_ref, qreq_ref, kid_ref, kreq_ref, o_ref,
                 max_ref, sum_ref, acc_ref, *, root):
    kb = pl.program_id(1)

    @pl.when(kb == 0)
    def _():
        max_ref[...] = jnp.full(max_ref.shape, -1e30, jnp.float32)
        sum_ref[...] = jnp.zeros(sum_ref.shape, jnp.float32)
        acc_ref[...] = jnp.zeros(acc_ref.shape, jnp.float32)

    @pl.when(needed_ref[kb] != 0)
    def _():
        scores = lax.dot_general(
            q_ref[...], k_ref[...], (((1,), (1,)), ((), ())), preferred_element_type=jnp.float32
        ) / root
        allowed = (kid_ref[...] <= qid_ref[...]) & (kreq_ref[...] == qreq_ref[...])
        scores = jnp.where(allowed, scores, -1e30)
        old_max = max_ref[...]
        new_max = jnp.maximum(old_max, jnp.max(scores, axis=1, keepdims=True))
        weights = jnp.where(allowed, jnp.exp(scores - new_max), 0.0)
        scale = jnp.exp(old_max - new_max)
        sum_ref[...] = sum_ref[...] * scale + jnp.sum(weights, axis=1, keepdims=True)
        acc_ref[...] = acc_ref[...] * scale + jnp.dot(
            weights.astype(jnp.bfloat16), v_ref[...], preferred_element_type=jnp.float32
        )
        max_ref[...] = new_max

    @pl.when(kb == pl.num_programs(1) - 1)
    def _():
        o_ref[...] = (acc_ref[...] / sum_ref[...]).astype(o_ref.dtype)


def flash_attention(needed, grouped_q, gathered, q_ids, q_req, k_ids, k_req, groups, tok_rows, root):
    blocks = gathered.shape[0]
    group_rows = grouped_q.shape[1]
    grid_spec = pltpu.PrefetchScalarGridSpec(
        num_scalar_prefetch=1,
        grid=(groups, blocks),
        in_specs=[
            pl.BlockSpec((None, group_rows, HD), lambda g, kb, n: (g, 0, 0)),
            pl.BlockSpec((None, tok_rows, HD), lambda g, kb, n: (kb, 0, g)),
            pl.BlockSpec((None, tok_rows, HD), lambda g, kb, n: (kb, 0, groups + g)),
            pl.BlockSpec((group_rows, 1), lambda g, kb, n: (0, 0)),
            pl.BlockSpec((group_rows, 1), lambda g, kb, n: (0, 0)),
            pl.BlockSpec((None, 1, tok_rows), lambda g, kb, n: (kb, 0, 0)),
            pl.BlockSpec((None, 1, tok_rows), lambda g, kb, n: (kb, 0, 0)),
        ],
        out_specs=pl.BlockSpec((None, group_rows, HD), lambda g, kb, n: (g, 0, 0)),
        scratch_shapes=[
            pltpu.VMEM((group_rows, 1), jnp.float32),
            pltpu.VMEM((group_rows, 1), jnp.float32),
            pltpu.VMEM((group_rows, HD), jnp.float32),
        ],
    )
    flops = 4 * groups * blocks * group_rows * tok_rows * HD
    return pl.pallas_call(
        functools.partial(flash_kernel, root=root),
        grid_spec=grid_spec,
        out_shape=jax.ShapeDtypeStruct((groups, group_rows, HD), jnp.bfloat16),
        compiler_params=pltpu.CompilerParams(dimension_semantics=("arbitrary", "arbitrary")),
        cost_estimate=pl.CostEstimate(
            flops=flops,
            transcendentals=groups * blocks * group_rows * tok_rows,
            bytes_accessed=2 * groups * blocks * tok_rows * HD * 2 + 4 * groups * group_rows * HD,
        ),
    )(needed, grouped_q, gathered, gathered, q_ids, q_req, k_ids, k_req)


def gather_by_permutes(local, count):
    me = lax.axis_index("kv")
    pieces = [local]
    for shift in range(1, count):
        pieces.append(
            lax.ppermute(local, "kv", perm=[(i, (i + shift) % count) for i in range(count)])
        )
    stacked = jnp.stack(pieces)
    order = (me - jnp.arange(count, dtype=jnp.int32)) % count
    ordered = jnp.take(stacked, order, axis=0)
    return jnp.concatenate([ordered[j] for j in range(count)], axis=1)


def permute_pieces(local, count):
    pieces = [local]
    for shift in range(1, count):
        pieces.append(
            lax.ppermute(local, "kv", perm=[(i, (i + shift) % count) for i in range(count)])
        )
    return pieces


def ordered_sum(pieces, count):
    me = lax.axis_index("kv")
    stacked = jnp.stack([piece.astype(jnp.float32) for piece in pieces])
    order = (me - jnp.arange(count, dtype=jnp.int32)) % count
    return jnp.sum(jnp.take(stacked, order, axis=0), axis=0)


def tree_max(values, axis, count):
    if count & (count - 1):
        return lax.pmax(values, axis)
    step = 1
    while step < count:
        other = lax.ppermute(values, axis, perm=[(i, i ^ step) for i in range(count)])
        values = jnp.maximum(values, other)
        step *= 2
    return values


def on_device(
    patches,
    merged_grid,
    picture_start,
    vis_gain,
    vis_qkv,
    vis_out,
    merge_weight,
    text_embed,
    dec_gain,
    w_query,
    w_keyval,
    w_out,
    req_lengths,
    final_gain,
    table,
):
    pictures, patch_max, vis_width = patches.shape
    merged_max = patch_max // 4
    vis_cols = vis_qkv.shape[2]
    vis_heads = vis_cols // VHD
    tok_rows, feat_dev = text_embed.shape
    kv_count = D // text_embed.shape[1]
    text_rows = gather_by_permutes(text_embed, kv_count)
    inputs = patches.astype(jnp.float32)
    normed = layer_norm(inputs, vis_gain).astype(jnp.bfloat16)
    packed = jnp.einsum(
        "pnd,dce->pnce", normed, vis_qkv, preferred_element_type=jnp.float32
    ).astype(jnp.bfloat16)
    packed = packed.reshape(pictures, patch_max, 3, vis_heads, VHD)
    scores = jnp.einsum(
        "pqhd,pkhd->phqk", packed[:, :, 0], packed[:, :, 1], preferred_element_type=jnp.float32
    ) / math.sqrt(VHD)
    cell_count = merged_grid[:, 0] * merged_grid[:, 1]
    valid_cols = jnp.arange(patch_max, dtype=jnp.int32)[None, :] < 4 * cell_count[:, None]
    scores = jnp.where(valid_cols[:, None, None, :], scores, -1e30)
    weights = jnp.exp(scores - jnp.max(scores, axis=-1, keepdims=True))
    weight_sum = jnp.sum(weights, axis=-1)
    mixed_rows = jnp.einsum(
        "phqk,pkhd->pqhd",
        weights.astype(jnp.bfloat16),
        packed[:, :, 2],
        preferred_element_type=jnp.float32,
    )
    mixed_rows = (
        (mixed_rows / jnp.transpose(weight_sum, (0, 2, 1))[..., None])
        .astype(jnp.bfloat16)
        .reshape(pictures, patch_max, vis_cols)
    )
    head_part = jnp.einsum("pnc,cd->pnd", mixed_rows, vis_out, preferred_element_type=jnp.float32)
    head_pooled = jnp.mean(head_part.reshape(pictures, merged_max, 4, vis_width), axis=2)
    head_total = lax.psum(head_pooled.astype(jnp.bfloat16), "kv").astype(jnp.float32)
    input_pooled = jnp.mean(inputs.reshape(pictures, merged_max, 4, vis_width), axis=2)
    pooled = (input_pooled + head_total).astype(jnp.bfloat16)
    merged = jnp.einsum(
        "pmd,de->pme", pooled, merge_weight, preferred_element_type=jnp.float32
    ).astype(jnp.bfloat16)
    me_kv = lax.axis_index("kv")
    out_source, merged = lax.optimization_barrier((w_out, merged))
    weight_pieces = [lax.dynamic_slice_in_dim(out_source, me_kv * feat_dev, feat_dev, 1)]
    for shift in range(1, kv_count):
        payload = lax.dynamic_slice_in_dim(
            out_source, ((me_kv + shift) % kv_count) * feat_dev, feat_dev, 1
        )
        weight_pieces.append(
            lax.ppermute(
                payload, "kv", perm=[(i, (i + shift) % kv_count) for i in range(kv_count)]
            )
        )
    block_base = lax.axis_index("blk") * tok_rows
    slot_index = jnp.arange(merged_max, dtype=jnp.int32)
    target = picture_start[:, None] + slot_index[None, :] - block_base
    target = jnp.where(slot_index[None, :] < cell_count[:, None], target, -1).reshape(-1)
    local_rows = jnp.arange(tok_rows, dtype=jnp.int32)
    one_hot = local_rows[:, None] == target[None, :]
    placed = jnp.dot(
        one_hot.astype(jnp.bfloat16),
        merged.reshape(pictures * merged_max, feat_dev),
        preferred_element_type=jnp.float32,
    )
    is_vision = jnp.any(one_hot, axis=1)
    seq_in = jnp.where(is_vision[:, None], placed.astype(jnp.bfloat16), text_embed)
    merged_rows = lax.all_gather(
        merged.reshape(pictures * merged_max, feat_dev), "kv", axis=1, tiled=True
    )
    placed_rows = jnp.dot(one_hot.astype(jnp.bfloat16), merged_rows, preferred_element_type=jnp.float32)
    full_rows = jnp.where(is_vision[:, None], placed_rows.astype(jnp.bfloat16), text_rows)
    full_float = full_rows.astype(jnp.float32)
    dec_normed = (
        full_float
        * lax.rsqrt(jnp.mean(full_float * full_float, axis=-1, keepdims=True) + 1e-05)
        * dec_gain
    ).astype(jnp.bfloat16)
    per_group = QHEADS // KVHEADS
    kv_heads = w_keyval.shape[2] // HD
    row_ids = block_base + local_rows
    request_id, request_begin = request_info(row_ids, req_lengths)
    position = row_ids - request_begin
    query_proj = jnp.dot(dec_normed, w_query, preferred_element_type=jnp.float32).reshape(
        tok_rows, kv_heads * per_group, HD
    )
    query_proj = (
        rotate(query_proj, position)
        .astype(jnp.bfloat16)
        .reshape(tok_rows, kv_heads * per_group * HD)
    )
    key_value = jnp.einsum("td,dce->tce", dec_normed, w_keyval, preferred_element_type=jnp.float32)
    key_rows = (
        rotate(key_value[:, 0].reshape(tok_rows, kv_heads, HD), position)
        .astype(jnp.bfloat16)
        .reshape(tok_rows, kv_heads * HD)
    )
    value_rows = key_value[:, 1].astype(jnp.bfloat16)
    query_req, query_begin = request_info(row_ids, req_lengths)
    root = math.sqrt(HD)
    reqs = req_lengths.shape[0]
    ends_at = jnp.cumsum(req_lengths)
    last_ids = ends_at - 1
    picker = (local_rows[None, :] == (last_ids - block_base)[:, None]).astype(jnp.bfloat16)
    query_last = jnp.dot(picker, query_proj, preferred_element_type=jnp.float32)
    seq_last = jnp.dot(picker, seq_in, preferred_element_type=jnp.float32)
    extras = jnp.concatenate([query_last, seq_last], axis=1).astype(jnp.bfloat16).reshape(-1)
    kv_width = key_rows.shape[1]
    ship_width = 2 * kv_width
    extra_rows = -(-extras.shape[0] // ship_width)
    extras = jnp.pad(extras, (0, extra_rows * ship_width - extras.shape[0]))
    shipped = jnp.concatenate([key_rows, value_rows], axis=1)
    shipped = jnp.concatenate([shipped, extras.reshape(extra_rows, ship_width)], axis=0)
    gathered = lax.all_gather(shipped, "blk", axis=0, tiled=False)
    gathered, weight_pieces = lax.optimization_barrier((gathered, weight_pieces))
    out_weights = jnp.take(
        jnp.stack(weight_pieces),
        (me_kv - jnp.arange(kv_count, dtype=jnp.int32)) % kv_count,
        axis=0,
    )
    blocks = gathered.shape[0]
    q_cols = query_proj.shape[1]
    extras_all = gathered[:, tok_rows:].reshape(blocks, -1)[:, : reqs * (q_cols + feat_dev)]
    extras_all = jnp.sum(extras_all.astype(jnp.float32).reshape(blocks, reqs, -1), axis=0)
    query_last = extras_all[:, :q_cols].astype(jnp.bfloat16)
    seq_last = extras_all[:, q_cols:]
    block_index = lax.axis_index("blk")
    first_begin = query_begin[0]
    block_ids = jnp.arange(blocks, dtype=jnp.int32)
    needed = (
        (block_ids <= block_index) & (block_ids * tok_rows + tok_rows - 1 >= first_begin)
    ).astype(jnp.int32)
    group_rows = tok_rows * per_group
    grouped_q = jnp.transpose(
        query_proj.reshape(tok_rows, kv_heads, per_group, HD), (1, 0, 2, 3)
    ).reshape(kv_heads, group_rows, HD)
    q_ids = jnp.repeat(row_ids, per_group)[:, None]
    q_req = jnp.repeat(query_req, per_group)[:, None]
    all_ids = jnp.arange(blocks * tok_rows, dtype=jnp.int32)
    all_req, unused = request_info(all_ids, req_lengths)
    k_ids = all_ids.reshape(blocks, 1, tok_rows)
    k_req = all_req.reshape(blocks, 1, tok_rows)
    context = flash_attention(
        needed, grouped_q, gathered, q_ids, q_req, k_ids, k_req, kv_heads, tok_rows, root
    )
    context = jnp.transpose(
        context.reshape(kv_heads, tok_rows, per_group, HD), (1, 0, 2, 3)
    ).reshape(tok_rows, kv_heads * per_group * HD)
    all_ids = jnp.arange(blocks * tok_rows, dtype=jnp.int32)
    last_begin = ends_at - req_lengths
    last_allowed = (all_ids[None, :] >= last_begin[:, None]) & (all_ids[None, :] <= last_ids[:, None])
    last_allowed = last_allowed[:, None, :]
    last_parts = []
    for g in range(kv_heads):
        keys_g = gathered[:, :tok_rows, g * HD : (g + 1) * HD].reshape(blocks * tok_rows, HD)
        values_g = gathered[:, :tok_rows, kv_width + g * HD : kv_width + (g + 1) * HD].reshape(
            blocks * tok_rows, HD
        )
        last_q = query_last[:, g * per_group * HD : (g + 1) * per_group * HD].reshape(
            reqs, per_group, HD
        )
        last_scores = (
            jnp.einsum("tqd,kd->tqk", last_q, keys_g, preferred_element_type=jnp.float32) / root
        )
        last_scores = jnp.where(last_allowed, last_scores, -1e30)
        last_max = jnp.max(last_scores, axis=-1)
        last_weights = jnp.where(last_allowed, jnp.exp(last_scores - last_max[..., None]), 0.0)
        last_sum = jnp.sum(last_weights, axis=-1)
        last_mix = jnp.einsum(
            "tqk,kd->tqd",
            last_weights.astype(jnp.bfloat16),
            values_g,
            preferred_element_type=jnp.float32,
        )
        last_parts.append((last_mix / last_sum[..., None]).reshape(reqs, per_group * HD))
    last_context = jnp.concatenate(last_parts, axis=1).astype(jnp.bfloat16)
    out_rows = jnp.concatenate([context, last_context], axis=0)
    context_all = lax.all_gather(out_rows, "kv", axis=0, tiled=False)
    group_parts = jnp.einsum(
        "grc,gcf->grf", context_all, out_weights, preferred_element_type=jnp.float32
    )
    head_sum = jnp.sum(group_parts.astype(jnp.bfloat16).astype(jnp.float32), axis=0)
    hidden = (seq_in.astype(jnp.float32) + head_sum[:tok_rows]).astype(jnp.bfloat16)
    chosen = (seq_last + head_sum[tok_rows:]).astype(jnp.bfloat16).astype(jnp.float32)
    square_part = jnp.sum(chosen * chosen, axis=-1)
    scaled = (chosen * final_gain).astype(jnp.bfloat16)
    logit_part = lax.dot_general(
        scaled, table, (((1,), (1,)), ((), ())), preferred_element_type=jnp.float32
    )
    packed_sums = ordered_sum(
        permute_pieces(jnp.concatenate([logit_part, square_part[:, None]], axis=1), kv_count),
        kv_count,
    )
    logit_sum = packed_sums[:, :-1]
    square_sum = packed_sums[:, -1]
    inv_rms = lax.rsqrt(square_sum / D + 1e-05)
    last_norm = (chosen * inv_rms[:, None] * final_gain).astype(jnp.bfloat16)
    local_max = jnp.max(inv_rms[:, None] * logit_sum, axis=-1)
    max_logit = tree_max(local_max, "blk", blocks)
    return (hidden, last_norm, max_logit)


def solution(mesh):
    placed = (
        P("blk", None, None),
        P("blk", None),
        P("blk"),
        P(),
        P(None, None, "kv"),
        P("kv", None),
        P(None, "kv"),
        P("blk", "kv"),
        P(),
        P(None, "kv"),
        P(None, None, "kv"),
        P("kv", None),
        P(),
        P("kv"),
        P("blk", "kv"),
    )
    return jax.shard_map(
        on_device,
        mesh=mesh,
        in_specs=placed,
        out_specs=(P("blk", "kv"), P(None, "kv"), P()),
        check_vma=False,
    )
```

```python
import functools
import math

import jax
import jax.numpy as jnp
from jax import lax
from jax.experimental import pallas as pl
from jax.experimental.pallas import tpu as pltpu
from jax.sharding import PartitionSpec as P

VHD = 88
D = 4096
QHEADS = 16
KVHEADS = 8
HD = 128


def layer_norm(inputs, gain):
    centre = jnp.mean(inputs, axis=-1, keepdims=True)
    centred = inputs - centre
    spread = jnp.mean(centred * centred, axis=-1, keepdims=True)
    return centred * lax.rsqrt(spread + 1e-06) * gain


def rotate(inputs, position):
    half_width = inputs.shape[-1] // 2
    inverse = 500000.0 ** (-jnp.arange(half_width, dtype=jnp.float32) * 2.0 / inputs.shape[-1])
    angles = position.astype(jnp.float32)[:, None] * inverse[None, :]
    cosine = jnp.cos(angles)[:, None, :]
    sine = jnp.sin(angles)[:, None, :]
    first = inputs[..., :half_width]
    second = inputs[..., half_width:]
    return jnp.concatenate(
        [first * cosine - second * sine, second * cosine + first * sine], axis=-1
    )


def request_info(row_index, req_lengths):
    ends_at = jnp.cumsum(req_lengths)
    starts_at = ends_at - req_lengths
    request_id = jnp.sum((row_index[:, None] >= ends_at[None, :]).astype(jnp.int32), axis=1)
    choose = request_id[:, None] == jnp.arange(req_lengths.shape[0], dtype=jnp.int32)[None, :]
    request_begin = jnp.sum(jnp.where(choose, starts_at[None, :], 0), axis=1)
    return (request_id, request_begin)


def flash_kernel(needed_ref, q_ref, k_ref, v_ref, qid_ref, qreq_ref, kid_ref, kreq_ref, o_ref,
                 max_ref, sum_ref, acc_ref, *, root):
    kb = pl.program_id(1)

    @pl.when(kb == 0)
    def _():
        max_ref[...] = jnp.full(max_ref.shape, -1e30, jnp.float32)
        sum_ref[...] = jnp.zeros(sum_ref.shape, jnp.float32)
        acc_ref[...] = jnp.zeros(acc_ref.shape, jnp.float32)

    @pl.when(needed_ref[kb] != 0)
    def _():
        scores = lax.dot_general(
            q_ref[...], k_ref[...], (((1,), (1,)), ((), ())), preferred_element_type=jnp.float32
        ) / root
        allowed = (kid_ref[...] <= qid_ref[...]) & (kreq_ref[...] == qreq_ref[...])
        scores = jnp.where(allowed, scores, -1e30)
        old_max = max_ref[...]
        new_max = jnp.maximum(old_max, jnp.max(scores, axis=1, keepdims=True))
        weights = jnp.where(allowed, jnp.exp(scores - new_max), 0.0)
        scale = jnp.exp(old_max - new_max)
        sum_ref[...] = sum_ref[...] * scale + jnp.sum(weights, axis=1, keepdims=True)
        acc_ref[...] = acc_ref[...] * scale + jnp.dot(
            weights.astype(jnp.bfloat16), v_ref[...], preferred_element_type=jnp.float32
        )
        max_ref[...] = new_max

    @pl.when(kb == pl.num_programs(1) - 1)
    def _():
        o_ref[...] = (acc_ref[...] / sum_ref[...]).astype(o_ref.dtype)


def flash_attention(needed, grouped_q, gathered, q_ids, q_req, k_ids, k_req, groups, tok_rows, root):
    blocks = gathered.shape[0]
    group_rows = grouped_q.shape[1]
    grid_spec = pltpu.PrefetchScalarGridSpec(
        num_scalar_prefetch=1,
        grid=(groups, blocks),
        in_specs=[
            pl.BlockSpec((None, group_rows, HD), lambda g, kb, n: (g, 0, 0)),
            pl.BlockSpec((None, tok_rows, HD), lambda g, kb, n: (kb, 0, g)),
            pl.BlockSpec((None, tok_rows, HD), lambda g, kb, n: (kb, 0, groups + g)),
            pl.BlockSpec((group_rows, 1), lambda g, kb, n: (0, 0)),
            pl.BlockSpec((group_rows, 1), lambda g, kb, n: (0, 0)),
            pl.BlockSpec((None, 1, tok_rows), lambda g, kb, n: (kb, 0, 0)),
            pl.BlockSpec((None, 1, tok_rows), lambda g, kb, n: (kb, 0, 0)),
        ],
        out_specs=pl.BlockSpec((None, group_rows, HD), lambda g, kb, n: (g, 0, 0)),
        scratch_shapes=[
            pltpu.VMEM((group_rows, 1), jnp.float32),
            pltpu.VMEM((group_rows, 1), jnp.float32),
            pltpu.VMEM((group_rows, HD), jnp.float32),
        ],
    )
    flops = 4 * groups * blocks * group_rows * tok_rows * HD
    return pl.pallas_call(
        functools.partial(flash_kernel, root=root),
        grid_spec=grid_spec,
        out_shape=jax.ShapeDtypeStruct((groups, group_rows, HD), jnp.bfloat16),
        compiler_params=pltpu.CompilerParams(dimension_semantics=("arbitrary", "arbitrary")),
        cost_estimate=pl.CostEstimate(
            flops=flops,
            transcendentals=groups * blocks * group_rows * tok_rows,
            bytes_accessed=2 * groups * blocks * tok_rows * HD * 2 + 4 * groups * group_rows * HD,
        ),
    )(needed, grouped_q, gathered, gathered, q_ids, q_req, k_ids, k_req)


def gather_by_permutes(local, count):
    me = lax.axis_index("kv")
    pieces = [local]
    for shift in range(1, count):
        pieces.append(
            lax.ppermute(local, "kv", perm=[(i, (i + shift) % count) for i in range(count)])
        )
    stacked = jnp.stack(pieces)
    order = (me - jnp.arange(count, dtype=jnp.int32)) % count
    ordered = jnp.take(stacked, order, axis=0)
    return jnp.concatenate([ordered[j] for j in range(count)], axis=1)


def permute_pieces(local, count):
    pieces = [local]
    for shift in range(1, count):
        pieces.append(
            lax.ppermute(local, "kv", perm=[(i, (i + shift) % count) for i in range(count)])
        )
    return pieces


def ordered_sum(pieces, count):
    me = lax.axis_index("kv")
    stacked = jnp.stack([piece.astype(jnp.float32) for piece in pieces])
    order = (me - jnp.arange(count, dtype=jnp.int32)) % count
    return jnp.sum(jnp.take(stacked, order, axis=0), axis=0)


def tree_max(values, axis, count):
    if count & (count - 1):
        return lax.pmax(values, axis)
    step = 1
    while step < count:
        other = lax.ppermute(values, axis, perm=[(i, i ^ step) for i in range(count)])
        values = jnp.maximum(values, other)
        step *= 2
    return values


def on_device(
    patches,
    merged_grid,
    picture_start,
    vis_gain,
    vis_qkv,
    vis_out,
    merge_weight,
    text_embed,
    dec_gain,
    w_query,
    w_keyval,
    w_out,
    req_lengths,
    final_gain,
    table,
):
    pictures, patch_max, vis_width = patches.shape
    merged_max = patch_max // 4
    vis_cols = vis_qkv.shape[2]
    vis_heads = vis_cols // VHD
    tok_rows, feat_dev = text_embed.shape
    kv_count = D // text_embed.shape[1]
    text_rows = gather_by_permutes(text_embed, kv_count)
    inputs = patches.astype(jnp.float32)
    normed = layer_norm(inputs, vis_gain).astype(jnp.bfloat16)
    packed = jnp.einsum(
        "pnd,dce->pnce", normed, vis_qkv, preferred_element_type=jnp.float32
    ).astype(jnp.bfloat16)
    packed = packed.reshape(pictures, patch_max, 3, vis_heads, VHD)
    scores = jnp.einsum(
        "pqhd,pkhd->phqk", packed[:, :, 0], packed[:, :, 1], preferred_element_type=jnp.float32
    ) / math.sqrt(VHD)
    cell_count = merged_grid[:, 0] * merged_grid[:, 1]
    valid_cols = jnp.arange(patch_max, dtype=jnp.int32)[None, :] < 4 * cell_count[:, None]
    scores = jnp.where(valid_cols[:, None, None, :], scores, -1e30)
    weights = jnp.exp(scores - jnp.max(scores, axis=-1, keepdims=True))
    weight_sum = jnp.sum(weights, axis=-1)
    mixed_rows = jnp.einsum(
        "phqk,pkhd->pqhd",
        weights.astype(jnp.bfloat16),
        packed[:, :, 2],
        preferred_element_type=jnp.float32,
    )
    mixed_rows = (
        (mixed_rows / jnp.transpose(weight_sum, (0, 2, 1))[..., None])
        .astype(jnp.bfloat16)
        .reshape(pictures, patch_max, vis_cols)
    )
    head_part = jnp.einsum("pnc,cd->pnd", mixed_rows, vis_out, preferred_element_type=jnp.float32)
    head_pooled = jnp.mean(head_part.reshape(pictures, merged_max, 4, vis_width), axis=2)
    head_total = lax.psum(head_pooled.astype(jnp.bfloat16), "kv").astype(jnp.float32)
    input_pooled = jnp.mean(inputs.reshape(pictures, merged_max, 4, vis_width), axis=2)
    pooled = (input_pooled + head_total).astype(jnp.bfloat16)
    merged = jnp.einsum(
        "pmd,de->pme", pooled, merge_weight, preferred_element_type=jnp.float32
    ).astype(jnp.bfloat16)
    me_kv = lax.axis_index("kv")
    out_source, merged = lax.optimization_barrier((w_out, merged))
    weight_pieces = [lax.dynamic_slice_in_dim(out_source, me_kv * feat_dev, feat_dev, 1)]
    for shift in range(1, kv_count):
        payload = lax.dynamic_slice_in_dim(
            out_source, ((me_kv + shift) % kv_count) * feat_dev, feat_dev, 1
        )
        weight_pieces.append(
            lax.ppermute(
                payload, "kv", perm=[(i, (i + shift) % kv_count) for i in range(kv_count)]
            )
        )
    block_base = lax.axis_index("blk") * tok_rows
    slot_index = jnp.arange(merged_max, dtype=jnp.int32)
    target = picture_start[:, None] + slot_index[None, :] - block_base
    target = jnp.where(slot_index[None, :] < cell_count[:, None], target, -1).reshape(-1)
    local_rows = jnp.arange(tok_rows, dtype=jnp.int32)
    one_hot = local_rows[:, None] == target[None, :]
    placed = jnp.dot(
        one_hot.astype(jnp.bfloat16),
        merged.reshape(pictures * merged_max, feat_dev),
        preferred_element_type=jnp.float32,
    )
    is_vision = jnp.any(one_hot, axis=1)
    seq_in = jnp.where(is_vision[:, None], placed.astype(jnp.bfloat16), text_embed)
    merged_rows = lax.all_gather(
        merged.reshape(pictures * merged_max, feat_dev), "kv", axis=1, tiled=True
    )
    placed_rows = jnp.dot(one_hot.astype(jnp.bfloat16), merged_rows, preferred_element_type=jnp.float32)
    full_rows = jnp.where(is_vision[:, None], placed_rows.astype(jnp.bfloat16), text_rows)
    full_float = full_rows.astype(jnp.float32)
    dec_normed = (
        full_float
        * lax.rsqrt(jnp.mean(full_float * full_float, axis=-1, keepdims=True) + 1e-05)
        * dec_gain
    ).astype(jnp.bfloat16)
    per_group = QHEADS // KVHEADS
    kv_heads = w_keyval.shape[2] // HD
    row_ids = block_base + local_rows
    request_id, request_begin = request_info(row_ids, req_lengths)
    position = row_ids - request_begin
    query_proj = jnp.dot(dec_normed, w_query, preferred_element_type=jnp.float32).reshape(
        tok_rows, kv_heads * per_group, HD
    )
    query_proj = (
        rotate(query_proj, position)
        .astype(jnp.bfloat16)
        .reshape(tok_rows, kv_heads * per_group * HD)
    )
    key_value = jnp.einsum("td,dce->tce", dec_normed, w_keyval, preferred_element_type=jnp.float32)
    key_rows = (
        rotate(key_value[:, 0].reshape(tok_rows, kv_heads, HD), position)
        .astype(jnp.bfloat16)
        .reshape(tok_rows, kv_heads * HD)
    )
    value_rows = key_value[:, 1].astype(jnp.bfloat16)
    query_req, query_begin = request_info(row_ids, req_lengths)
    root = math.sqrt(HD)
    reqs = req_lengths.shape[0]
    ends_at = jnp.cumsum(req_lengths)
    last_ids = ends_at - 1
    picker = (local_rows[None, :] == (last_ids - block_base)[:, None]).astype(jnp.bfloat16)
    query_last = jnp.dot(picker, query_proj, preferred_element_type=jnp.float32)
    seq_last = jnp.dot(picker, seq_in, preferred_element_type=jnp.float32)
    extras = jnp.concatenate([query_last, seq_last], axis=1).astype(jnp.bfloat16).reshape(-1)
    kv_width = key_rows.shape[1]
    ship_width = 2 * kv_width
    extra_rows = -(-extras.shape[0] // ship_width)
    extras = jnp.pad(extras, (0, extra_rows * ship_width - extras.shape[0]))
    shipped = jnp.concatenate([key_rows, value_rows], axis=1)
    shipped = jnp.concatenate([shipped, extras.reshape(extra_rows, ship_width)], axis=0)
    gathered = lax.all_gather(shipped, "blk", axis=0, tiled=False)
    gathered, weight_pieces = lax.optimization_barrier((gathered, weight_pieces))
    blocks = gathered.shape[0]
    q_cols = query_proj.shape[1]
    extras_all = gathered[:, tok_rows:].reshape(blocks, -1)[:, : reqs * (q_cols + feat_dev)]
    extras_all = jnp.sum(extras_all.astype(jnp.float32).reshape(blocks, reqs, -1), axis=0)
    query_last = extras_all[:, :q_cols].astype(jnp.bfloat16)
    seq_last = extras_all[:, q_cols:]
    block_index = lax.axis_index("blk")
    first_begin = query_begin[0]
    block_ids = jnp.arange(blocks, dtype=jnp.int32)
    needed = (
        (block_ids <= block_index) & (block_ids * tok_rows + tok_rows - 1 >= first_begin)
    ).astype(jnp.int32)
    group_rows = tok_rows * per_group
    grouped_q = jnp.transpose(
        query_proj.reshape(tok_rows, kv_heads, per_group, HD), (1, 0, 2, 3)
    ).reshape(kv_heads, group_rows, HD)
    q_ids = jnp.repeat(row_ids, per_group)[:, None]
    q_req = jnp.repeat(query_req, per_group)[:, None]
    all_ids = jnp.arange(blocks * tok_rows, dtype=jnp.int32)
    all_req, unused = request_info(all_ids, req_lengths)
    k_ids = all_ids.reshape(blocks, 1, tok_rows)
    k_req = all_req.reshape(blocks, 1, tok_rows)
    context = flash_attention(
        needed, grouped_q, gathered, q_ids, q_req, k_ids, k_req, kv_heads, tok_rows, root
    )
    context = jnp.transpose(
        context.reshape(kv_heads, tok_rows, per_group, HD), (1, 0, 2, 3)
    ).reshape(tok_rows, kv_heads * per_group * HD)
    all_ids = jnp.arange(blocks * tok_rows, dtype=jnp.int32)
    last_begin = ends_at - req_lengths
    last_allowed = (all_ids[None, :] >= last_begin[:, None]) & (all_ids[None, :] <= last_ids[:, None])
    last_allowed = last_allowed[:, None, :]
    last_parts = []
    for g in range(kv_heads):
        keys_g = gathered[:, :tok_rows, g * HD : (g + 1) * HD].reshape(blocks * tok_rows, HD)
        values_g = gathered[:, :tok_rows, kv_width + g * HD : kv_width + (g + 1) * HD].reshape(
            blocks * tok_rows, HD
        )
        last_q = query_last[:, g * per_group * HD : (g + 1) * per_group * HD].reshape(
            reqs, per_group, HD
        )
        last_scores = (
            jnp.einsum("tqd,kd->tqk", last_q, keys_g, preferred_element_type=jnp.float32) / root
        )
        last_scores = jnp.where(last_allowed, last_scores, -1e30)
        last_max = jnp.max(last_scores, axis=-1)
        last_weights = jnp.where(last_allowed, jnp.exp(last_scores - last_max[..., None]), 0.0)
        last_sum = jnp.sum(last_weights, axis=-1)
        last_mix = jnp.einsum(
            "tqk,kd->tqd",
            last_weights.astype(jnp.bfloat16),
            values_g,
            preferred_element_type=jnp.float32,
        )
        last_parts.append((last_mix / last_sum[..., None]).reshape(reqs, per_group * HD))
    last_context = jnp.concatenate(last_parts, axis=1).astype(jnp.bfloat16)
    out_rows = jnp.concatenate([context, last_context], axis=0)
    context_all = lax.all_gather(out_rows, "kv", axis=0, tiled=False)
    head_sum = None
    for shift, piece in enumerate(weight_pieces):
        source = lax.dynamic_index_in_dim(
            context_all, (me_kv - shift) % kv_count, 0, keepdims=False
        )
        part = jnp.dot(source, piece, preferred_element_type=jnp.float32)
        part = part.astype(jnp.bfloat16).astype(jnp.float32)
        head_sum = part if head_sum is None else head_sum + part
    hidden = (seq_in.astype(jnp.float32) + head_sum[:tok_rows]).astype(jnp.bfloat16)
    chosen = (seq_last + head_sum[tok_rows:]).astype(jnp.bfloat16).astype(jnp.float32)
    square_part = jnp.sum(chosen * chosen, axis=-1)
    scaled = (chosen * final_gain).astype(jnp.bfloat16)
    logit_part = lax.dot_general(
        scaled, table, (((1,), (1,)), ((), ())), preferred_element_type=jnp.float32
    )
    packed_sums = ordered_sum(
        permute_pieces(jnp.concatenate([logit_part, square_part[:, None]], axis=1), kv_count),
        kv_count,
    )
    logit_sum = packed_sums[:, :-1]
    square_sum = packed_sums[:, -1]
    inv_rms = lax.rsqrt(square_sum / D + 1e-05)
    last_norm = (chosen * inv_rms[:, None] * final_gain).astype(jnp.bfloat16)
    local_max = jnp.max(inv_rms[:, None] * logit_sum, axis=-1)
    max_logit = tree_max(local_max, "blk", blocks)
    return (hidden, last_norm, max_logit)


def solution(mesh):
    placed = (
        P("blk", None, None),
        P("blk", None),
        P("blk"),
        P(),
        P(None, None, "kv"),
        P("kv", None),
        P(None, "kv"),
        P("blk", "kv"),
        P(),
        P(None, "kv"),
        P(None, None, "kv"),
        P("kv", None),
        P(),
        P("kv"),
        P("blk", "kv"),
    )
    return jax.shard_map(
        on_device,
        mesh=mesh,
        in_specs=placed,
        out_specs=(P("blk", "kv"), P(None, "kv"), P()),
        check_vma=False,
    )
```

```python
import functools
import math

import jax
import jax.numpy as jnp
from jax import lax
from jax.experimental import pallas as pl
from jax.experimental.pallas import tpu as pltpu
from jax.sharding import PartitionSpec as P

VHD = 88
D = 4096
QHEADS = 16
KVHEADS = 8
HD = 128


def layer_norm(inputs, gain):
    centre = jnp.mean(inputs, axis=-1, keepdims=True)
    centred = inputs - centre
    spread = jnp.mean(centred * centred, axis=-1, keepdims=True)
    return centred * lax.rsqrt(spread + 1e-06) * gain


def rotate(inputs, position):
    half_width = inputs.shape[-1] // 2
    inverse = 500000.0 ** (-jnp.arange(half_width, dtype=jnp.float32) * 2.0 / inputs.shape[-1])
    angles = position.astype(jnp.float32)[:, None] * inverse[None, :]
    cosine = jnp.cos(angles)[:, None, :]
    sine = jnp.sin(angles)[:, None, :]
    first = inputs[..., :half_width]
    second = inputs[..., half_width:]
    return jnp.concatenate(
        [first * cosine - second * sine, second * cosine + first * sine], axis=-1
    )


def request_info(row_index, req_lengths):
    ends_at = jnp.cumsum(req_lengths)
    starts_at = ends_at - req_lengths
    request_id = jnp.sum((row_index[:, None] >= ends_at[None, :]).astype(jnp.int32), axis=1)
    choose = request_id[:, None] == jnp.arange(req_lengths.shape[0], dtype=jnp.int32)[None, :]
    request_begin = jnp.sum(jnp.where(choose, starts_at[None, :], 0), axis=1)
    return (request_id, request_begin)


def flash_kernel(needed_ref, q_ref, k_ref, v_ref, qid_ref, qreq_ref, kid_ref, kreq_ref, o_ref,
                 max_ref, sum_ref, acc_ref, *, root):
    kb = pl.program_id(1)

    @pl.when(kb == 0)
    def _():
        max_ref[...] = jnp.full(max_ref.shape, -1e30, jnp.float32)
        sum_ref[...] = jnp.zeros(sum_ref.shape, jnp.float32)
        acc_ref[...] = jnp.zeros(acc_ref.shape, jnp.float32)

    def accumulate(masked):
        scores = lax.dot_general(
            q_ref[...], k_ref[...], (((1,), (1,)), ((), ())), preferred_element_type=jnp.float32
        ) / root
        if masked:
            allowed = (kid_ref[...] <= qid_ref[...]) & (kreq_ref[...] == qreq_ref[...])
            scores = jnp.where(allowed, scores, -1e30)
        old_max = max_ref[...]
        new_max = jnp.maximum(old_max, jnp.max(scores, axis=1, keepdims=True))
        weights = jnp.exp(scores - new_max)
        if masked:
            weights = jnp.where(allowed, weights, 0.0)
        scale = jnp.exp(old_max - new_max)
        sum_ref[...] = sum_ref[...] * scale + jnp.sum(weights, axis=1, keepdims=True)
        acc_ref[...] = acc_ref[...] * scale + jnp.dot(
            weights.astype(jnp.bfloat16), v_ref[...], preferred_element_type=jnp.float32
        )
        max_ref[...] = new_max

    @pl.when(needed_ref[kb] == 1)
    def _():
        accumulate(True)

    @pl.when(needed_ref[kb] == 2)
    def _():
        accumulate(False)

    @pl.when(kb == pl.num_programs(1) - 1)
    def _():
        o_ref[...] = (acc_ref[...] / sum_ref[...]).astype(o_ref.dtype)


def flash_attention(needed, grouped_q, gathered, q_ids, q_req, k_ids, k_req, groups, tok_rows, root):
    blocks = gathered.shape[0]
    group_rows = grouped_q.shape[1]
    grid_spec = pltpu.PrefetchScalarGridSpec(
        num_scalar_prefetch=1,
        grid=(groups, blocks),
        in_specs=[
            pl.BlockSpec((None, group_rows, HD), lambda g, kb, n: (g, 0, 0)),
            pl.BlockSpec((None, tok_rows, HD), lambda g, kb, n: (kb, 0, g)),
            pl.BlockSpec((None, tok_rows, HD), lambda g, kb, n: (kb, 0, groups + g)),
            pl.BlockSpec((group_rows, 1), lambda g, kb, n: (0, 0)),
            pl.BlockSpec((group_rows, 1), lambda g, kb, n: (0, 0)),
            pl.BlockSpec((None, 1, tok_rows), lambda g, kb, n: (kb, 0, 0)),
            pl.BlockSpec((None, 1, tok_rows), lambda g, kb, n: (kb, 0, 0)),
        ],
        out_specs=pl.BlockSpec((None, group_rows, HD), lambda g, kb, n: (g, 0, 0)),
        scratch_shapes=[
            pltpu.VMEM((group_rows, 1), jnp.float32),
            pltpu.VMEM((group_rows, 1), jnp.float32),
            pltpu.VMEM((group_rows, HD), jnp.float32),
        ],
    )
    flops = 4 * groups * blocks * group_rows * tok_rows * HD
    return pl.pallas_call(
        functools.partial(flash_kernel, root=root),
        grid_spec=grid_spec,
        out_shape=jax.ShapeDtypeStruct((groups, group_rows, HD), jnp.bfloat16),
        compiler_params=pltpu.CompilerParams(dimension_semantics=("arbitrary", "arbitrary")),
        cost_estimate=pl.CostEstimate(
            flops=flops,
            transcendentals=groups * blocks * group_rows * tok_rows,
            bytes_accessed=2 * groups * blocks * tok_rows * HD * 2 + 4 * groups * group_rows * HD,
        ),
    )(needed, grouped_q, gathered, gathered, q_ids, q_req, k_ids, k_req)


def gather_by_permutes(local, count):
    me = lax.axis_index("kv")
    pieces = [local]
    for shift in range(1, count):
        pieces.append(
            lax.ppermute(local, "kv", perm=[(i, (i + shift) % count) for i in range(count)])
        )
    stacked = jnp.stack(pieces)
    order = (me - jnp.arange(count, dtype=jnp.int32)) % count
    ordered = jnp.take(stacked, order, axis=0)
    return jnp.concatenate([ordered[j] for j in range(count)], axis=1)


def permute_pieces(local, count):
    pieces = [local]
    for shift in range(1, count):
        pieces.append(
            lax.ppermute(local, "kv", perm=[(i, (i + shift) % count) for i in range(count)])
        )
    return pieces


def ordered_sum(pieces, count):
    me = lax.axis_index("kv")
    stacked = jnp.stack([piece.astype(jnp.float32) for piece in pieces])
    order = (me - jnp.arange(count, dtype=jnp.int32)) % count
    return jnp.sum(jnp.take(stacked, order, axis=0), axis=0)


def tree_max(values, axis, count):
    if count <= 8:
        result = values
        for shift in range(1, count):
            result = jnp.maximum(
                result,
                lax.ppermute(values, axis, perm=[(i, (i + shift) % count) for i in range(count)]),
            )
        return result
    if count & (count - 1):
        return lax.pmax(values, axis)
    step = 1
    while step < count:
        other = lax.ppermute(values, axis, perm=[(i, i ^ step) for i in range(count)])
        values = jnp.maximum(values, other)
        step *= 2
    return values


def on_device(
    patches,
    merged_grid,
    picture_start,
    vis_gain,
    vis_qkv,
    vis_out,
    merge_weight,
    text_embed,
    dec_gain,
    w_query,
    w_keyval,
    w_out,
    req_lengths,
    final_gain,
    table,
):
    pictures, patch_max, vis_width = patches.shape
    merged_max = patch_max // 4
    vis_cols = vis_qkv.shape[2]
    vis_heads = vis_cols // VHD
    tok_rows, feat_dev = text_embed.shape
    kv_count = D // text_embed.shape[1]
    text_rows = gather_by_permutes(text_embed, kv_count)
    inputs = patches.astype(jnp.float32)
    normed = layer_norm(inputs, vis_gain).astype(jnp.bfloat16)
    packed = jnp.einsum(
        "pnd,dce->pnce", normed, vis_qkv, preferred_element_type=jnp.float32
    ).astype(jnp.bfloat16)
    packed = packed.reshape(pictures, patch_max, 3, vis_heads, VHD)
    scores = jnp.einsum(
        "pqhd,pkhd->phqk", packed[:, :, 0], packed[:, :, 1], preferred_element_type=jnp.float32
    ) / math.sqrt(VHD)
    cell_count = merged_grid[:, 0] * merged_grid[:, 1]
    valid_cols = jnp.arange(patch_max, dtype=jnp.int32)[None, :] < 4 * cell_count[:, None]
    scores = jnp.where(valid_cols[:, None, None, :], scores, -1e30)
    weights = jnp.exp(scores - jnp.max(scores, axis=-1, keepdims=True))
    weight_sum = jnp.sum(weights, axis=-1)
    mixed_rows = jnp.einsum(
        "phqk,pkhd->pqhd",
        weights.astype(jnp.bfloat16),
        packed[:, :, 2],
        preferred_element_type=jnp.float32,
    )
    mixed_rows = (
        (mixed_rows / jnp.transpose(weight_sum, (0, 2, 1))[..., None])
        .astype(jnp.bfloat16)
        .reshape(pictures, patch_max, vis_cols)
    )
    head_part = jnp.einsum("pnc,cd->pnd", mixed_rows, vis_out, preferred_element_type=jnp.float32)
    head_pooled = jnp.mean(head_part.reshape(pictures, merged_max, 4, vis_width), axis=2)
    head_total = lax.psum(head_pooled.astype(jnp.bfloat16), "kv").astype(jnp.float32)
    input_pooled = jnp.mean(inputs.reshape(pictures, merged_max, 4, vis_width), axis=2)
    pooled = (input_pooled + head_total).astype(jnp.bfloat16)
    merged = jnp.einsum(
        "pmd,de->pme", pooled, merge_weight, preferred_element_type=jnp.float32
    ).astype(jnp.bfloat16)
    me_kv = lax.axis_index("kv")
    out_source, merged = lax.optimization_barrier((w_out, merged))
    weight_pieces = [lax.dynamic_slice_in_dim(out_source, me_kv * feat_dev, feat_dev, 1)]
    for shift in range(1, kv_count):
        payload = lax.dynamic_slice_in_dim(
            out_source, ((me_kv + shift) % kv_count) * feat_dev, feat_dev, 1
        )
        weight_pieces.append(
            lax.ppermute(
                payload, "kv", perm=[(i, (i + shift) % kv_count) for i in range(kv_count)]
            )
        )
    block_base = lax.axis_index("blk") * tok_rows
    slot_index = jnp.arange(merged_max, dtype=jnp.int32)
    target = picture_start[:, None] + slot_index[None, :] - block_base
    target = jnp.where(slot_index[None, :] < cell_count[:, None], target, -1).reshape(-1)
    local_rows = jnp.arange(tok_rows, dtype=jnp.int32)
    one_hot = local_rows[:, None] == target[None, :]
    placed = jnp.dot(
        one_hot.astype(jnp.bfloat16),
        merged.reshape(pictures * merged_max, feat_dev),
        preferred_element_type=jnp.float32,
    )
    is_vision = jnp.any(one_hot, axis=1)
    seq_in = jnp.where(is_vision[:, None], placed.astype(jnp.bfloat16), text_embed)
    merged_rows = lax.all_gather(
        merged.reshape(pictures * merged_max, feat_dev), "kv", axis=1, tiled=True
    )
    placed_rows = jnp.dot(one_hot.astype(jnp.bfloat16), merged_rows, preferred_element_type=jnp.float32)
    full_rows = jnp.where(is_vision[:, None], placed_rows.astype(jnp.bfloat16), text_rows)
    full_float = full_rows.astype(jnp.float32)
    dec_normed = (
        full_float
        * lax.rsqrt(jnp.mean(full_float * full_float, axis=-1, keepdims=True) + 1e-05)
        * dec_gain
    ).astype(jnp.bfloat16)
    per_group = QHEADS // KVHEADS
    kv_heads = w_keyval.shape[2] // HD
    row_ids = block_base + local_rows
    request_id, request_begin = request_info(row_ids, req_lengths)
    position = row_ids - request_begin
    query_proj = jnp.dot(dec_normed, w_query, preferred_element_type=jnp.float32).reshape(
        tok_rows, kv_heads * per_group, HD
    )
    query_proj = (
        rotate(query_proj, position)
        .astype(jnp.bfloat16)
        .reshape(tok_rows, kv_heads * per_group * HD)
    )
    key_value = jnp.einsum("td,dce->tce", dec_normed, w_keyval, preferred_element_type=jnp.float32)
    key_rows = (
        rotate(key_value[:, 0].reshape(tok_rows, kv_heads, HD), position)
        .astype(jnp.bfloat16)
        .reshape(tok_rows, kv_heads * HD)
    )
    value_rows = key_value[:, 1].astype(jnp.bfloat16)
    query_req, query_begin = request_info(row_ids, req_lengths)
    root = math.sqrt(HD)
    reqs = req_lengths.shape[0]
    ends_at = jnp.cumsum(req_lengths)
    last_ids = ends_at - 1
    picker = (local_rows[None, :] == (last_ids - block_base)[:, None]).astype(jnp.bfloat16)
    query_last = jnp.dot(picker, query_proj, preferred_element_type=jnp.float32)
    seq_last = jnp.dot(picker, seq_in, preferred_element_type=jnp.float32)
    extras = jnp.concatenate([query_last, seq_last], axis=1).astype(jnp.bfloat16).reshape(-1)
    kv_width = key_rows.shape[1]
    ship_width = 2 * kv_width
    extra_rows = -(-extras.shape[0] // ship_width)
    extras = jnp.pad(extras, (0, extra_rows * ship_width - extras.shape[0]))
    shipped = jnp.concatenate([key_rows, value_rows], axis=1)
    shipped = jnp.concatenate([shipped, extras.reshape(extra_rows, ship_width)], axis=0)
    gathered = lax.all_gather(shipped, "blk", axis=0, tiled=False)
    gathered, weight_pieces = lax.optimization_barrier((gathered, weight_pieces))
    blocks = gathered.shape[0]
    q_cols = query_proj.shape[1]
    extras_all = gathered[:, tok_rows:].reshape(blocks, -1)[:, : reqs * (q_cols + feat_dev)]
    extras_all = jnp.sum(extras_all.astype(jnp.float32).reshape(blocks, reqs, -1), axis=0)
    query_last = extras_all[:, :q_cols].astype(jnp.bfloat16)
    seq_last = extras_all[:, q_cols:]
    block_index = lax.axis_index("blk")
    first_begin = query_begin[0]
    block_ids = jnp.arange(blocks, dtype=jnp.int32)
    needed = (
        (block_ids <= block_index) & (block_ids * tok_rows + tok_rows - 1 >= first_begin)
    ).astype(jnp.int32)
    group_rows = tok_rows * per_group
    grouped_q = jnp.transpose(
        query_proj.reshape(tok_rows, kv_heads, per_group, HD), (1, 0, 2, 3)
    ).reshape(kv_heads, group_rows, HD)
    q_ids = jnp.repeat(row_ids, per_group)[:, None]
    q_req = jnp.repeat(query_req, per_group)[:, None]
    all_ids = jnp.arange(blocks * tok_rows, dtype=jnp.int32)
    all_req, unused = request_info(all_ids, req_lengths)
    block_first_req = all_req.reshape(blocks, tok_rows)[:, 0]
    full = (block_ids < block_index) & (block_first_req == query_req[tok_rows - 1])
    needed = jnp.where(full, 2, needed)
    k_ids = all_ids.reshape(blocks, 1, tok_rows)
    k_req = all_req.reshape(blocks, 1, tok_rows)
    context = flash_attention(
        needed, grouped_q, gathered, q_ids, q_req, k_ids, k_req, kv_heads, tok_rows, root
    )
    context = jnp.transpose(
        context.reshape(kv_heads, tok_rows, per_group, HD), (1, 0, 2, 3)
    ).reshape(tok_rows, kv_heads * per_group * HD)
    all_ids = jnp.arange(blocks * tok_rows, dtype=jnp.int32)
    last_begin = ends_at - req_lengths
    last_allowed = (all_ids[None, :] >= last_begin[:, None]) & (all_ids[None, :] <= last_ids[:, None])
    last_allowed = last_allowed[:, None, :]
    last_parts = []
    for g in range(kv_heads):
        keys_g = gathered[:, :tok_rows, g * HD : (g + 1) * HD].reshape(blocks * tok_rows, HD)
        values_g = gathered[:, :tok_rows, kv_width + g * HD : kv_width + (g + 1) * HD].reshape(
            blocks * tok_rows, HD
        )
        last_q = query_last[:, g * per_group * HD : (g + 1) * per_group * HD].reshape(
            reqs, per_group, HD
        )
        last_scores = (
            jnp.einsum("tqd,kd->tqk", last_q, keys_g, preferred_element_type=jnp.float32) / root
        )
        last_scores = jnp.where(last_allowed, last_scores, -1e30)
        last_max = jnp.max(last_scores, axis=-1)
        last_weights = jnp.where(last_allowed, jnp.exp(last_scores - last_max[..., None]), 0.0)
        last_sum = jnp.sum(last_weights, axis=-1)
        last_mix = jnp.einsum(
            "tqk,kd->tqd",
            last_weights.astype(jnp.bfloat16),
            values_g,
            preferred_element_type=jnp.float32,
        )
        last_parts.append((last_mix / last_sum[..., None]).reshape(reqs, per_group * HD))
    last_context = jnp.concatenate(last_parts, axis=1).astype(jnp.bfloat16)
    out_rows = jnp.concatenate([context, last_context], axis=0)
    context_all = lax.all_gather(out_rows, "kv", axis=0, tiled=False)
    head_sum = None
    for shift, piece in enumerate(weight_pieces):
        source = lax.dynamic_index_in_dim(
            context_all, (me_kv - shift) % kv_count, 0, keepdims=False
        )
        part = jnp.dot(source, piece, preferred_element_type=jnp.float32)
        part = part.astype(jnp.bfloat16).astype(jnp.float32)
        head_sum = part if head_sum is None else head_sum + part
    hidden = (seq_in.astype(jnp.float32) + head_sum[:tok_rows]).astype(jnp.bfloat16)
    chosen = (seq_last + head_sum[tok_rows:]).astype(jnp.bfloat16).astype(jnp.float32)
    square_part = jnp.sum(chosen * chosen, axis=-1)
    scaled = (chosen * final_gain).astype(jnp.bfloat16)
    logit_part = lax.dot_general(
        scaled, table, (((1,), (1,)), ((), ())), preferred_element_type=jnp.float32
    )
    packed_sums = ordered_sum(
        permute_pieces(jnp.concatenate([logit_part, square_part[:, None]], axis=1), kv_count),
        kv_count,
    )
    logit_sum = packed_sums[:, :-1]
    square_sum = packed_sums[:, -1]
    inv_rms = lax.rsqrt(square_sum / D + 1e-05)
    last_norm = (chosen * inv_rms[:, None] * final_gain).astype(jnp.bfloat16)
    local_max = jnp.max(inv_rms[:, None] * logit_sum, axis=-1)
    max_logit = tree_max(local_max, "blk", blocks)
    return (hidden, last_norm, max_logit)


def solution(mesh):
    placed = (
        P("blk", None, None),
        P("blk", None),
        P("blk"),
        P(),
        P(None, None, "kv"),
        P("kv", None),
        P(None, "kv"),
        P("blk", "kv"),
        P(),
        P(None, "kv"),
        P(None, None, "kv"),
        P("kv", None),
        P(),
        P("kv"),
        P("blk", "kv"),
    )
    return jax.shard_map(
        on_device,
        mesh=mesh,
        in_specs=placed,
        out_specs=(P("blk", "kv"), P(None, "kv"), P()),
        check_vma=False,
    )
```

```python
import functools
import math

import jax
import jax.numpy as jnp
from jax import lax
from jax.experimental import pallas as pl
from jax.experimental.pallas import tpu as pltpu
from jax.sharding import PartitionSpec as P

VHD = 88
D = 4096
QHEADS = 16
KVHEADS = 8
HD = 128


def layer_norm(inputs, gain):
    centre = jnp.mean(inputs, axis=-1, keepdims=True)
    centred = inputs - centre
    spread = jnp.mean(centred * centred, axis=-1, keepdims=True)
    return centred * lax.rsqrt(spread + 1e-06) * gain


def rotate(inputs, position):
    half_width = inputs.shape[-1] // 2
    inverse = 500000.0 ** (-jnp.arange(half_width, dtype=jnp.float32) * 2.0 / inputs.shape[-1])
    angles = position.astype(jnp.float32)[:, None] * inverse[None, :]
    cosine = jnp.cos(angles)[:, None, :]
    sine = jnp.sin(angles)[:, None, :]
    first = inputs[..., :half_width]
    second = inputs[..., half_width:]
    return jnp.concatenate(
        [first * cosine - second * sine, second * cosine + first * sine], axis=-1
    )


def request_info(row_index, req_lengths):
    ends_at = jnp.cumsum(req_lengths)
    starts_at = ends_at - req_lengths
    request_id = jnp.sum((row_index[:, None] >= ends_at[None, :]).astype(jnp.int32), axis=1)
    choose = request_id[:, None] == jnp.arange(req_lengths.shape[0], dtype=jnp.int32)[None, :]
    request_begin = jnp.sum(jnp.where(choose, starts_at[None, :], 0), axis=1)
    return (request_id, request_begin)


def flash_kernel(needed_ref, q_ref, k_ref, v_ref, qid_ref, qreq_ref, kid_ref, kreq_ref, o_ref,
                 max_ref, sum_ref, acc_ref, *, root):
    kb = pl.program_id(1)

    @pl.when(kb == 0)
    def _():
        max_ref[...] = jnp.full(max_ref.shape, -1e30, jnp.float32)
        sum_ref[...] = jnp.zeros(sum_ref.shape, jnp.float32)
        acc_ref[...] = jnp.zeros(acc_ref.shape, jnp.float32)

    @pl.when(needed_ref[kb] != 0)
    def _():
        scores = lax.dot_general(
            q_ref[...], k_ref[...], (((1,), (1,)), ((), ())), preferred_element_type=jnp.float32
        ) / root
        allowed = (kid_ref[...] <= qid_ref[...]) & (kreq_ref[...] == qreq_ref[...])
        scores = jnp.where(allowed, scores, -1e30)
        old_max = max_ref[...]
        new_max = jnp.maximum(old_max, jnp.max(scores, axis=1, keepdims=True))
        weights = jnp.where(allowed, jnp.exp(scores - new_max), 0.0)
        scale = jnp.exp(old_max - new_max)
        sum_ref[...] = sum_ref[...] * scale + jnp.sum(weights, axis=1, keepdims=True)
        acc_ref[...] = acc_ref[...] * scale + jnp.dot(
            weights.astype(jnp.bfloat16), v_ref[...], preferred_element_type=jnp.float32
        )
        max_ref[...] = new_max

    @pl.when(kb == pl.num_programs(1) - 1)
    def _():
        o_ref[...] = (acc_ref[...] / sum_ref[...]).astype(o_ref.dtype)


def flash_attention(needed, grouped_q, gathered, q_ids, q_req, k_ids, k_req, groups, tok_rows, root):
    blocks = gathered.shape[0]
    group_rows = grouped_q.shape[1]
    grid_spec = pltpu.PrefetchScalarGridSpec(
        num_scalar_prefetch=1,
        grid=(groups, blocks),
        in_specs=[
            pl.BlockSpec((None, group_rows, HD), lambda g, kb, n: (g, 0, 0)),
            pl.BlockSpec((None, tok_rows, HD), lambda g, kb, n: (kb, 0, g)),
            pl.BlockSpec((None, tok_rows, HD), lambda g, kb, n: (kb, 0, groups + g)),
            pl.BlockSpec((group_rows, 1), lambda g, kb, n: (0, 0)),
            pl.BlockSpec((group_rows, 1), lambda g, kb, n: (0, 0)),
            pl.BlockSpec((None, 1, tok_rows), lambda g, kb, n: (kb, 0, 0)),
            pl.BlockSpec((None, 1, tok_rows), lambda g, kb, n: (kb, 0, 0)),
        ],
        out_specs=pl.BlockSpec((None, group_rows, HD), lambda g, kb, n: (g, 0, 0)),
        scratch_shapes=[
            pltpu.VMEM((group_rows, 1), jnp.float32),
            pltpu.VMEM((group_rows, 1), jnp.float32),
            pltpu.VMEM((group_rows, HD), jnp.float32),
        ],
    )
    flops = 4 * groups * blocks * group_rows * tok_rows * HD
    return pl.pallas_call(
        functools.partial(flash_kernel, root=root),
        grid_spec=grid_spec,
        out_shape=jax.ShapeDtypeStruct((groups, group_rows, HD), jnp.bfloat16),
        compiler_params=pltpu.CompilerParams(dimension_semantics=("arbitrary", "arbitrary")),
        cost_estimate=pl.CostEstimate(
            flops=flops,
            transcendentals=groups * blocks * group_rows * tok_rows,
            bytes_accessed=2 * groups * blocks * tok_rows * HD * 2 + 4 * groups * group_rows * HD,
        ),
    )(needed, grouped_q, gathered, gathered, q_ids, q_req, k_ids, k_req)


def gather_by_permutes(local, count):
    me = lax.axis_index("kv")
    pieces = [local]
    for shift in range(1, count):
        pieces.append(
            lax.ppermute(local, "kv", perm=[(i, (i + shift) % count) for i in range(count)])
        )
    stacked = jnp.stack(pieces)
    order = (me - jnp.arange(count, dtype=jnp.int32)) % count
    ordered = jnp.take(stacked, order, axis=0)
    return jnp.concatenate([ordered[j] for j in range(count)], axis=1)


def permute_pieces(local, count):
    pieces = [local]
    for shift in range(1, count):
        pieces.append(
            lax.ppermute(local, "kv", perm=[(i, (i + shift) % count) for i in range(count)])
        )
    return pieces


def ordered_sum(pieces, count):
    me = lax.axis_index("kv")
    stacked = jnp.stack([piece.astype(jnp.float32) for piece in pieces])
    order = (me - jnp.arange(count, dtype=jnp.int32)) % count
    return jnp.sum(jnp.take(stacked, order, axis=0), axis=0)


def tree_max(values, axis, count):
    if count & (count - 1):
        return lax.pmax(values, axis)
    step = 1
    while step < count:
        other = lax.ppermute(values, axis, perm=[(i, i ^ step) for i in range(count)])
        values = jnp.maximum(values, other)
        step *= 2
    return values


def on_device(
    patches,
    merged_grid,
    picture_start,
    vis_gain,
    vis_qkv,
    vis_out,
    merge_weight,
    text_embed,
    dec_gain,
    w_query,
    w_keyval,
    w_out,
    req_lengths,
    final_gain,
    table,
):
    pictures, patch_max, vis_width = patches.shape
    merged_max = patch_max // 4
    vis_cols = vis_qkv.shape[2]
    vis_heads = vis_cols // VHD
    tok_rows, feat_dev = text_embed.shape
    kv_count = D // text_embed.shape[1]
    text_rows = gather_by_permutes(text_embed, kv_count)
    inputs = patches.astype(jnp.float32)
    normed = layer_norm(inputs, vis_gain).astype(jnp.bfloat16)
    packed = jnp.einsum(
        "pnd,dce->pnce", normed, vis_qkv, preferred_element_type=jnp.float32
    ).astype(jnp.bfloat16)
    packed = packed.reshape(pictures, patch_max, 3, vis_heads, VHD)
    scores = jnp.einsum(
        "pqhd,pkhd->phqk", packed[:, :, 0], packed[:, :, 1], preferred_element_type=jnp.float32
    ) / math.sqrt(VHD)
    cell_count = merged_grid[:, 0] * merged_grid[:, 1]
    valid_cols = jnp.arange(patch_max, dtype=jnp.int32)[None, :] < 4 * cell_count[:, None]
    scores = jnp.where(valid_cols[:, None, None, :], scores, -1e30)
    weights = jnp.exp(scores - jnp.max(scores, axis=-1, keepdims=True))
    weight_sum = jnp.sum(weights, axis=-1)
    mixed_rows = jnp.einsum(
        "phqk,pkhd->pqhd",
        weights.astype(jnp.bfloat16),
        packed[:, :, 2],
        preferred_element_type=jnp.float32,
    )
    mixed_rows = (
        (mixed_rows / jnp.transpose(weight_sum, (0, 2, 1))[..., None])
        .astype(jnp.bfloat16)
        .reshape(pictures, patch_max, vis_cols)
    )
    head_part = jnp.einsum("pnc,cd->pnd", mixed_rows, vis_out, preferred_element_type=jnp.float32)
    head_pooled = jnp.mean(head_part.reshape(pictures, merged_max, 4, vis_width), axis=2)
    head_total = jnp.sum(
        lax.all_gather(head_pooled.astype(jnp.bfloat16), "kv", axis=0, tiled=False).astype(
            jnp.float32
        ),
        axis=0,
    )
    input_pooled = jnp.mean(inputs.reshape(pictures, merged_max, 4, vis_width), axis=2)
    pooled = (input_pooled + head_total).astype(jnp.bfloat16)
    merged = jnp.einsum(
        "pmd,de->pme", pooled, merge_weight, preferred_element_type=jnp.float32
    ).astype(jnp.bfloat16)
    me_kv = lax.axis_index("kv")
    out_source, merged = lax.optimization_barrier((w_out, merged))
    weight_pieces = [lax.dynamic_slice_in_dim(out_source, me_kv * feat_dev, feat_dev, 1)]
    for shift in range(1, kv_count):
        payload = lax.dynamic_slice_in_dim(
            out_source, ((me_kv + shift) % kv_count) * feat_dev, feat_dev, 1
        )
        weight_pieces.append(
            lax.ppermute(
                payload, "kv", perm=[(i, (i + shift) % kv_count) for i in range(kv_count)]
            )
        )
    block_base = lax.axis_index("blk") * tok_rows
    slot_index = jnp.arange(merged_max, dtype=jnp.int32)
    target = picture_start[:, None] + slot_index[None, :] - block_base
    target = jnp.where(slot_index[None, :] < cell_count[:, None], target, -1).reshape(-1)
    local_rows = jnp.arange(tok_rows, dtype=jnp.int32)
    one_hot = local_rows[:, None] == target[None, :]
    placed = jnp.dot(
        one_hot.astype(jnp.bfloat16),
        merged.reshape(pictures * merged_max, feat_dev),
        preferred_element_type=jnp.float32,
    )
    is_vision = jnp.any(one_hot, axis=1)
    seq_in = jnp.where(is_vision[:, None], placed.astype(jnp.bfloat16), text_embed)
    merged_rows = lax.all_gather(
        merged.reshape(pictures * merged_max, feat_dev), "kv", axis=1, tiled=True
    )
    placed_rows = jnp.dot(one_hot.astype(jnp.bfloat16), merged_rows, preferred_element_type=jnp.float32)
    full_rows = jnp.where(is_vision[:, None], placed_rows.astype(jnp.bfloat16), text_rows)
    full_float = full_rows.astype(jnp.float32)
    dec_normed = (
        full_float
        * lax.rsqrt(jnp.mean(full_float * full_float, axis=-1, keepdims=True) + 1e-05)
        * dec_gain
    ).astype(jnp.bfloat16)
    per_group = QHEADS // KVHEADS
    kv_heads = w_keyval.shape[2] // HD
    row_ids = block_base + local_rows
    request_id, request_begin = request_info(row_ids, req_lengths)
    position = row_ids - request_begin
    query_proj = jnp.dot(dec_normed, w_query, preferred_element_type=jnp.float32).reshape(
        tok_rows, kv_heads * per_group, HD
    )
    query_proj = (
        rotate(query_proj, position)
        .astype(jnp.bfloat16)
        .reshape(tok_rows, kv_heads * per_group * HD)
    )
    key_value = jnp.einsum("td,dce->tce", dec_normed, w_keyval, preferred_element_type=jnp.float32)
    key_rows = (
        rotate(key_value[:, 0].reshape(tok_rows, kv_heads, HD), position)
        .astype(jnp.bfloat16)
        .reshape(tok_rows, kv_heads * HD)
    )
    value_rows = key_value[:, 1].astype(jnp.bfloat16)
    query_req, query_begin = request_info(row_ids, req_lengths)
    root = math.sqrt(HD)
    reqs = req_lengths.shape[0]
    ends_at = jnp.cumsum(req_lengths)
    last_ids = ends_at - 1
    picker = (local_rows[None, :] == (last_ids - block_base)[:, None]).astype(jnp.bfloat16)
    query_last = jnp.dot(picker, query_proj, preferred_element_type=jnp.float32)
    seq_last = jnp.dot(picker, seq_in, preferred_element_type=jnp.float32)
    extras = jnp.concatenate([query_last, seq_last], axis=1).astype(jnp.bfloat16).reshape(-1)
    kv_width = key_rows.shape[1]
    ship_width = 2 * kv_width
    extra_rows = -(-extras.shape[0] // ship_width)
    extras = jnp.pad(extras, (0, extra_rows * ship_width - extras.shape[0]))
    shipped = jnp.concatenate([key_rows, value_rows], axis=1)
    shipped = jnp.concatenate([shipped, extras.reshape(extra_rows, ship_width)], axis=0)
    gathered = lax.all_gather(shipped, "blk", axis=0, tiled=False)
    gathered, weight_pieces = lax.optimization_barrier((gathered, weight_pieces))
    blocks = gathered.shape[0]
    q_cols = query_proj.shape[1]
    extras_all = gathered[:, tok_rows:].reshape(blocks, -1)[:, : reqs * (q_cols + feat_dev)]
    extras_all = jnp.sum(extras_all.astype(jnp.float32).reshape(blocks, reqs, -1), axis=0)
    query_last = extras_all[:, :q_cols].astype(jnp.bfloat16)
    seq_last = extras_all[:, q_cols:]
    block_index = lax.axis_index("blk")
    first_begin = query_begin[0]
    block_ids = jnp.arange(blocks, dtype=jnp.int32)
    needed = (
        (block_ids <= block_index) & (block_ids * tok_rows + tok_rows - 1 >= first_begin)
    ).astype(jnp.int32)
    group_rows = tok_rows * per_group
    grouped_q = jnp.transpose(
        query_proj.reshape(tok_rows, kv_heads, per_group, HD), (1, 0, 2, 3)
    ).reshape(kv_heads, group_rows, HD)
    q_ids = jnp.repeat(row_ids, per_group)[:, None]
    q_req = jnp.repeat(query_req, per_group)[:, None]
    all_ids = jnp.arange(blocks * tok_rows, dtype=jnp.int32)
    all_req, unused = request_info(all_ids, req_lengths)
    k_ids = all_ids.reshape(blocks, 1, tok_rows)
    k_req = all_req.reshape(blocks, 1, tok_rows)
    context = flash_attention(
        needed, grouped_q, gathered, q_ids, q_req, k_ids, k_req, kv_heads, tok_rows, root
    )
    context = jnp.transpose(
        context.reshape(kv_heads, tok_rows, per_group, HD), (1, 0, 2, 3)
    ).reshape(tok_rows, kv_heads * per_group * HD)
    all_ids = jnp.arange(blocks * tok_rows, dtype=jnp.int32)
    last_begin = ends_at - req_lengths
    last_allowed = (all_ids[None, :] >= last_begin[:, None]) & (all_ids[None, :] <= last_ids[:, None])
    last_allowed = last_allowed[:, None, :]
    last_parts = []
    for g in range(kv_heads):
        keys_g = gathered[:, :tok_rows, g * HD : (g + 1) * HD].reshape(blocks * tok_rows, HD)
        values_g = gathered[:, :tok_rows, kv_width + g * HD : kv_width + (g + 1) * HD].reshape(
            blocks * tok_rows, HD
        )
        last_q = query_last[:, g * per_group * HD : (g + 1) * per_group * HD].reshape(
            reqs, per_group, HD
        )
        last_scores = (
            jnp.einsum("tqd,kd->tqk", last_q, keys_g, preferred_element_type=jnp.float32) / root
        )
        last_scores = jnp.where(last_allowed, last_scores, -1e30)
        last_max = jnp.max(last_scores, axis=-1)
        last_weights = jnp.where(last_allowed, jnp.exp(last_scores - last_max[..., None]), 0.0)
        last_sum = jnp.sum(last_weights, axis=-1)
        last_mix = jnp.einsum(
            "tqk,kd->tqd",
            last_weights.astype(jnp.bfloat16),
            values_g,
            preferred_element_type=jnp.float32,
        )
        last_parts.append((last_mix / last_sum[..., None]).reshape(reqs, per_group * HD))
    last_context = jnp.concatenate(last_parts, axis=1).astype(jnp.bfloat16)
    out_rows = jnp.concatenate([context, last_context], axis=0)
    context_all = lax.all_gather(out_rows, "kv", axis=0, tiled=False)
    head_sum = None
    for shift, piece in enumerate(weight_pieces):
        source = lax.dynamic_index_in_dim(
            context_all, (me_kv - shift) % kv_count, 0, keepdims=False
        )
        part = jnp.dot(source, piece, preferred_element_type=jnp.float32)
        part = part.astype(jnp.bfloat16).astype(jnp.float32)
        head_sum = part if head_sum is None else head_sum + part
    hidden = (seq_in.astype(jnp.float32) + head_sum[:tok_rows]).astype(jnp.bfloat16)
    chosen = (seq_last + head_sum[tok_rows:]).astype(jnp.bfloat16).astype(jnp.float32)
    square_part = jnp.sum(chosen * chosen, axis=-1)
    scaled = (chosen * final_gain).astype(jnp.bfloat16)
    logit_part = lax.dot_general(
        scaled, table, (((1,), (1,)), ((), ())), preferred_element_type=jnp.float32
    )
    packed_sums = ordered_sum(
        permute_pieces(jnp.concatenate([logit_part, square_part[:, None]], axis=1), kv_count),
        kv_count,
    )
    logit_sum = packed_sums[:, :-1]
    square_sum = packed_sums[:, -1]
    inv_rms = lax.rsqrt(square_sum / D + 1e-05)
    last_norm = (chosen * inv_rms[:, None] * final_gain).astype(jnp.bfloat16)
    local_max = jnp.max(inv_rms[:, None] * logit_sum, axis=-1)
    max_logit = tree_max(local_max, "blk", blocks)
    return (hidden, last_norm, max_logit)


def solution(mesh):
    placed = (
        P("blk", None, None),
        P("blk", None),
        P("blk"),
        P(),
        P(None, None, "kv"),
        P("kv", None),
        P(None, "kv"),
        P("blk", "kv"),
        P(),
        P(None, "kv"),
        P(None, None, "kv"),
        P("kv", None),
        P(),
        P("kv"),
        P("blk", "kv"),
    )
    return jax.shard_map(
        on_device,
        mesh=mesh,
        in_specs=placed,
        out_specs=(P("blk", "kv"), P(None, "kv"), P()),
        check_vma=False,
    )
```

```python
import functools
import math

import jax
import jax.numpy as jnp
from jax import lax
from jax.experimental import pallas as pl
from jax.experimental.pallas import tpu as pltpu
from jax.sharding import PartitionSpec as P

VHD = 88
D = 4096
QHEADS = 16
KVHEADS = 8
HD = 128


def layer_norm(inputs, gain):
    centre = jnp.mean(inputs, axis=-1, keepdims=True)
    centred = inputs - centre
    spread = jnp.mean(centred * centred, axis=-1, keepdims=True)
    return centred * lax.rsqrt(spread + 1e-06) * gain


def rotate(inputs, position):
    half_width = inputs.shape[-1] // 2
    inverse = 500000.0 ** (-jnp.arange(half_width, dtype=jnp.float32) * 2.0 / inputs.shape[-1])
    angles = position.astype(jnp.float32)[:, None] * inverse[None, :]
    cosine = jnp.cos(angles)[:, None, :]
    sine = jnp.sin(angles)[:, None, :]
    first = inputs[..., :half_width]
    second = inputs[..., half_width:]
    return jnp.concatenate(
        [first * cosine - second * sine, second * cosine + first * sine], axis=-1
    )


def request_info(row_index, req_lengths):
    ends_at = jnp.cumsum(req_lengths)
    starts_at = ends_at - req_lengths
    request_id = jnp.sum((row_index[:, None] >= ends_at[None, :]).astype(jnp.int32), axis=1)
    choose = request_id[:, None] == jnp.arange(req_lengths.shape[0], dtype=jnp.int32)[None, :]
    request_begin = jnp.sum(jnp.where(choose, starts_at[None, :], 0), axis=1)
    return (request_id, request_begin)


def flash_kernel(needed_ref, q_ref, k_ref, v_ref, qid_ref, qreq_ref, kid_ref, kreq_ref, o_ref,
                 max_ref, sum_ref, acc_ref, *, root):
    kb = pl.program_id(1)

    @pl.when(kb == 0)
    def _():
        max_ref[...] = jnp.full(max_ref.shape, -1e30, jnp.float32)
        sum_ref[...] = jnp.zeros(sum_ref.shape, jnp.float32)
        acc_ref[...] = jnp.zeros(acc_ref.shape, jnp.float32)

    @pl.when(needed_ref[kb] != 0)
    def _():
        scores = lax.dot_general(
            q_ref[...], k_ref[...], (((1,), (1,)), ((), ())), preferred_element_type=jnp.float32
        ) / root
        allowed = (kid_ref[...] <= qid_ref[...]) & (kreq_ref[...] == qreq_ref[...])
        scores = jnp.where(allowed, scores, -1e30)
        old_max = max_ref[...]
        new_max = jnp.maximum(old_max, jnp.max(scores, axis=1, keepdims=True))
        weights = jnp.where(allowed, jnp.exp(scores - new_max), 0.0)
        scale = jnp.exp(old_max - new_max)
        sum_ref[...] = sum_ref[...] * scale + jnp.sum(weights, axis=1, keepdims=True)
        acc_ref[...] = acc_ref[...] * scale + jnp.dot(
            weights.astype(jnp.bfloat16), v_ref[...], preferred_element_type=jnp.float32
        )
        max_ref[...] = new_max

    @pl.when(kb == pl.num_programs(1) - 1)
    def _():
        o_ref[...] = (acc_ref[...] / sum_ref[...]).astype(o_ref.dtype)


def flash_attention(needed, grouped_q, gathered, q_ids, q_req, k_ids, k_req, groups, tok_rows, root):
    blocks = gathered.shape[0]
    group_rows = grouped_q.shape[1]
    grid_spec = pltpu.PrefetchScalarGridSpec(
        num_scalar_prefetch=1,
        grid=(groups, blocks),
        in_specs=[
            pl.BlockSpec((None, group_rows, HD), lambda g, kb, n: (g, 0, 0)),
            pl.BlockSpec((None, tok_rows, HD), lambda g, kb, n: (kb, 0, g)),
            pl.BlockSpec((None, tok_rows, HD), lambda g, kb, n: (kb, 0, groups + g)),
            pl.BlockSpec((group_rows, 1), lambda g, kb, n: (0, 0)),
            pl.BlockSpec((group_rows, 1), lambda g, kb, n: (0, 0)),
            pl.BlockSpec((None, 1, tok_rows), lambda g, kb, n: (kb, 0, 0)),
            pl.BlockSpec((None, 1, tok_rows), lambda g, kb, n: (kb, 0, 0)),
        ],
        out_specs=pl.BlockSpec((None, group_rows, HD), lambda g, kb, n: (g, 0, 0)),
        scratch_shapes=[
            pltpu.VMEM((group_rows, 1), jnp.float32),
            pltpu.VMEM((group_rows, 1), jnp.float32),
            pltpu.VMEM((group_rows, HD), jnp.float32),
        ],
    )
    flops = 4 * groups * blocks * group_rows * tok_rows * HD
    return pl.pallas_call(
        functools.partial(flash_kernel, root=root),
        grid_spec=grid_spec,
        out_shape=jax.ShapeDtypeStruct((groups, group_rows, HD), jnp.bfloat16),
        compiler_params=pltpu.CompilerParams(dimension_semantics=("arbitrary", "arbitrary")),
        cost_estimate=pl.CostEstimate(
            flops=flops,
            transcendentals=groups * blocks * group_rows * tok_rows,
            bytes_accessed=2 * groups * blocks * tok_rows * HD * 2 + 4 * groups * group_rows * HD,
        ),
    )(needed, grouped_q, gathered, gathered, q_ids, q_req, k_ids, k_req)


def gather_by_permutes(local, count):
    me = lax.axis_index("kv")
    pieces = [local]
    for shift in range(1, count):
        pieces.append(
            lax.ppermute(local, "kv", perm=[(i, (i + shift) % count) for i in range(count)])
        )
    stacked = jnp.stack(pieces)
    order = (me - jnp.arange(count, dtype=jnp.int32)) % count
    ordered = jnp.take(stacked, order, axis=0)
    return jnp.concatenate([ordered[j] for j in range(count)], axis=1)


def permute_pieces(local, count):
    pieces = [local]
    for shift in range(1, count):
        pieces.append(
            lax.ppermute(local, "kv", perm=[(i, (i + shift) % count) for i in range(count)])
        )
    return pieces


def ordered_sum(pieces, count):
    me = lax.axis_index("kv")
    stacked = jnp.stack([piece.astype(jnp.float32) for piece in pieces])
    order = (me - jnp.arange(count, dtype=jnp.int32)) % count
    return jnp.sum(jnp.take(stacked, order, axis=0), axis=0)


def tree_max(values, axis, count):
    if count & (count - 1):
        return lax.pmax(values, axis)
    step = 1
    while step < count:
        other = lax.ppermute(values, axis, perm=[(i, i ^ step) for i in range(count)])
        values = jnp.maximum(values, other)
        step *= 2
    return values


def on_device(
    patches,
    merged_grid,
    picture_start,
    vis_gain,
    vis_qkv,
    vis_out,
    merge_weight,
    text_embed,
    dec_gain,
    w_query,
    w_keyval,
    w_out,
    req_lengths,
    final_gain,
    table,
):
    pictures, patch_max, vis_width = patches.shape
    merged_max = patch_max // 4
    vis_cols = vis_qkv.shape[2]
    vis_heads = vis_cols // VHD
    tok_rows, feat_dev = text_embed.shape
    kv_count = D // text_embed.shape[1]
    text_rows = gather_by_permutes(text_embed, kv_count)
    inputs = patches.astype(jnp.float32)
    normed = layer_norm(inputs, vis_gain).astype(jnp.bfloat16)
    packed = jnp.einsum(
        "pnd,dce->pnce", normed, vis_qkv, preferred_element_type=jnp.float32
    ).astype(jnp.bfloat16)
    packed = packed.reshape(pictures, patch_max, 3, vis_heads, VHD)
    scores = jnp.einsum(
        "pqhd,pkhd->phqk", packed[:, :, 0], packed[:, :, 1], preferred_element_type=jnp.float32
    ) / math.sqrt(VHD)
    cell_count = merged_grid[:, 0] * merged_grid[:, 1]
    valid_cols = jnp.arange(patch_max, dtype=jnp.int32)[None, :] < 4 * cell_count[:, None]
    scores = jnp.where(valid_cols[:, None, None, :], scores, -1e30)
    weights = jnp.exp(scores - jnp.max(scores, axis=-1, keepdims=True))
    weight_sum = jnp.sum(weights, axis=-1)
    mixed_rows = jnp.einsum(
        "phqk,pkhd->pqhd",
        weights.astype(jnp.bfloat16),
        packed[:, :, 2],
        preferred_element_type=jnp.float32,
    )
    mixed_rows = (
        (mixed_rows / jnp.transpose(weight_sum, (0, 2, 1))[..., None])
        .astype(jnp.bfloat16)
        .reshape(pictures, patch_max, vis_cols)
    )
    head_part = jnp.einsum("pnc,cd->pnd", mixed_rows, vis_out, preferred_element_type=jnp.float32)
    head_pooled = jnp.mean(head_part.reshape(pictures, merged_max, 4, vis_width), axis=2)
    head_total = lax.psum(head_pooled.astype(jnp.bfloat16), "kv").astype(jnp.float32)
    input_pooled = jnp.mean(inputs.reshape(pictures, merged_max, 4, vis_width), axis=2)
    pooled = (input_pooled + head_total).astype(jnp.bfloat16)
    merged = jnp.einsum(
        "pmd,de->pme", pooled, merge_weight, preferred_element_type=jnp.float32
    ).astype(jnp.bfloat16)
    me_kv = lax.axis_index("kv")
    out_source, merged = lax.optimization_barrier((w_out, merged))
    weight_pieces = [lax.dynamic_slice_in_dim(out_source, me_kv * feat_dev, feat_dev, 1)]
    for shift in range(1, kv_count):
        payload = lax.dynamic_slice_in_dim(
            out_source, ((me_kv + shift) % kv_count) * feat_dev, feat_dev, 1
        )
        weight_pieces.append(
            lax.ppermute(
                payload, "kv", perm=[(i, (i + shift) % kv_count) for i in range(kv_count)]
            )
        )
    block_base = lax.axis_index("blk") * tok_rows
    slot_index = jnp.arange(merged_max, dtype=jnp.int32)
    target = picture_start[:, None] + slot_index[None, :] - block_base
    target = jnp.where(slot_index[None, :] < cell_count[:, None], target, -1).reshape(-1)
    local_rows = jnp.arange(tok_rows, dtype=jnp.int32)
    one_hot = local_rows[:, None] == target[None, :]
    placed = jnp.dot(
        one_hot.astype(jnp.bfloat16),
        merged.reshape(pictures * merged_max, feat_dev),
        preferred_element_type=jnp.float32,
    )
    is_vision = jnp.any(one_hot, axis=1)
    seq_in = jnp.where(is_vision[:, None], placed.astype(jnp.bfloat16), text_embed)
    merged_rows = lax.all_gather(
        merged.reshape(pictures * merged_max, feat_dev), "kv", axis=1, tiled=True
    )
    placed_rows = jnp.dot(one_hot.astype(jnp.bfloat16), merged_rows, preferred_element_type=jnp.float32)
    full_rows = jnp.where(is_vision[:, None], placed_rows.astype(jnp.bfloat16), text_rows)
    full_float = full_rows.astype(jnp.float32)
    dec_normed = (
        full_float
        * lax.rsqrt(jnp.mean(full_float * full_float, axis=-1, keepdims=True) + 1e-05)
        * dec_gain
    ).astype(jnp.bfloat16)
    per_group = QHEADS // KVHEADS
    kv_heads = w_keyval.shape[2] // HD
    row_ids = block_base + local_rows
    request_id, request_begin = request_info(row_ids, req_lengths)
    position = row_ids - request_begin
    query_proj = jnp.dot(dec_normed, w_query, preferred_element_type=jnp.float32).reshape(
        tok_rows, kv_heads * per_group, HD
    )
    query_proj = (
        rotate(query_proj, position)
        .astype(jnp.bfloat16)
        .reshape(tok_rows, kv_heads * per_group * HD)
    )
    key_value = jnp.einsum("td,dce->tce", dec_normed, w_keyval, preferred_element_type=jnp.float32)
    key_rows = (
        rotate(key_value[:, 0].reshape(tok_rows, kv_heads, HD), position)
        .astype(jnp.bfloat16)
        .reshape(tok_rows, kv_heads * HD)
    )
    value_rows = key_value[:, 1].astype(jnp.bfloat16)
    query_req, query_begin = request_info(row_ids, req_lengths)
    root = math.sqrt(HD)
    reqs = req_lengths.shape[0]
    ends_at = jnp.cumsum(req_lengths)
    last_ids = ends_at - 1
    picker = (local_rows[None, :] == (last_ids - block_base)[:, None]).astype(jnp.bfloat16)
    query_last = jnp.dot(picker, query_proj, preferred_element_type=jnp.float32)
    seq_last = jnp.dot(picker, seq_in, preferred_element_type=jnp.float32)
    extras = jnp.concatenate([query_last, seq_last], axis=1).astype(jnp.bfloat16).reshape(-1)
    kv_width = key_rows.shape[1]
    ship_width = 2 * kv_width
    extra_rows = -(-extras.shape[0] // ship_width)
    extras = jnp.pad(extras, (0, extra_rows * ship_width - extras.shape[0]))
    shipped = jnp.concatenate([key_rows, value_rows], axis=1)
    shipped = jnp.concatenate([shipped, extras.reshape(extra_rows, ship_width)], axis=0)
    gathered = lax.all_gather(shipped, "blk", axis=0, tiled=False)
    gathered, weight_pieces = lax.optimization_barrier((gathered, weight_pieces))
    blocks = gathered.shape[0]
    q_cols = query_proj.shape[1]
    extras_all = gathered[:, tok_rows:].reshape(blocks, -1)[:, : reqs * (q_cols + feat_dev)]
    extras_all = jnp.sum(extras_all.astype(jnp.float32).reshape(blocks, reqs, -1), axis=0)
    query_last = extras_all[:, :q_cols].astype(jnp.bfloat16)
    seq_last = extras_all[:, q_cols:]
    block_index = lax.axis_index("blk")
    first_begin = query_begin[0]
    block_ids = jnp.arange(blocks, dtype=jnp.int32)
    needed = (
        (block_ids <= block_index) & (block_ids * tok_rows + tok_rows - 1 >= first_begin)
    ).astype(jnp.int32)
    group_rows = tok_rows * per_group
    grouped_q = jnp.transpose(
        query_proj.reshape(tok_rows, kv_heads, per_group, HD), (1, 0, 2, 3)
    ).reshape(kv_heads, group_rows, HD)
    q_ids = jnp.repeat(row_ids, per_group)[:, None]
    q_req = jnp.repeat(query_req, per_group)[:, None]
    all_ids = jnp.arange(blocks * tok_rows, dtype=jnp.int32)
    all_req, unused = request_info(all_ids, req_lengths)
    k_ids = all_ids.reshape(blocks, 1, tok_rows)
    k_req = all_req.reshape(blocks, 1, tok_rows)
    context = flash_attention(
        needed, grouped_q, gathered, q_ids, q_req, k_ids, k_req, kv_heads, tok_rows, root
    )
    context = jnp.transpose(
        context.reshape(kv_heads, tok_rows, per_group, HD), (1, 0, 2, 3)
    ).reshape(tok_rows, kv_heads * per_group * HD)
    all_ids = jnp.arange(blocks * tok_rows, dtype=jnp.int32)
    last_begin = ends_at - req_lengths
    last_allowed = (all_ids[None, :] >= last_begin[:, None]) & (all_ids[None, :] <= last_ids[:, None])
    last_allowed = last_allowed[:, None, :]
    last_parts = []
    for g in range(kv_heads):
        keys_g = gathered[:, :tok_rows, g * HD : (g + 1) * HD].reshape(blocks * tok_rows, HD)
        values_g = gathered[:, :tok_rows, kv_width + g * HD : kv_width + (g + 1) * HD].reshape(
            blocks * tok_rows, HD
        )
        last_q = query_last[:, g * per_group * HD : (g + 1) * per_group * HD].reshape(
            reqs, per_group, HD
        )
        last_scores = (
            jnp.einsum("tqd,kd->tqk", last_q, keys_g, preferred_element_type=jnp.float32) / root
        )
        last_scores = jnp.where(last_allowed, last_scores, -1e30)
        last_max = jnp.max(last_scores, axis=-1)
        last_weights = jnp.where(last_allowed, jnp.exp(last_scores - last_max[..., None]), 0.0)
        last_sum = jnp.sum(last_weights, axis=-1)
        last_mix = jnp.einsum(
            "tqk,kd->tqd",
            last_weights.astype(jnp.bfloat16),
            values_g,
            preferred_element_type=jnp.float32,
        )
        last_parts.append((last_mix / last_sum[..., None]).reshape(reqs, per_group * HD))
    last_context = jnp.concatenate(last_parts, axis=1).astype(jnp.bfloat16)
    out_rows = jnp.concatenate([context, last_context], axis=0)
    context_all = lax.all_gather(out_rows, "kv", axis=0, tiled=False)
    head_sum = None
    last_sum = None
    for shift, piece in enumerate(weight_pieces):
        source = lax.dynamic_index_in_dim(
            context_all, (me_kv - shift) % kv_count, 0, keepdims=False
        )
        part = jnp.dot(source[:tok_rows], piece, preferred_element_type=jnp.float32)
        part = part.astype(jnp.bfloat16).astype(jnp.float32)
        head_sum = part if head_sum is None else head_sum + part
        last_part = jnp.dot(source[tok_rows:], piece, preferred_element_type=jnp.float32)
        last_part = last_part.astype(jnp.bfloat16).astype(jnp.float32)
        last_sum = last_part if last_sum is None else last_sum + last_part
    hidden = (seq_in.astype(jnp.float32) + head_sum).astype(jnp.bfloat16)
    chosen = (seq_last + last_sum).astype(jnp.bfloat16).astype(jnp.float32)
    square_part = jnp.sum(chosen * chosen, axis=-1)
    scaled = (chosen * final_gain).astype(jnp.bfloat16)
    logit_part = lax.dot_general(
        scaled, table, (((1,), (1,)), ((), ())), preferred_element_type=jnp.float32
    )
    packed_sums = ordered_sum(
        permute_pieces(jnp.concatenate([logit_part, square_part[:, None]], axis=1), kv_count),
        kv_count,
    )
    logit_sum = packed_sums[:, :-1]
    square_sum = packed_sums[:, -1]
    inv_rms = lax.rsqrt(square_sum / D + 1e-05)
    last_norm = (chosen * inv_rms[:, None] * final_gain).astype(jnp.bfloat16)
    local_max = jnp.max(inv_rms[:, None] * logit_sum, axis=-1)
    max_logit = tree_max(local_max, "blk", blocks)
    return (hidden, last_norm, max_logit)


def solution(mesh):
    placed = (
        P("blk", None, None),
        P("blk", None),
        P("blk"),
        P(),
        P(None, None, "kv"),
        P("kv", None),
        P(None, "kv"),
        P("blk", "kv"),
        P(),
        P(None, "kv"),
        P(None, None, "kv"),
        P("kv", None),
        P(),
        P("kv"),
        P("blk", "kv"),
    )
    return jax.shard_map(
        on_device,
        mesh=mesh,
        in_specs=placed,
        out_specs=(P("blk", "kv"), P(None, "kv"), P()),
        check_vma=False,
    )
```

```python
import functools
import math

import jax
import jax.numpy as jnp
from jax import lax
from jax.experimental import pallas as pl
from jax.experimental.pallas import tpu as pltpu
from jax.sharding import PartitionSpec as P

VHD = 88
D = 4096
QHEADS = 16
KVHEADS = 8
HD = 128


def layer_norm(inputs, gain):
    centre = jnp.mean(inputs, axis=-1, keepdims=True)
    centred = inputs - centre
    spread = jnp.mean(centred * centred, axis=-1, keepdims=True)
    return centred * lax.rsqrt(spread + 1e-06) * gain


def rotate(inputs, position):
    half_width = inputs.shape[-1] // 2
    inverse = 500000.0 ** (-jnp.arange(half_width, dtype=jnp.float32) * 2.0 / inputs.shape[-1])
    angles = position.astype(jnp.float32)[:, None] * inverse[None, :]
    cosine = jnp.cos(angles)[:, None, :]
    sine = jnp.sin(angles)[:, None, :]
    first = inputs[..., :half_width]
    second = inputs[..., half_width:]
    return jnp.concatenate(
        [first * cosine - second * sine, second * cosine + first * sine], axis=-1
    )


def request_info(row_index, req_lengths):
    ends_at = jnp.cumsum(req_lengths)
    starts_at = ends_at - req_lengths
    request_id = jnp.sum((row_index[:, None] >= ends_at[None, :]).astype(jnp.int32), axis=1)
    choose = request_id[:, None] == jnp.arange(req_lengths.shape[0], dtype=jnp.int32)[None, :]
    request_begin = jnp.sum(jnp.where(choose, starts_at[None, :], 0), axis=1)
    return (request_id, request_begin)


def flash_kernel(needed_ref, q_ref, k_ref, v_ref, qid_ref, qreq_ref, kid_ref, kreq_ref, o_ref,
                 max_ref, sum_ref, acc_ref, *, root):
    kb = pl.program_id(1)

    @pl.when(kb == 0)
    def _():
        max_ref[...] = jnp.full(max_ref.shape, -1e30, jnp.float32)
        sum_ref[...] = jnp.zeros(sum_ref.shape, jnp.float32)
        acc_ref[...] = jnp.zeros(acc_ref.shape, jnp.float32)

    @pl.when(needed_ref[kb] != 0)
    def _():
        scores = lax.dot_general(
            q_ref[...], k_ref[...], (((1,), (1,)), ((), ())), preferred_element_type=jnp.float32
        ) / root
        allowed = (kid_ref[...] <= qid_ref[...]) & (kreq_ref[...] == qreq_ref[...])
        scores = jnp.where(allowed, scores, -1e30)
        old_max = max_ref[...]
        new_max = jnp.maximum(old_max, jnp.max(scores, axis=1, keepdims=True))
        weights = jnp.where(allowed, jnp.exp(scores - new_max), 0.0)
        scale = jnp.exp(old_max - new_max)
        sum_ref[...] = sum_ref[...] * scale + jnp.sum(weights, axis=1, keepdims=True)
        acc_ref[...] = acc_ref[...] * scale + jnp.dot(
            weights.astype(jnp.bfloat16), v_ref[...], preferred_element_type=jnp.float32
        )
        max_ref[...] = new_max

    @pl.when(kb == pl.num_programs(1) - 1)
    def _():
        o_ref[...] = (acc_ref[...] / sum_ref[...]).astype(o_ref.dtype)


def flash_attention(needed, grouped_q, gathered, q_ids, q_req, k_ids, k_req, groups, tok_rows, root):
    blocks = gathered.shape[0]
    group_rows = grouped_q.shape[1]
    grid_spec = pltpu.PrefetchScalarGridSpec(
        num_scalar_prefetch=1,
        grid=(groups, blocks),
        in_specs=[
            pl.BlockSpec((None, group_rows, HD), lambda g, kb, n: (g, 0, 0)),
            pl.BlockSpec((None, tok_rows, HD), lambda g, kb, n: (kb, 0, g)),
            pl.BlockSpec((None, tok_rows, HD), lambda g, kb, n: (kb, 0, groups + g)),
            pl.BlockSpec((group_rows, 1), lambda g, kb, n: (0, 0)),
            pl.BlockSpec((group_rows, 1), lambda g, kb, n: (0, 0)),
            pl.BlockSpec((None, 1, tok_rows), lambda g, kb, n: (kb, 0, 0)),
            pl.BlockSpec((None, 1, tok_rows), lambda g, kb, n: (kb, 0, 0)),
        ],
        out_specs=pl.BlockSpec((None, group_rows, HD), lambda g, kb, n: (g, 0, 0)),
        scratch_shapes=[
            pltpu.VMEM((group_rows, 1), jnp.float32),
            pltpu.VMEM((group_rows, 1), jnp.float32),
            pltpu.VMEM((group_rows, HD), jnp.float32),
        ],
    )
    flops = 4 * groups * blocks * group_rows * tok_rows * HD
    return pl.pallas_call(
        functools.partial(flash_kernel, root=root),
        grid_spec=grid_spec,
        out_shape=jax.ShapeDtypeStruct((groups, group_rows, HD), jnp.bfloat16),
        compiler_params=pltpu.CompilerParams(dimension_semantics=("arbitrary", "arbitrary")),
        cost_estimate=pl.CostEstimate(
            flops=flops,
            transcendentals=groups * blocks * group_rows * tok_rows,
            bytes_accessed=2 * groups * blocks * tok_rows * HD * 2 + 4 * groups * group_rows * HD,
        ),
    )(needed, grouped_q, gathered, gathered, q_ids, q_req, k_ids, k_req)


def kv_exchange(local, count, paired):
    me = lax.axis_index("kv")
    if paired:
        chips = count // 2
        chip, core = me // 2, me % 2
        pieces = [local]
        for shift in range(1, chips):
            pieces.append(
                lax.ppermute(
                    local,
                    "kv",
                    perm=[(i, ((i // 2 + shift) % chips) * 2 + i % 2) for i in range(count)],
                )
            )
        bundle = jnp.stack(pieces)
        other = lax.ppermute(bundle, "kv", perm=[(i, i ^ 1) for i in range(count)])
        stacked = jnp.concatenate([bundle, other])
        source = jnp.arange(count, dtype=jnp.int32)
        slot = (chip - source // 2) % chips + jnp.where(source % 2 == core, 0, chips)
    else:
        pieces = [local]
        for shift in range(1, count):
            pieces.append(
                lax.ppermute(local, "kv", perm=[(i, (i + shift) % count) for i in range(count)])
            )
        stacked = jnp.stack(pieces)
        slot = (me - jnp.arange(count, dtype=jnp.int32)) % count
    return jnp.take(stacked, slot, axis=0)


def permute_pieces(local, count):
    pieces = [local]
    for shift in range(1, count):
        pieces.append(
            lax.ppermute(local, "kv", perm=[(i, (i + shift) % count) for i in range(count)])
        )
    return pieces


def ordered_sum(pieces, count):
    me = lax.axis_index("kv")
    stacked = jnp.stack([piece.astype(jnp.float32) for piece in pieces])
    order = (me - jnp.arange(count, dtype=jnp.int32)) % count
    return jnp.sum(jnp.take(stacked, order, axis=0), axis=0)


def tree_max(values, axis, count):
    if count & (count - 1):
        return lax.pmax(values, axis)
    step = 1
    while step < count:
        other = lax.ppermute(values, axis, perm=[(i, i ^ step) for i in range(count)])
        values = jnp.maximum(values, other)
        step *= 2
    return values


def on_device(
    paired,
    patches,
    merged_grid,
    picture_start,
    vis_gain,
    vis_qkv,
    vis_out,
    merge_weight,
    text_embed,
    dec_gain,
    w_query,
    w_keyval,
    w_out,
    req_lengths,
    final_gain,
    table,
):
    pictures, patch_max, vis_width = patches.shape
    merged_max = patch_max // 4
    vis_cols = vis_qkv.shape[2]
    vis_heads = vis_cols // VHD
    tok_rows, feat_dev = text_embed.shape
    kv_count = D // text_embed.shape[1]
    text_all = kv_exchange(text_embed, kv_count, paired)
    text_rows = jnp.concatenate([text_all[j] for j in range(kv_count)], axis=1)
    inputs = patches.astype(jnp.float32)
    normed = layer_norm(inputs, vis_gain).astype(jnp.bfloat16)
    packed = jnp.einsum(
        "pnd,dce->pnce", normed, vis_qkv, preferred_element_type=jnp.float32
    ).astype(jnp.bfloat16)
    packed = packed.reshape(pictures, patch_max, 3, vis_heads, VHD)
    scores = jnp.einsum(
        "pqhd,pkhd->phqk", packed[:, :, 0], packed[:, :, 1], preferred_element_type=jnp.float32
    ) / math.sqrt(VHD)
    cell_count = merged_grid[:, 0] * merged_grid[:, 1]
    valid_cols = jnp.arange(patch_max, dtype=jnp.int32)[None, :] < 4 * cell_count[:, None]
    scores = jnp.where(valid_cols[:, None, None, :], scores, -1e30)
    weights = jnp.exp(scores - jnp.max(scores, axis=-1, keepdims=True))
    weight_sum = jnp.sum(weights, axis=-1)
    mixed_rows = jnp.einsum(
        "phqk,pkhd->pqhd",
        weights.astype(jnp.bfloat16),
        packed[:, :, 2],
        preferred_element_type=jnp.float32,
    )
    mixed_rows = (
        (mixed_rows / jnp.transpose(weight_sum, (0, 2, 1))[..., None])
        .astype(jnp.bfloat16)
        .reshape(pictures, patch_max, vis_cols)
    )
    head_part = jnp.einsum("pnc,cd->pnd", mixed_rows, vis_out, preferred_element_type=jnp.float32)
    head_pooled = jnp.mean(head_part.reshape(pictures, merged_max, 4, vis_width), axis=2)
    head_total = jnp.sum(
        kv_exchange(head_pooled.astype(jnp.bfloat16), kv_count, paired).astype(jnp.float32),
        axis=0,
    )
    input_pooled = jnp.mean(inputs.reshape(pictures, merged_max, 4, vis_width), axis=2)
    pooled = (input_pooled + head_total).astype(jnp.bfloat16)
    merged = jnp.einsum(
        "pmd,de->pme", pooled, merge_weight, preferred_element_type=jnp.float32
    ).astype(jnp.bfloat16)
    me_kv = lax.axis_index("kv")
    out_source, merged = lax.optimization_barrier((w_out, merged))
    weight_pieces = [lax.dynamic_slice_in_dim(out_source, me_kv * feat_dev, feat_dev, 1)]
    for shift in range(1, kv_count):
        payload = lax.dynamic_slice_in_dim(
            out_source, ((me_kv + shift) % kv_count) * feat_dev, feat_dev, 1
        )
        weight_pieces.append(
            lax.ppermute(
                payload, "kv", perm=[(i, (i + shift) % kv_count) for i in range(kv_count)]
            )
        )
    block_base = lax.axis_index("blk") * tok_rows
    slot_index = jnp.arange(merged_max, dtype=jnp.int32)
    target = picture_start[:, None] + slot_index[None, :] - block_base
    target = jnp.where(slot_index[None, :] < cell_count[:, None], target, -1).reshape(-1)
    local_rows = jnp.arange(tok_rows, dtype=jnp.int32)
    one_hot = local_rows[:, None] == target[None, :]
    placed = jnp.dot(
        one_hot.astype(jnp.bfloat16),
        merged.reshape(pictures * merged_max, feat_dev),
        preferred_element_type=jnp.float32,
    )
    is_vision = jnp.any(one_hot, axis=1)
    seq_in = jnp.where(is_vision[:, None], placed.astype(jnp.bfloat16), text_embed)
    merged_all = kv_exchange(merged.reshape(pictures * merged_max, feat_dev), kv_count, paired)
    merged_rows = jnp.concatenate([merged_all[j] for j in range(kv_count)], axis=1)
    placed_rows = jnp.dot(one_hot.astype(jnp.bfloat16), merged_rows, preferred_element_type=jnp.float32)
    full_rows = jnp.where(is_vision[:, None], placed_rows.astype(jnp.bfloat16), text_rows)
    full_float = full_rows.astype(jnp.float32)
    dec_normed = (
        full_float
        * lax.rsqrt(jnp.mean(full_float * full_float, axis=-1, keepdims=True) + 1e-05)
        * dec_gain
    ).astype(jnp.bfloat16)
    per_group = QHEADS // KVHEADS
    kv_heads = w_keyval.shape[2] // HD
    row_ids = block_base + local_rows
    request_id, request_begin = request_info(row_ids, req_lengths)
    position = row_ids - request_begin
    query_proj = jnp.dot(dec_normed, w_query, preferred_element_type=jnp.float32).reshape(
        tok_rows, kv_heads * per_group, HD
    )
    query_proj = (
        rotate(query_proj, position)
        .astype(jnp.bfloat16)
        .reshape(tok_rows, kv_heads * per_group * HD)
    )
    key_value = jnp.einsum("td,dce->tce", dec_normed, w_keyval, preferred_element_type=jnp.float32)
    key_rows = (
        rotate(key_value[:, 0].reshape(tok_rows, kv_heads, HD), position)
        .astype(jnp.bfloat16)
        .reshape(tok_rows, kv_heads * HD)
    )
    value_rows = key_value[:, 1].astype(jnp.bfloat16)
    query_req, query_begin = request_info(row_ids, req_lengths)
    root = math.sqrt(HD)
    reqs = req_lengths.shape[0]
    ends_at = jnp.cumsum(req_lengths)
    last_ids = ends_at - 1
    picker = (local_rows[None, :] == (last_ids - block_base)[:, None]).astype(jnp.bfloat16)
    query_last = jnp.dot(picker, query_proj, preferred_element_type=jnp.float32)
    seq_last = jnp.dot(picker, seq_in, preferred_element_type=jnp.float32)
    extras = jnp.concatenate([query_last, seq_last], axis=1).astype(jnp.bfloat16).reshape(-1)
    kv_width = key_rows.shape[1]
    ship_width = 2 * kv_width
    extra_rows = -(-extras.shape[0] // ship_width)
    extras = jnp.pad(extras, (0, extra_rows * ship_width - extras.shape[0]))
    shipped = jnp.concatenate([key_rows, value_rows], axis=1)
    shipped = jnp.concatenate([shipped, extras.reshape(extra_rows, ship_width)], axis=0)
    gathered = lax.all_gather(shipped, "blk", axis=0, tiled=False)
    gathered, weight_pieces = lax.optimization_barrier((gathered, weight_pieces))
    blocks = gathered.shape[0]
    q_cols = query_proj.shape[1]
    extras_all = gathered[:, tok_rows:].reshape(blocks, -1)[:, : reqs * (q_cols + feat_dev)]
    extras_all = jnp.sum(extras_all.astype(jnp.float32).reshape(blocks, reqs, -1), axis=0)
    query_last = extras_all[:, :q_cols].astype(jnp.bfloat16)
    seq_last = extras_all[:, q_cols:]
    block_index = lax.axis_index("blk")
    first_begin = query_begin[0]
    block_ids = jnp.arange(blocks, dtype=jnp.int32)
    needed = (
        (block_ids <= block_index) & (block_ids * tok_rows + tok_rows - 1 >= first_begin)
    ).astype(jnp.int32)
    group_rows = tok_rows * per_group
    grouped_q = jnp.transpose(
        query_proj.reshape(tok_rows, kv_heads, per_group, HD), (1, 0, 2, 3)
    ).reshape(kv_heads, group_rows, HD)
    q_ids = jnp.repeat(row_ids, per_group)[:, None]
    q_req = jnp.repeat(query_req, per_group)[:, None]
    all_ids = jnp.arange(blocks * tok_rows, dtype=jnp.int32)
    all_req, unused = request_info(all_ids, req_lengths)
    k_ids = all_ids.reshape(blocks, 1, tok_rows)
    k_req = all_req.reshape(blocks, 1, tok_rows)
    context = flash_attention(
        needed, grouped_q, gathered, q_ids, q_req, k_ids, k_req, kv_heads, tok_rows, root
    )
    context = jnp.transpose(
        context.reshape(kv_heads, tok_rows, per_group, HD), (1, 0, 2, 3)
    ).reshape(tok_rows, kv_heads * per_group * HD)
    all_ids = jnp.arange(blocks * tok_rows, dtype=jnp.int32)
    last_begin = ends_at - req_lengths
    last_allowed = (all_ids[None, :] >= last_begin[:, None]) & (all_ids[None, :] <= last_ids[:, None])
    last_allowed = last_allowed[:, None, :]
    last_parts = []
    for g in range(kv_heads):
        keys_g = gathered[:, :tok_rows, g * HD : (g + 1) * HD].reshape(blocks * tok_rows, HD)
        values_g = gathered[:, :tok_rows, kv_width + g * HD : kv_width + (g + 1) * HD].reshape(
            blocks * tok_rows, HD
        )
        last_q = query_last[:, g * per_group * HD : (g + 1) * per_group * HD].reshape(
            reqs, per_group, HD
        )
        last_scores = (
            jnp.einsum("tqd,kd->tqk", last_q, keys_g, preferred_element_type=jnp.float32) / root
        )
        last_scores = jnp.where(last_allowed, last_scores, -1e30)
        last_max = jnp.max(last_scores, axis=-1)
        last_weights = jnp.where(last_allowed, jnp.exp(last_scores - last_max[..., None]), 0.0)
        last_sum = jnp.sum(last_weights, axis=-1)
        last_mix = jnp.einsum(
            "tqk,kd->tqd",
            last_weights.astype(jnp.bfloat16),
            values_g,
            preferred_element_type=jnp.float32,
        )
        last_parts.append((last_mix / last_sum[..., None]).reshape(reqs, per_group * HD))
    last_context = jnp.concatenate(last_parts, axis=1).astype(jnp.bfloat16)
    out_rows = jnp.concatenate([context, last_context], axis=0)
    context_all = kv_exchange(out_rows, kv_count, paired)
    head_sum = None
    for shift, piece in enumerate(weight_pieces):
        source = lax.dynamic_index_in_dim(
            context_all, (me_kv - shift) % kv_count, 0, keepdims=False
        )
        part = jnp.dot(source, piece, preferred_element_type=jnp.float32)
        part = part.astype(jnp.bfloat16).astype(jnp.float32)
        head_sum = part if head_sum is None else head_sum + part
    hidden = (seq_in.astype(jnp.float32) + head_sum[:tok_rows]).astype(jnp.bfloat16)
    chosen = (seq_last + head_sum[tok_rows:]).astype(jnp.bfloat16).astype(jnp.float32)
    square_part = jnp.sum(chosen * chosen, axis=-1)
    scaled = (chosen * final_gain).astype(jnp.bfloat16)
    logit_part = lax.dot_general(
        scaled, table, (((1,), (1,)), ((), ())), preferred_element_type=jnp.float32
    )
    packed_sums = ordered_sum(
        permute_pieces(jnp.concatenate([logit_part, square_part[:, None]], axis=1), kv_count),
        kv_count,
    )
    logit_sum = packed_sums[:, :-1]
    square_sum = packed_sums[:, -1]
    inv_rms = lax.rsqrt(square_sum / D + 1e-05)
    last_norm = (chosen * inv_rms[:, None] * final_gain).astype(jnp.bfloat16)
    local_max = jnp.max(inv_rms[:, None] * logit_sum, axis=-1)
    max_logit = tree_max(local_max, "blk", blocks)
    return (hidden, last_norm, max_logit)


def solution(mesh):
    placed = (
        P("blk", None, None),
        P("blk", None),
        P("blk"),
        P(),
        P(None, None, "kv"),
        P("kv", None),
        P(None, "kv"),
        P("blk", "kv"),
        P(),
        P(None, "kv"),
        P(None, None, "kv"),
        P("kv", None),
        P(),
        P("kv"),
        P("blk", "kv"),
    )
    devices = mesh.devices
    kv_size = devices.shape[0]
    paired = kv_size % 2 == 0 and all(
        getattr(devices[2 * a, 0], "coords", None) == getattr(devices[2 * a + 1, 0], "coords", None)
        for a in range(kv_size // 2)
    )
    return jax.shard_map(
        functools.partial(on_device, bool(paired)),
        mesh=mesh,
        in_specs=placed,
        out_specs=(P("blk", "kv"), P(None, "kv"), P()),
        check_vma=False,
    )
```

```python
import functools
import math

import jax
import jax.numpy as jnp
from jax import lax
from jax.experimental import pallas as pl
from jax.experimental.pallas import tpu as pltpu
from jax.sharding import PartitionSpec as P

VHD = 88
D = 4096
QHEADS = 16
KVHEADS = 8
HD = 128


def layer_norm(inputs, gain):
    centre = jnp.mean(inputs, axis=-1, keepdims=True)
    centred = inputs - centre
    spread = jnp.mean(centred * centred, axis=-1, keepdims=True)
    return centred * lax.rsqrt(spread + 1e-06) * gain


def rotate(inputs, position):
    half_width = inputs.shape[-1] // 2
    inverse = 500000.0 ** (-jnp.arange(half_width, dtype=jnp.float32) * 2.0 / inputs.shape[-1])
    angles = position.astype(jnp.float32)[:, None] * inverse[None, :]
    cosine = jnp.cos(angles)[:, None, :]
    sine = jnp.sin(angles)[:, None, :]
    first = inputs[..., :half_width]
    second = inputs[..., half_width:]
    return jnp.concatenate(
        [first * cosine - second * sine, second * cosine + first * sine], axis=-1
    )


def request_info(row_index, req_lengths):
    ends_at = jnp.cumsum(req_lengths)
    starts_at = ends_at - req_lengths
    request_id = jnp.sum((row_index[:, None] >= ends_at[None, :]).astype(jnp.int32), axis=1)
    choose = request_id[:, None] == jnp.arange(req_lengths.shape[0], dtype=jnp.int32)[None, :]
    request_begin = jnp.sum(jnp.where(choose, starts_at[None, :], 0), axis=1)
    return (request_id, request_begin)


def flash_kernel(needed_ref, q_ref, k_ref, v_ref, qid_ref, qreq_ref, kid_ref, kreq_ref, o_ref,
                 max_ref, sum_ref, acc_ref, *, root):
    kb = pl.program_id(1)

    @pl.when(kb == 0)
    def _():
        max_ref[...] = jnp.full(max_ref.shape, -1e30, jnp.float32)
        sum_ref[...] = jnp.zeros(sum_ref.shape, jnp.float32)
        acc_ref[...] = jnp.zeros(acc_ref.shape, jnp.float32)

    @pl.when(needed_ref[kb] != 0)
    def _():
        scores = lax.dot_general(
            q_ref[...], k_ref[...], (((1,), (1,)), ((), ())), preferred_element_type=jnp.float32
        ) / root
        allowed = (kid_ref[...] <= qid_ref[...]) & (kreq_ref[...] == qreq_ref[...])
        scores = jnp.where(allowed, scores, -1e30)
        old_max = max_ref[...]
        new_max = jnp.maximum(old_max, jnp.max(scores, axis=1, keepdims=True))
        weights = jnp.where(allowed, jnp.exp(scores - new_max), 0.0)
        scale = jnp.exp(old_max - new_max)
        sum_ref[...] = sum_ref[...] * scale + jnp.sum(weights, axis=1, keepdims=True)
        acc_ref[...] = acc_ref[...] * scale + jnp.dot(
            weights.astype(jnp.bfloat16), v_ref[...], preferred_element_type=jnp.float32
        )
        max_ref[...] = new_max

    @pl.when(kb == pl.num_programs(1) - 1)
    def _():
        rows = o_ref.shape[0]
        for head in range(o_ref.shape[1] // HD):
            part = slice(head * rows, (head + 1) * rows)
            o_ref[:, head * HD : (head + 1) * HD] = (acc_ref[part, :] / sum_ref[part, :]).astype(
                o_ref.dtype
            )


def flash_attention(needed, grouped_q, gathered, q_ids, q_req, k_ids, k_req, groups, tok_rows, root):
    blocks = gathered.shape[0]
    group_rows = grouped_q.shape[1]
    grid_spec = pltpu.PrefetchScalarGridSpec(
        num_scalar_prefetch=1,
        grid=(groups, blocks),
        in_specs=[
            pl.BlockSpec((None, group_rows, HD), lambda g, kb, n: (g, 0, 0)),
            pl.BlockSpec((None, tok_rows, HD), lambda g, kb, n: (kb, 0, g)),
            pl.BlockSpec((None, tok_rows, HD), lambda g, kb, n: (kb, 0, groups + g)),
            pl.BlockSpec((group_rows, 1), lambda g, kb, n: (0, 0)),
            pl.BlockSpec((group_rows, 1), lambda g, kb, n: (0, 0)),
            pl.BlockSpec((None, 1, tok_rows), lambda g, kb, n: (kb, 0, 0)),
            pl.BlockSpec((None, 1, tok_rows), lambda g, kb, n: (kb, 0, 0)),
        ],
        out_specs=pl.BlockSpec((tok_rows, group_rows // tok_rows * HD), lambda g, kb, n: (0, g)),
        scratch_shapes=[
            pltpu.VMEM((group_rows, 1), jnp.float32),
            pltpu.VMEM((group_rows, 1), jnp.float32),
            pltpu.VMEM((group_rows, HD), jnp.float32),
        ],
    )
    flops = 4 * groups * blocks * group_rows * tok_rows * HD
    return pl.pallas_call(
        functools.partial(flash_kernel, root=root),
        grid_spec=grid_spec,
        out_shape=jax.ShapeDtypeStruct((tok_rows, groups * group_rows // tok_rows * HD), jnp.bfloat16),
        compiler_params=pltpu.CompilerParams(dimension_semantics=("arbitrary", "arbitrary")),
        cost_estimate=pl.CostEstimate(
            flops=flops,
            transcendentals=groups * blocks * group_rows * tok_rows,
            bytes_accessed=2 * groups * blocks * tok_rows * HD * 2 + 4 * groups * group_rows * HD,
        ),
    )(needed, grouped_q, gathered, gathered, q_ids, q_req, k_ids, k_req)


def gather_by_permutes(local, count):
    me = lax.axis_index("kv")
    pieces = [local]
    for shift in range(1, count):
        pieces.append(
            lax.ppermute(local, "kv", perm=[(i, (i + shift) % count) for i in range(count)])
        )
    stacked = jnp.stack(pieces)
    order = (me - jnp.arange(count, dtype=jnp.int32)) % count
    ordered = jnp.take(stacked, order, axis=0)
    return jnp.concatenate([ordered[j] for j in range(count)], axis=1)


def permute_pieces(local, count):
    pieces = [local]
    for shift in range(1, count):
        pieces.append(
            lax.ppermute(local, "kv", perm=[(i, (i + shift) % count) for i in range(count)])
        )
    return pieces


def ordered_sum(pieces, count):
    me = lax.axis_index("kv")
    stacked = jnp.stack([piece.astype(jnp.float32) for piece in pieces])
    order = (me - jnp.arange(count, dtype=jnp.int32)) % count
    return jnp.sum(jnp.take(stacked, order, axis=0), axis=0)


def tree_max(values, axis, count):
    if count & (count - 1):
        return lax.pmax(values, axis)
    step = 1
    while step < count:
        other = lax.ppermute(values, axis, perm=[(i, i ^ step) for i in range(count)])
        values = jnp.maximum(values, other)
        step *= 2
    return values


def on_device(
    patches,
    merged_grid,
    picture_start,
    vis_gain,
    vis_qkv,
    vis_out,
    merge_weight,
    text_embed,
    dec_gain,
    w_query,
    w_keyval,
    w_out,
    req_lengths,
    final_gain,
    table,
):
    pictures, patch_max, vis_width = patches.shape
    merged_max = patch_max // 4
    vis_cols = vis_qkv.shape[2]
    vis_heads = vis_cols // VHD
    tok_rows, feat_dev = text_embed.shape
    kv_count = D // text_embed.shape[1]
    text_rows = gather_by_permutes(text_embed, kv_count)
    inputs = patches.astype(jnp.float32)
    normed = layer_norm(inputs, vis_gain).astype(jnp.bfloat16)
    packed = jnp.einsum(
        "pnd,dce->pnce", normed, vis_qkv, preferred_element_type=jnp.float32
    ).astype(jnp.bfloat16)
    packed = packed.reshape(pictures, patch_max, 3, vis_heads, VHD)
    scores = jnp.einsum(
        "pqhd,pkhd->phqk", packed[:, :, 0], packed[:, :, 1], preferred_element_type=jnp.float32
    ) / math.sqrt(VHD)
    cell_count = merged_grid[:, 0] * merged_grid[:, 1]
    valid_cols = jnp.arange(patch_max, dtype=jnp.int32)[None, :] < 4 * cell_count[:, None]
    scores = jnp.where(valid_cols[:, None, None, :], scores, -1e30)
    weights = jnp.exp(scores - jnp.max(scores, axis=-1, keepdims=True))
    weight_sum = jnp.sum(weights, axis=-1)
    mixed_rows = jnp.einsum(
        "phqk,pkhd->pqhd",
        weights.astype(jnp.bfloat16),
        packed[:, :, 2],
        preferred_element_type=jnp.float32,
    )
    mixed_rows = (
        (mixed_rows / jnp.transpose(weight_sum, (0, 2, 1))[..., None])
        .astype(jnp.bfloat16)
        .reshape(pictures, patch_max, vis_cols)
    )
    head_part = jnp.einsum("pnc,cd->pnd", mixed_rows, vis_out, preferred_element_type=jnp.float32)
    head_pooled = jnp.mean(head_part.reshape(pictures, merged_max, 4, vis_width), axis=2)
    head_total = lax.psum(head_pooled.astype(jnp.bfloat16), "kv").astype(jnp.float32)
    input_pooled = jnp.mean(inputs.reshape(pictures, merged_max, 4, vis_width), axis=2)
    pooled = (input_pooled + head_total).astype(jnp.bfloat16)
    merged = jnp.einsum(
        "pmd,de->pme", pooled, merge_weight, preferred_element_type=jnp.float32
    ).astype(jnp.bfloat16)
    me_kv = lax.axis_index("kv")
    out_source, merged = lax.optimization_barrier((w_out, merged))
    weight_pieces = [lax.dynamic_slice_in_dim(out_source, me_kv * feat_dev, feat_dev, 1)]
    for shift in range(1, kv_count):
        payload = lax.dynamic_slice_in_dim(
            out_source, ((me_kv + shift) % kv_count) * feat_dev, feat_dev, 1
        )
        weight_pieces.append(
            lax.ppermute(
                payload, "kv", perm=[(i, (i + shift) % kv_count) for i in range(kv_count)]
            )
        )
    block_base = lax.axis_index("blk") * tok_rows
    slot_index = jnp.arange(merged_max, dtype=jnp.int32)
    target = picture_start[:, None] + slot_index[None, :] - block_base
    target = jnp.where(slot_index[None, :] < cell_count[:, None], target, -1).reshape(-1)
    local_rows = jnp.arange(tok_rows, dtype=jnp.int32)
    one_hot = local_rows[:, None] == target[None, :]
    placed = jnp.dot(
        one_hot.astype(jnp.bfloat16),
        merged.reshape(pictures * merged_max, feat_dev),
        preferred_element_type=jnp.float32,
    )
    is_vision = jnp.any(one_hot, axis=1)
    seq_in = jnp.where(is_vision[:, None], placed.astype(jnp.bfloat16), text_embed)
    merged_rows = lax.all_gather(
        merged.reshape(pictures * merged_max, feat_dev), "kv", axis=1, tiled=True
    )
    placed_rows = jnp.dot(one_hot.astype(jnp.bfloat16), merged_rows, preferred_element_type=jnp.float32)
    full_rows = jnp.where(is_vision[:, None], placed_rows.astype(jnp.bfloat16), text_rows)
    full_float = full_rows.astype(jnp.float32)
    dec_normed = (
        full_float
        * lax.rsqrt(jnp.mean(full_float * full_float, axis=-1, keepdims=True) + 1e-05)
        * dec_gain
    ).astype(jnp.bfloat16)
    per_group = QHEADS // KVHEADS
    kv_heads = w_keyval.shape[2] // HD
    row_ids = block_base + local_rows
    request_id, request_begin = request_info(row_ids, req_lengths)
    position = row_ids - request_begin
    query_proj = jnp.dot(dec_normed, w_query, preferred_element_type=jnp.float32).reshape(
        tok_rows, kv_heads * per_group, HD
    )
    query_proj = (
        rotate(query_proj, position)
        .astype(jnp.bfloat16)
        .reshape(tok_rows, kv_heads * per_group * HD)
    )
    key_value = jnp.einsum("td,dce->tce", dec_normed, w_keyval, preferred_element_type=jnp.float32)
    key_rows = (
        rotate(key_value[:, 0].reshape(tok_rows, kv_heads, HD), position)
        .astype(jnp.bfloat16)
        .reshape(tok_rows, kv_heads * HD)
    )
    value_rows = key_value[:, 1].astype(jnp.bfloat16)
    query_req, query_begin = request_info(row_ids, req_lengths)
    root = math.sqrt(HD)
    reqs = req_lengths.shape[0]
    ends_at = jnp.cumsum(req_lengths)
    last_ids = ends_at - 1
    picker = (local_rows[None, :] == (last_ids - block_base)[:, None]).astype(jnp.bfloat16)
    query_last = jnp.dot(picker, query_proj, preferred_element_type=jnp.float32)
    seq_last = jnp.dot(picker, seq_in, preferred_element_type=jnp.float32)
    extras = jnp.concatenate([query_last, seq_last], axis=1).astype(jnp.bfloat16).reshape(-1)
    kv_width = key_rows.shape[1]
    ship_width = 2 * kv_width
    extra_rows = -(-extras.shape[0] // ship_width)
    extras = jnp.pad(extras, (0, extra_rows * ship_width - extras.shape[0]))
    shipped = jnp.concatenate([key_rows, value_rows], axis=1)
    shipped = jnp.concatenate([shipped, extras.reshape(extra_rows, ship_width)], axis=0)
    gathered = lax.all_gather(shipped, "blk", axis=0, tiled=False)
    gathered, weight_pieces = lax.optimization_barrier((gathered, weight_pieces))
    blocks = gathered.shape[0]
    q_cols = query_proj.shape[1]
    extras_all = gathered[:, tok_rows:].reshape(blocks, -1)[:, : reqs * (q_cols + feat_dev)]
    extras_all = jnp.sum(extras_all.astype(jnp.float32).reshape(blocks, reqs, -1), axis=0)
    query_last = extras_all[:, :q_cols].astype(jnp.bfloat16)
    seq_last = extras_all[:, q_cols:]
    block_index = lax.axis_index("blk")
    first_begin = query_begin[0]
    block_ids = jnp.arange(blocks, dtype=jnp.int32)
    needed = (
        (block_ids <= block_index) & (block_ids * tok_rows + tok_rows - 1 >= first_begin)
    ).astype(jnp.int32)
    group_rows = tok_rows * per_group
    grouped_q = jnp.transpose(
        query_proj.reshape(tok_rows, kv_heads, per_group, HD), (1, 2, 0, 3)
    ).reshape(kv_heads, group_rows, HD)
    q_ids = jnp.tile(row_ids, per_group)[:, None]
    q_req = jnp.tile(query_req, per_group)[:, None]
    all_ids = jnp.arange(blocks * tok_rows, dtype=jnp.int32)
    all_req, unused = request_info(all_ids, req_lengths)
    k_ids = all_ids.reshape(blocks, 1, tok_rows)
    k_req = all_req.reshape(blocks, 1, tok_rows)
    context = flash_attention(
        needed, grouped_q, gathered, q_ids, q_req, k_ids, k_req, kv_heads, tok_rows, root
    )
    all_ids = jnp.arange(blocks * tok_rows, dtype=jnp.int32)
    last_begin = ends_at - req_lengths
    last_allowed = (all_ids[None, :] >= last_begin[:, None]) & (all_ids[None, :] <= last_ids[:, None])
    last_allowed = last_allowed[:, None, :]
    last_parts = []
    for g in range(kv_heads):
        keys_g = gathered[:, :tok_rows, g * HD : (g + 1) * HD].reshape(blocks * tok_rows, HD)
        values_g = gathered[:, :tok_rows, kv_width + g * HD : kv_width + (g + 1) * HD].reshape(
            blocks * tok_rows, HD
        )
        last_q = query_last[:, g * per_group * HD : (g + 1) * per_group * HD].reshape(
            reqs, per_group, HD
        )
        last_scores = (
            jnp.einsum("tqd,kd->tqk", last_q, keys_g, preferred_element_type=jnp.float32) / root
        )
        last_scores = jnp.where(last_allowed, last_scores, -1e30)
        last_max = jnp.max(last_scores, axis=-1)
        last_weights = jnp.where(last_allowed, jnp.exp(last_scores - last_max[..., None]), 0.0)
        last_sum = jnp.sum(last_weights, axis=-1)
        last_mix = jnp.einsum(
            "tqk,kd->tqd",
            last_weights.astype(jnp.bfloat16),
            values_g,
            preferred_element_type=jnp.float32,
        )
        last_parts.append((last_mix / last_sum[..., None]).reshape(reqs, per_group * HD))
    last_context = jnp.concatenate(last_parts, axis=1).astype(jnp.bfloat16)
    out_rows = jnp.concatenate([context, last_context], axis=0)
    context_all = lax.all_gather(out_rows, "kv", axis=0, tiled=False)
    head_sum = None
    for shift, piece in enumerate(weight_pieces):
        source = lax.dynamic_index_in_dim(
            context_all, (me_kv - shift) % kv_count, 0, keepdims=False
        )
        part = jnp.dot(source, piece, preferred_element_type=jnp.float32)
        part = part.astype(jnp.bfloat16).astype(jnp.float32)
        head_sum = part if head_sum is None else head_sum + part
    hidden = (seq_in.astype(jnp.float32) + head_sum[:tok_rows]).astype(jnp.bfloat16)
    chosen = (seq_last + head_sum[tok_rows:]).astype(jnp.bfloat16).astype(jnp.float32)
    square_part = jnp.sum(chosen * chosen, axis=-1)
    scaled = (chosen * final_gain).astype(jnp.bfloat16)
    logit_part = lax.dot_general(
        scaled, table, (((1,), (1,)), ((), ())), preferred_element_type=jnp.float32
    )
    packed_sums = ordered_sum(
        permute_pieces(jnp.concatenate([logit_part, square_part[:, None]], axis=1), kv_count),
        kv_count,
    )
    logit_sum = packed_sums[:, :-1]
    square_sum = packed_sums[:, -1]
    inv_rms = lax.rsqrt(square_sum / D + 1e-05)
    last_norm = (chosen * inv_rms[:, None] * final_gain).astype(jnp.bfloat16)
    local_max = jnp.max(inv_rms[:, None] * logit_sum, axis=-1)
    max_logit = tree_max(local_max, "blk", blocks)
    return (hidden, last_norm, max_logit)


def solution(mesh):
    placed = (
        P("blk", None, None),
        P("blk", None),
        P("blk"),
        P(),
        P(None, None, "kv"),
        P("kv", None),
        P(None, "kv"),
        P("blk", "kv"),
        P(),
        P(None, "kv"),
        P(None, None, "kv"),
        P("kv", None),
        P(),
        P("kv"),
        P("blk", "kv"),
    )
    return jax.shard_map(
        on_device,
        mesh=mesh,
        in_specs=placed,
        out_specs=(P("blk", "kv"), P(None, "kv"), P()),
        check_vma=False,
    )
```

```python
import functools
import math

import jax
import jax.numpy as jnp
from jax import lax
from jax.experimental import pallas as pl
from jax.experimental.pallas import tpu as pltpu
from jax.sharding import PartitionSpec as P

VHD = 88
D = 4096
QHEADS = 16
KVHEADS = 8
HD = 128


def layer_norm(inputs, gain):
    centre = jnp.mean(inputs, axis=-1, keepdims=True)
    centred = inputs - centre
    spread = jnp.mean(centred * centred, axis=-1, keepdims=True)
    return centred * lax.rsqrt(spread + 1e-06) * gain


def rotate(inputs, position):
    half_width = inputs.shape[-1] // 2
    inverse = 500000.0 ** (-jnp.arange(half_width, dtype=jnp.float32) * 2.0 / inputs.shape[-1])
    angles = position.astype(jnp.float32)[:, None] * inverse[None, :]
    cosine = jnp.cos(angles)[:, None, :]
    sine = jnp.sin(angles)[:, None, :]
    first = inputs[..., :half_width]
    second = inputs[..., half_width:]
    return jnp.concatenate(
        [first * cosine - second * sine, second * cosine + first * sine], axis=-1
    )


def request_info(row_index, req_lengths):
    ends_at = jnp.cumsum(req_lengths)
    starts_at = ends_at - req_lengths
    request_id = jnp.sum((row_index[:, None] >= ends_at[None, :]).astype(jnp.int32), axis=1)
    choose = request_id[:, None] == jnp.arange(req_lengths.shape[0], dtype=jnp.int32)[None, :]
    request_begin = jnp.sum(jnp.where(choose, starts_at[None, :], 0), axis=1)
    return (request_id, request_begin)


def flash_kernel(needed_ref, q_ref, k_ref, v_ref, qid_ref, qreq_ref, kid_ref, kreq_ref,
                 max_in, sum_in, acc_in, o_ref, max_out, sum_out, acc_out,
                 max_ref, sum_ref, acc_ref, *, root):
    kb = pl.program_id(1)

    @pl.when(kb == 0)
    def _():
        max_ref[...] = max_in[...]
        sum_ref[...] = sum_in[...]
        acc_ref[...] = acc_in[...]

    @pl.when(needed_ref[kb] != 0)
    def _():
        scores = lax.dot_general(
            q_ref[...], k_ref[...], (((1,), (1,)), ((), ())), preferred_element_type=jnp.float32
        ) / root
        allowed = (kid_ref[...] <= qid_ref[...]) & (kreq_ref[...] == qreq_ref[...])
        scores = jnp.where(allowed, scores, -1e30)
        old_max = max_ref[...]
        new_max = jnp.maximum(old_max, jnp.max(scores, axis=1, keepdims=True))
        weights = jnp.where(allowed, jnp.exp(scores - new_max), 0.0)
        scale = jnp.exp(old_max - new_max)
        sum_ref[...] = sum_ref[...] * scale + jnp.sum(weights, axis=1, keepdims=True)
        acc_ref[...] = acc_ref[...] * scale + jnp.dot(
            weights.astype(jnp.bfloat16), v_ref[...], preferred_element_type=jnp.float32
        )
        max_ref[...] = new_max

    @pl.when(kb == pl.num_programs(1) - 1)
    def _():
        max_out[...] = max_ref[...]
        sum_out[...] = sum_ref[...]
        acc_out[...] = acc_ref[...]
        rows = o_ref.shape[0]
        for head in range(o_ref.shape[1] // HD):
            part = slice(head * rows, (head + 1) * rows)
            o_ref[:, head * HD : (head + 1) * HD] = (acc_ref[part, :] / sum_ref[part, :]).astype(
                o_ref.dtype
            )


def flash_attention(needed, grouped_q, gathered, q_ids, q_req, k_ids, k_req, groups, tok_rows, root,
                    state, key_rows):
    blocks = gathered.shape[0]
    group_rows = grouped_q.shape[1]
    state_spec = pl.BlockSpec((None, group_rows, 1), lambda g, kb, n: (g, 0, 0))
    acc_spec = pl.BlockSpec((None, group_rows, HD), lambda g, kb, n: (g, 0, 0))
    grid_spec = pltpu.PrefetchScalarGridSpec(
        num_scalar_prefetch=1,
        grid=(groups, blocks),
        in_specs=[
            pl.BlockSpec((None, group_rows, HD), lambda g, kb, n: (g, 0, 0)),
            pl.BlockSpec((None, key_rows, HD), lambda g, kb, n: (kb, 0, g)),
            pl.BlockSpec((None, key_rows, HD), lambda g, kb, n: (kb, 0, groups + g)),
            pl.BlockSpec((group_rows, 1), lambda g, kb, n: (0, 0)),
            pl.BlockSpec((group_rows, 1), lambda g, kb, n: (0, 0)),
            pl.BlockSpec((None, 1, key_rows), lambda g, kb, n: (kb, 0, 0)),
            pl.BlockSpec((None, 1, key_rows), lambda g, kb, n: (kb, 0, 0)),
            state_spec,
            state_spec,
            acc_spec,
        ],
        out_specs=[
            pl.BlockSpec((tok_rows, group_rows // tok_rows * HD), lambda g, kb, n: (0, g)),
            state_spec,
            state_spec,
            acc_spec,
        ],
        scratch_shapes=[
            pltpu.VMEM((group_rows, 1), jnp.float32),
            pltpu.VMEM((group_rows, 1), jnp.float32),
            pltpu.VMEM((group_rows, HD), jnp.float32),
        ],
    )
    flops = 4 * groups * blocks * group_rows * key_rows * HD
    return pl.pallas_call(
        functools.partial(flash_kernel, root=root),
        grid_spec=grid_spec,
        out_shape=[
            jax.ShapeDtypeStruct((tok_rows, groups * group_rows // tok_rows * HD), jnp.bfloat16),
            jax.ShapeDtypeStruct((groups, group_rows, 1), jnp.float32),
            jax.ShapeDtypeStruct((groups, group_rows, 1), jnp.float32),
            jax.ShapeDtypeStruct((groups, group_rows, HD), jnp.float32),
        ],
        compiler_params=pltpu.CompilerParams(dimension_semantics=("arbitrary", "arbitrary")),
        cost_estimate=pl.CostEstimate(
            flops=flops,
            transcendentals=groups * blocks * group_rows * key_rows,
            bytes_accessed=2 * groups * blocks * key_rows * HD * 2 + 12 * groups * group_rows * HD,
        ),
    )(needed, grouped_q, gathered, gathered, q_ids, q_req, k_ids, k_req, *state)


def gather_by_permutes(local, count):
    me = lax.axis_index("kv")
    pieces = [local]
    for shift in range(1, count):
        pieces.append(
            lax.ppermute(local, "kv", perm=[(i, (i + shift) % count) for i in range(count)])
        )
    stacked = jnp.stack(pieces)
    order = (me - jnp.arange(count, dtype=jnp.int32)) % count
    ordered = jnp.take(stacked, order, axis=0)
    return jnp.concatenate([ordered[j] for j in range(count)], axis=1)


def permute_pieces(local, count):
    pieces = [local]
    for shift in range(1, count):
        pieces.append(
            lax.ppermute(local, "kv", perm=[(i, (i + shift) % count) for i in range(count)])
        )
    return pieces


def ordered_sum(pieces, count):
    me = lax.axis_index("kv")
    stacked = jnp.stack([piece.astype(jnp.float32) for piece in pieces])
    order = (me - jnp.arange(count, dtype=jnp.int32)) % count
    return jnp.sum(jnp.take(stacked, order, axis=0), axis=0)


def tree_max(values, axis, count):
    if count & (count - 1):
        return lax.pmax(values, axis)
    step = 1
    while step < count:
        other = lax.ppermute(values, axis, perm=[(i, i ^ step) for i in range(count)])
        values = jnp.maximum(values, other)
        step *= 2
    return values


def on_device(
    patches,
    merged_grid,
    picture_start,
    vis_gain,
    vis_qkv,
    vis_out,
    merge_weight,
    text_embed,
    dec_gain,
    w_query,
    w_keyval,
    w_out,
    req_lengths,
    final_gain,
    table,
):
    pictures, patch_max, vis_width = patches.shape
    merged_max = patch_max // 4
    vis_cols = vis_qkv.shape[2]
    vis_heads = vis_cols // VHD
    tok_rows, feat_dev = text_embed.shape
    kv_count = D // text_embed.shape[1]
    text_rows = gather_by_permutes(text_embed, kv_count)
    inputs = patches.astype(jnp.float32)
    normed = layer_norm(inputs, vis_gain).astype(jnp.bfloat16)
    packed = jnp.einsum(
        "pnd,dce->pnce", normed, vis_qkv, preferred_element_type=jnp.float32
    ).astype(jnp.bfloat16)
    packed = packed.reshape(pictures, patch_max, 3, vis_heads, VHD)
    scores = jnp.einsum(
        "pqhd,pkhd->phqk", packed[:, :, 0], packed[:, :, 1], preferred_element_type=jnp.float32
    ) / math.sqrt(VHD)
    cell_count = merged_grid[:, 0] * merged_grid[:, 1]
    valid_cols = jnp.arange(patch_max, dtype=jnp.int32)[None, :] < 4 * cell_count[:, None]
    scores = jnp.where(valid_cols[:, None, None, :], scores, -1e30)
    weights = jnp.exp(scores - jnp.max(scores, axis=-1, keepdims=True))
    weight_sum = jnp.sum(weights, axis=-1)
    mixed_rows = jnp.einsum(
        "phqk,pkhd->pqhd",
        weights.astype(jnp.bfloat16),
        packed[:, :, 2],
        preferred_element_type=jnp.float32,
    )
    mixed_rows = (
        (mixed_rows / jnp.transpose(weight_sum, (0, 2, 1))[..., None])
        .astype(jnp.bfloat16)
        .reshape(pictures, patch_max, vis_cols)
    )
    head_part = jnp.einsum("pnc,cd->pnd", mixed_rows, vis_out, preferred_element_type=jnp.float32)
    head_pooled = jnp.mean(head_part.reshape(pictures, merged_max, 4, vis_width), axis=2)
    head_total = lax.psum(head_pooled.astype(jnp.bfloat16), "kv").astype(jnp.float32)
    input_pooled = jnp.mean(inputs.reshape(pictures, merged_max, 4, vis_width), axis=2)
    pooled = (input_pooled + head_total).astype(jnp.bfloat16)
    merged = jnp.einsum(
        "pmd,de->pme", pooled, merge_weight, preferred_element_type=jnp.float32
    ).astype(jnp.bfloat16)
    me_kv = lax.axis_index("kv")
    out_source, merged = lax.optimization_barrier((w_out, merged))
    weight_pieces = [lax.dynamic_slice_in_dim(out_source, me_kv * feat_dev, feat_dev, 1)]
    for shift in range(1, kv_count):
        payload = lax.dynamic_slice_in_dim(
            out_source, ((me_kv + shift) % kv_count) * feat_dev, feat_dev, 1
        )
        weight_pieces.append(
            lax.ppermute(
                payload, "kv", perm=[(i, (i + shift) % kv_count) for i in range(kv_count)]
            )
        )
    block_base = lax.axis_index("blk") * tok_rows
    slot_index = jnp.arange(merged_max, dtype=jnp.int32)
    target = picture_start[:, None] + slot_index[None, :] - block_base
    target = jnp.where(slot_index[None, :] < cell_count[:, None], target, -1).reshape(-1)
    local_rows = jnp.arange(tok_rows, dtype=jnp.int32)
    one_hot = local_rows[:, None] == target[None, :]
    placed = jnp.dot(
        one_hot.astype(jnp.bfloat16),
        merged.reshape(pictures * merged_max, feat_dev),
        preferred_element_type=jnp.float32,
    )
    is_vision = jnp.any(one_hot, axis=1)
    seq_in = jnp.where(is_vision[:, None], placed.astype(jnp.bfloat16), text_embed)
    merged_rows = lax.all_gather(
        merged.reshape(pictures * merged_max, feat_dev), "kv", axis=1, tiled=True
    )
    placed_rows = jnp.dot(one_hot.astype(jnp.bfloat16), merged_rows, preferred_element_type=jnp.float32)
    full_rows = jnp.where(is_vision[:, None], placed_rows.astype(jnp.bfloat16), text_rows)
    full_float = full_rows.astype(jnp.float32)
    dec_normed = (
        full_float
        * lax.rsqrt(jnp.mean(full_float * full_float, axis=-1, keepdims=True) + 1e-05)
        * dec_gain
    ).astype(jnp.bfloat16)
    per_group = QHEADS // KVHEADS
    kv_heads = w_keyval.shape[2] // HD
    row_ids = block_base + local_rows
    request_id, request_begin = request_info(row_ids, req_lengths)
    position = row_ids - request_begin
    query_proj = jnp.dot(dec_normed, w_query, preferred_element_type=jnp.float32).reshape(
        tok_rows, kv_heads * per_group, HD
    )
    query_proj = (
        rotate(query_proj, position)
        .astype(jnp.bfloat16)
        .reshape(tok_rows, kv_heads * per_group * HD)
    )
    key_value = jnp.einsum("td,dce->tce", dec_normed, w_keyval, preferred_element_type=jnp.float32)
    key_rows = (
        rotate(key_value[:, 0].reshape(tok_rows, kv_heads, HD), position)
        .astype(jnp.bfloat16)
        .reshape(tok_rows, kv_heads * HD)
    )
    value_rows = key_value[:, 1].astype(jnp.bfloat16)
    query_req, query_begin = request_info(row_ids, req_lengths)
    root = math.sqrt(HD)
    reqs = req_lengths.shape[0]
    ends_at = jnp.cumsum(req_lengths)
    last_ids = ends_at - 1
    picker = (local_rows[None, :] == (last_ids - block_base)[:, None]).astype(jnp.bfloat16)
    query_last = jnp.dot(picker, query_proj, preferred_element_type=jnp.float32)
    seq_last = jnp.dot(picker, seq_in, preferred_element_type=jnp.float32)
    extras = jnp.concatenate([query_last, seq_last], axis=1).astype(jnp.bfloat16).reshape(-1)
    kv_width = key_rows.shape[1]
    ship_width = 2 * kv_width
    extra_rows = -(-extras.shape[0] // ship_width)
    extras = jnp.pad(extras, (0, extra_rows * ship_width - extras.shape[0]))
    half = tok_rows // 2
    shipped = jnp.concatenate([key_rows, value_rows], axis=1)
    ship_a = jnp.concatenate([shipped[:half], extras.reshape(extra_rows, ship_width)], axis=0)
    ship_b = jnp.pad(shipped[half:], ((0, extra_rows), (0, 0)))
    gathered_a = lax.all_gather(ship_a, "blk", axis=0, tiled=False)
    gathered_b = lax.all_gather(ship_b, "blk", axis=0, tiled=False)
    gathered = gathered_a
    blocks = gathered_a.shape[0]
    q_cols = query_proj.shape[1]
    extras_all = gathered_a[:, half:].reshape(blocks, -1)[:, : reqs * (q_cols + feat_dev)]
    extras_all = jnp.sum(extras_all.astype(jnp.float32).reshape(blocks, reqs, -1), axis=0)
    query_last = extras_all[:, :q_cols].astype(jnp.bfloat16)
    seq_last = extras_all[:, q_cols:]
    block_index = lax.axis_index("blk")
    first_begin = query_begin[0]
    block_ids = jnp.arange(blocks, dtype=jnp.int32)
    needed_a = (
        (block_ids <= block_index) & (block_ids * tok_rows + half - 1 >= first_begin)
    ).astype(jnp.int32)
    needed_b = (
        (block_ids <= block_index) & (block_ids * tok_rows + tok_rows - 1 >= first_begin)
    ).astype(jnp.int32)
    group_rows = tok_rows * per_group
    grouped_q = jnp.transpose(
        query_proj.reshape(tok_rows, kv_heads, per_group, HD), (1, 2, 0, 3)
    ).reshape(kv_heads, group_rows, HD)
    q_ids = jnp.tile(row_ids, per_group)[:, None]
    q_req = jnp.tile(query_req, per_group)[:, None]
    all_ids = jnp.arange(blocks * tok_rows, dtype=jnp.int32)
    all_req, unused = request_info(all_ids, req_lengths)
    k_ids = all_ids.reshape(blocks, 2, 1, half)
    k_req = all_req.reshape(blocks, 2, 1, half)
    start_state = (
        jnp.full((kv_heads, group_rows, 1), -1e30, jnp.float32),
        jnp.zeros((kv_heads, group_rows, 1), jnp.float32),
        jnp.zeros((kv_heads, group_rows, HD), jnp.float32),
    )
    outcome = flash_attention(
        needed_a, grouped_q, gathered_a, q_ids, q_req, k_ids[:, 0], k_req[:, 0], kv_heads,
        tok_rows, root, start_state, half,
    )
    gathered_b, weight_pieces, first_state = lax.optimization_barrier(
        (gathered_b, weight_pieces, tuple(outcome[1:]))
    )
    outcome = flash_attention(
        needed_b, grouped_q, gathered_b, q_ids, q_req, k_ids[:, 1], k_req[:, 1], kv_heads,
        tok_rows, root, first_state, half,
    )
    context = outcome[0]
    gathered = jnp.concatenate([gathered_a[:, :half], gathered_b[:, :half]], axis=1)
    all_ids = jnp.arange(blocks * tok_rows, dtype=jnp.int32)
    last_begin = ends_at - req_lengths
    last_allowed = (all_ids[None, :] >= last_begin[:, None]) & (all_ids[None, :] <= last_ids[:, None])
    last_allowed = last_allowed[:, None, :]
    last_parts = []
    for g in range(kv_heads):
        keys_g = gathered[:, :tok_rows, g * HD : (g + 1) * HD].reshape(blocks * tok_rows, HD)
        values_g = gathered[:, :tok_rows, kv_width + g * HD : kv_width + (g + 1) * HD].reshape(
            blocks * tok_rows, HD
        )
        last_q = query_last[:, g * per_group * HD : (g + 1) * per_group * HD].reshape(
            reqs, per_group, HD
        )
        last_scores = (
            jnp.einsum("tqd,kd->tqk", last_q, keys_g, preferred_element_type=jnp.float32) / root
        )
        last_scores = jnp.where(last_allowed, last_scores, -1e30)
        last_max = jnp.max(last_scores, axis=-1)
        last_weights = jnp.where(last_allowed, jnp.exp(last_scores - last_max[..., None]), 0.0)
        last_sum = jnp.sum(last_weights, axis=-1)
        last_mix = jnp.einsum(
            "tqk,kd->tqd",
            last_weights.astype(jnp.bfloat16),
            values_g,
            preferred_element_type=jnp.float32,
        )
        last_parts.append((last_mix / last_sum[..., None]).reshape(reqs, per_group * HD))
    last_context = jnp.concatenate(last_parts, axis=1).astype(jnp.bfloat16)
    out_rows = jnp.concatenate([context, last_context], axis=0)
    context_all = lax.all_gather(out_rows, "kv", axis=0, tiled=False)
    head_sum = None
    for shift, piece in enumerate(weight_pieces):
        source = lax.dynamic_index_in_dim(
            context_all, (me_kv - shift) % kv_count, 0, keepdims=False
        )
        part = jnp.dot(source, piece, preferred_element_type=jnp.float32)
        part = part.astype(jnp.bfloat16).astype(jnp.float32)
        head_sum = part if head_sum is None else head_sum + part
    hidden = (seq_in.astype(jnp.float32) + head_sum[:tok_rows]).astype(jnp.bfloat16)
    chosen = (seq_last + head_sum[tok_rows:]).astype(jnp.bfloat16).astype(jnp.float32)
    square_part = jnp.sum(chosen * chosen, axis=-1)
    scaled = (chosen * final_gain).astype(jnp.bfloat16)
    logit_part = lax.dot_general(
        scaled, table, (((1,), (1,)), ((), ())), preferred_element_type=jnp.float32
    )
    packed_sums = ordered_sum(
        permute_pieces(jnp.concatenate([logit_part, square_part[:, None]], axis=1), kv_count),
        kv_count,
    )
    logit_sum = packed_sums[:, :-1]
    square_sum = packed_sums[:, -1]
    inv_rms = lax.rsqrt(square_sum / D + 1e-05)
    last_norm = (chosen * inv_rms[:, None] * final_gain).astype(jnp.bfloat16)
    local_max = jnp.max(inv_rms[:, None] * logit_sum, axis=-1)
    max_logit = tree_max(local_max, "blk", blocks)
    return (hidden, last_norm, max_logit)


def solution(mesh):
    placed = (
        P("blk", None, None),
        P("blk", None),
        P("blk"),
        P(),
        P(None, None, "kv"),
        P("kv", None),
        P(None, "kv"),
        P("blk", "kv"),
        P(),
        P(None, "kv"),
        P(None, None, "kv"),
        P("kv", None),
        P(),
        P("kv"),
        P("blk", "kv"),
    )
    return jax.shard_map(
        on_device,
        mesh=mesh,
        in_specs=placed,
        out_specs=(P("blk", "kv"), P(None, "kv"), P()),
        check_vma=False,
    )
```

```python
import functools
import math

import jax
import jax.numpy as jnp
from jax import lax
from jax.experimental import pallas as pl
from jax.experimental.pallas import tpu as pltpu
from jax.sharding import PartitionSpec as P

VHD = 88
D = 4096
QHEADS = 16
KVHEADS = 8
HD = 128


def layer_norm(inputs, gain):
    centre = jnp.mean(inputs, axis=-1, keepdims=True)
    centred = inputs - centre
    spread = jnp.mean(centred * centred, axis=-1, keepdims=True)
    return centred * lax.rsqrt(spread + 1e-06) * gain


def rotate(inputs, position):
    half_width = inputs.shape[-1] // 2
    inverse = 500000.0 ** (-jnp.arange(half_width, dtype=jnp.float32) * 2.0 / inputs.shape[-1])
    angles = position.astype(jnp.float32)[:, None] * inverse[None, :]
    cosine = jnp.cos(angles)[:, None, :]
    sine = jnp.sin(angles)[:, None, :]
    first = inputs[..., :half_width]
    second = inputs[..., half_width:]
    return jnp.concatenate(
        [first * cosine - second * sine, second * cosine + first * sine], axis=-1
    )


def request_info(row_index, req_lengths):
    ends_at = jnp.cumsum(req_lengths)
    starts_at = ends_at - req_lengths
    request_id = jnp.sum((row_index[:, None] >= ends_at[None, :]).astype(jnp.int32), axis=1)
    choose = request_id[:, None] == jnp.arange(req_lengths.shape[0], dtype=jnp.int32)[None, :]
    request_begin = jnp.sum(jnp.where(choose, starts_at[None, :], 0), axis=1)
    return (request_id, request_begin)


def flash_kernel(needed_ref, q_ref, k_ref, v_ref, qid_ref, qreq_ref, kid_ref, kreq_ref, o_ref,
                 max_ref, sum_ref, acc_ref, *, root):
    kb = pl.program_id(0)
    groups = q_ref.shape[0]

    @pl.when(kb == 0)
    def _():
        max_ref[...] = jnp.full(max_ref.shape, -1e30, jnp.float32)
        sum_ref[...] = jnp.zeros(sum_ref.shape, jnp.float32)
        acc_ref[...] = jnp.zeros(acc_ref.shape, jnp.float32)

    @pl.when(needed_ref[kb] != 0)
    def _():
        allowed = (kid_ref[...] <= qid_ref[...]) & (kreq_ref[...] == qreq_ref[...])
        for g in range(groups):
            scores = lax.dot_general(
                q_ref[g], k_ref[:, g * HD : (g + 1) * HD], (((1,), (1,)), ((), ())),
                preferred_element_type=jnp.float32,
            ) / root
            scores = jnp.where(allowed, scores, -1e30)
            old_max = max_ref[g]
            new_max = jnp.maximum(old_max, jnp.max(scores, axis=1, keepdims=True))
            weights = jnp.where(allowed, jnp.exp(scores - new_max), 0.0)
            scale = jnp.exp(old_max - new_max)
            sum_ref[g] = sum_ref[g] * scale + jnp.sum(weights, axis=1, keepdims=True)
            acc_ref[g] = acc_ref[g] * scale + jnp.dot(
                weights.astype(jnp.bfloat16), v_ref[:, g * HD : (g + 1) * HD],
                preferred_element_type=jnp.float32,
            )
            max_ref[g] = new_max

    @pl.when(kb == pl.num_programs(0) - 1)
    def _():
        rows = o_ref.shape[0]
        per_group = q_ref.shape[1] // rows
        for g in range(groups):
            for head in range(per_group):
                part = slice(head * rows, (head + 1) * rows)
                col = (g * per_group + head) * HD
                o_ref[:, col : col + HD] = (acc_ref[g, part, :] / sum_ref[g, part, :]).astype(
                    o_ref.dtype
                )


def flash_attention(needed, grouped_q, gathered, q_ids, q_req, k_ids, k_req, groups, tok_rows, root):
    blocks = gathered.shape[0]
    group_rows = grouped_q.shape[1]
    width = groups * HD
    grid_spec = pltpu.PrefetchScalarGridSpec(
        num_scalar_prefetch=1,
        grid=(blocks,),
        in_specs=[
            pl.BlockSpec((groups, group_rows, HD), lambda kb, n: (0, 0, 0)),
            pl.BlockSpec((None, tok_rows, width), lambda kb, n: (kb, 0, 0)),
            pl.BlockSpec((None, tok_rows, width), lambda kb, n: (kb, 0, 1)),
            pl.BlockSpec((group_rows, 1), lambda kb, n: (0, 0)),
            pl.BlockSpec((group_rows, 1), lambda kb, n: (0, 0)),
            pl.BlockSpec((None, 1, tok_rows), lambda kb, n: (kb, 0, 0)),
            pl.BlockSpec((None, 1, tok_rows), lambda kb, n: (kb, 0, 0)),
        ],
        out_specs=pl.BlockSpec((tok_rows, groups * group_rows // tok_rows * HD), lambda kb, n: (0, 0)),
        scratch_shapes=[
            pltpu.VMEM((groups, group_rows, 1), jnp.float32),
            pltpu.VMEM((groups, group_rows, 1), jnp.float32),
            pltpu.VMEM((groups, group_rows, HD), jnp.float32),
        ],
    )
    flops = 4 * groups * blocks * group_rows * tok_rows * HD
    return pl.pallas_call(
        functools.partial(flash_kernel, root=root),
        grid_spec=grid_spec,
        out_shape=jax.ShapeDtypeStruct((tok_rows, groups * group_rows // tok_rows * HD), jnp.bfloat16),
        compiler_params=pltpu.CompilerParams(dimension_semantics=("arbitrary",)),
        cost_estimate=pl.CostEstimate(
            flops=flops,
            transcendentals=groups * blocks * group_rows * tok_rows,
            bytes_accessed=2 * groups * blocks * tok_rows * HD * 2 + 4 * groups * group_rows * HD,
        ),
    )(needed, grouped_q, gathered, gathered, q_ids, q_req, k_ids, k_req)


def gather_by_permutes(local, count):
    me = lax.axis_index("kv")
    pieces = [local]
    for shift in range(1, count):
        pieces.append(
            lax.ppermute(local, "kv", perm=[(i, (i + shift) % count) for i in range(count)])
        )
    stacked = jnp.stack(pieces)
    order = (me - jnp.arange(count, dtype=jnp.int32)) % count
    ordered = jnp.take(stacked, order, axis=0)
    return jnp.concatenate([ordered[j] for j in range(count)], axis=1)


def permute_pieces(local, count):
    pieces = [local]
    for shift in range(1, count):
        pieces.append(
            lax.ppermute(local, "kv", perm=[(i, (i + shift) % count) for i in range(count)])
        )
    return pieces


def ordered_sum(pieces, count):
    me = lax.axis_index("kv")
    stacked = jnp.stack([piece.astype(jnp.float32) for piece in pieces])
    order = (me - jnp.arange(count, dtype=jnp.int32)) % count
    return jnp.sum(jnp.take(stacked, order, axis=0), axis=0)


def tree_max(values, axis, count):
    if count & (count - 1):
        return lax.pmax(values, axis)
    step = 1
    while step < count:
        other = lax.ppermute(values, axis, perm=[(i, i ^ step) for i in range(count)])
        values = jnp.maximum(values, other)
        step *= 2
    return values


def on_device(
    patches,
    merged_grid,
    picture_start,
    vis_gain,
    vis_qkv,
    vis_out,
    merge_weight,
    text_embed,
    dec_gain,
    w_query,
    w_keyval,
    w_out,
    req_lengths,
    final_gain,
    table,
):
    pictures, patch_max, vis_width = patches.shape
    merged_max = patch_max // 4
    vis_cols = vis_qkv.shape[2]
    vis_heads = vis_cols // VHD
    tok_rows, feat_dev = text_embed.shape
    kv_count = D // text_embed.shape[1]
    text_rows = gather_by_permutes(text_embed, kv_count)
    inputs = patches.astype(jnp.float32)
    normed = layer_norm(inputs, vis_gain).astype(jnp.bfloat16)
    packed = jnp.einsum(
        "pnd,dce->pnce", normed, vis_qkv, preferred_element_type=jnp.float32
    ).astype(jnp.bfloat16)
    packed = packed.reshape(pictures, patch_max, 3, vis_heads, VHD)
    scores = jnp.einsum(
        "pqhd,pkhd->phqk", packed[:, :, 0], packed[:, :, 1], preferred_element_type=jnp.float32
    ) / math.sqrt(VHD)
    cell_count = merged_grid[:, 0] * merged_grid[:, 1]
    valid_cols = jnp.arange(patch_max, dtype=jnp.int32)[None, :] < 4 * cell_count[:, None]
    scores = jnp.where(valid_cols[:, None, None, :], scores, -1e30)
    weights = jnp.exp(scores - jnp.max(scores, axis=-1, keepdims=True))
    weight_sum = jnp.sum(weights, axis=-1)
    mixed_rows = jnp.einsum(
        "phqk,pkhd->pqhd",
        weights.astype(jnp.bfloat16),
        packed[:, :, 2],
        preferred_element_type=jnp.float32,
    )
    mixed_rows = (
        (mixed_rows / jnp.transpose(weight_sum, (0, 2, 1))[..., None])
        .astype(jnp.bfloat16)
        .reshape(pictures, patch_max, vis_cols)
    )
    head_part = jnp.einsum("pnc,cd->pnd", mixed_rows, vis_out, preferred_element_type=jnp.float32)
    head_pooled = jnp.mean(head_part.reshape(pictures, merged_max, 4, vis_width), axis=2)
    head_total = lax.psum(head_pooled.astype(jnp.bfloat16), "kv").astype(jnp.float32)
    input_pooled = jnp.mean(inputs.reshape(pictures, merged_max, 4, vis_width), axis=2)
    pooled = (input_pooled + head_total).astype(jnp.bfloat16)
    merged = jnp.einsum(
        "pmd,de->pme", pooled, merge_weight, preferred_element_type=jnp.float32
    ).astype(jnp.bfloat16)
    me_kv = lax.axis_index("kv")
    out_source, merged = lax.optimization_barrier((w_out, merged))
    weight_pieces = [lax.dynamic_slice_in_dim(out_source, me_kv * feat_dev, feat_dev, 1)]
    for shift in range(1, kv_count):
        payload = lax.dynamic_slice_in_dim(
            out_source, ((me_kv + shift) % kv_count) * feat_dev, feat_dev, 1
        )
        weight_pieces.append(
            lax.ppermute(
                payload, "kv", perm=[(i, (i + shift) % kv_count) for i in range(kv_count)]
            )
        )
    block_base = lax.axis_index("blk") * tok_rows
    slot_index = jnp.arange(merged_max, dtype=jnp.int32)
    target = picture_start[:, None] + slot_index[None, :] - block_base
    target = jnp.where(slot_index[None, :] < cell_count[:, None], target, -1).reshape(-1)
    local_rows = jnp.arange(tok_rows, dtype=jnp.int32)
    one_hot = local_rows[:, None] == target[None, :]
    placed = jnp.dot(
        one_hot.astype(jnp.bfloat16),
        merged.reshape(pictures * merged_max, feat_dev),
        preferred_element_type=jnp.float32,
    )
    is_vision = jnp.any(one_hot, axis=1)
    seq_in = jnp.where(is_vision[:, None], placed.astype(jnp.bfloat16), text_embed)
    merged_rows = lax.all_gather(
        merged.reshape(pictures * merged_max, feat_dev), "kv", axis=1, tiled=True
    )
    placed_rows = jnp.dot(one_hot.astype(jnp.bfloat16), merged_rows, preferred_element_type=jnp.float32)
    full_rows = jnp.where(is_vision[:, None], placed_rows.astype(jnp.bfloat16), text_rows)
    full_float = full_rows.astype(jnp.float32)
    dec_normed = (
        full_float
        * lax.rsqrt(jnp.mean(full_float * full_float, axis=-1, keepdims=True) + 1e-05)
        * dec_gain
    ).astype(jnp.bfloat16)
    per_group = QHEADS // KVHEADS
    kv_heads = w_keyval.shape[2] // HD
    row_ids = block_base + local_rows
    request_id, request_begin = request_info(row_ids, req_lengths)
    position = row_ids - request_begin
    query_proj = jnp.dot(dec_normed, w_query, preferred_element_type=jnp.float32).reshape(
        tok_rows, kv_heads * per_group, HD
    )
    query_proj = (
        rotate(query_proj, position)
        .astype(jnp.bfloat16)
        .reshape(tok_rows, kv_heads * per_group * HD)
    )
    key_value = jnp.einsum("td,dce->tce", dec_normed, w_keyval, preferred_element_type=jnp.float32)
    key_rows = (
        rotate(key_value[:, 0].reshape(tok_rows, kv_heads, HD), position)
        .astype(jnp.bfloat16)
        .reshape(tok_rows, kv_heads * HD)
    )
    value_rows = key_value[:, 1].astype(jnp.bfloat16)
    query_req, query_begin = request_info(row_ids, req_lengths)
    root = math.sqrt(HD)
    reqs = req_lengths.shape[0]
    ends_at = jnp.cumsum(req_lengths)
    last_ids = ends_at - 1
    picker = (local_rows[None, :] == (last_ids - block_base)[:, None]).astype(jnp.bfloat16)
    query_last = jnp.dot(picker, query_proj, preferred_element_type=jnp.float32)
    seq_last = jnp.dot(picker, seq_in, preferred_element_type=jnp.float32)
    extras = jnp.concatenate([query_last, seq_last], axis=1).astype(jnp.bfloat16).reshape(-1)
    kv_width = key_rows.shape[1]
    ship_width = 2 * kv_width
    extra_rows = -(-extras.shape[0] // ship_width)
    extras = jnp.pad(extras, (0, extra_rows * ship_width - extras.shape[0]))
    shipped = jnp.concatenate([key_rows, value_rows], axis=1)
    shipped = jnp.concatenate([shipped, extras.reshape(extra_rows, ship_width)], axis=0)
    gathered = lax.all_gather(shipped, "blk", axis=0, tiled=False)
    gathered, weight_pieces = lax.optimization_barrier((gathered, weight_pieces))
    blocks = gathered.shape[0]
    q_cols = query_proj.shape[1]
    extras_all = gathered[:, tok_rows:].reshape(blocks, -1)[:, : reqs * (q_cols + feat_dev)]
    extras_all = jnp.sum(extras_all.astype(jnp.float32).reshape(blocks, reqs, -1), axis=0)
    query_last = extras_all[:, :q_cols].astype(jnp.bfloat16)
    seq_last = extras_all[:, q_cols:]
    block_index = lax.axis_index("blk")
    first_begin = query_begin[0]
    block_ids = jnp.arange(blocks, dtype=jnp.int32)
    needed = (
        (block_ids <= block_index) & (block_ids * tok_rows + tok_rows - 1 >= first_begin)
    ).astype(jnp.int32)
    group_rows = tok_rows * per_group
    grouped_q = jnp.transpose(
        query_proj.reshape(tok_rows, kv_heads, per_group, HD), (1, 2, 0, 3)
    ).reshape(kv_heads, group_rows, HD)
    q_ids = jnp.tile(row_ids, per_group)[:, None]
    q_req = jnp.tile(query_req, per_group)[:, None]
    all_ids = jnp.arange(blocks * tok_rows, dtype=jnp.int32)
    all_req, unused = request_info(all_ids, req_lengths)
    k_ids = all_ids.reshape(blocks, 1, tok_rows)
    k_req = all_req.reshape(blocks, 1, tok_rows)
    context = flash_attention(
        needed, grouped_q, gathered, q_ids, q_req, k_ids, k_req, kv_heads, tok_rows, root
    )
    all_ids = jnp.arange(blocks * tok_rows, dtype=jnp.int32)
    last_begin = ends_at - req_lengths
    last_allowed = (all_ids[None, :] >= last_begin[:, None]) & (all_ids[None, :] <= last_ids[:, None])
    last_allowed = last_allowed[:, None, :]
    last_parts = []
    for g in range(kv_heads):
        keys_g = gathered[:, :tok_rows, g * HD : (g + 1) * HD].reshape(blocks * tok_rows, HD)
        values_g = gathered[:, :tok_rows, kv_width + g * HD : kv_width + (g + 1) * HD].reshape(
            blocks * tok_rows, HD
        )
        last_q = query_last[:, g * per_group * HD : (g + 1) * per_group * HD].reshape(
            reqs, per_group, HD
        )
        last_scores = (
            jnp.einsum("tqd,kd->tqk", last_q, keys_g, preferred_element_type=jnp.float32) / root
        )
        last_scores = jnp.where(last_allowed, last_scores, -1e30)
        last_max = jnp.max(last_scores, axis=-1)
        last_weights = jnp.where(last_allowed, jnp.exp(last_scores - last_max[..., None]), 0.0)
        last_sum = jnp.sum(last_weights, axis=-1)
        last_mix = jnp.einsum(
            "tqk,kd->tqd",
            last_weights.astype(jnp.bfloat16),
            values_g,
            preferred_element_type=jnp.float32,
        )
        last_parts.append((last_mix / last_sum[..., None]).reshape(reqs, per_group * HD))
    last_context = jnp.concatenate(last_parts, axis=1).astype(jnp.bfloat16)
    out_rows = jnp.concatenate([context, last_context], axis=0)
    context_all = lax.all_gather(out_rows, "kv", axis=0, tiled=False)
    head_sum = None
    for shift, piece in enumerate(weight_pieces):
        source = lax.dynamic_index_in_dim(
            context_all, (me_kv - shift) % kv_count, 0, keepdims=False
        )
        part = jnp.dot(source, piece, preferred_element_type=jnp.float32)
        part = part.astype(jnp.bfloat16).astype(jnp.float32)
        head_sum = part if head_sum is None else head_sum + part
    hidden = (seq_in.astype(jnp.float32) + head_sum[:tok_rows]).astype(jnp.bfloat16)
    chosen = (seq_last + head_sum[tok_rows:]).astype(jnp.bfloat16).astype(jnp.float32)
    square_part = jnp.sum(chosen * chosen, axis=-1)
    scaled = (chosen * final_gain).astype(jnp.bfloat16)
    logit_part = lax.dot_general(
        scaled, table, (((1,), (1,)), ((), ())), preferred_element_type=jnp.float32
    )
    packed_sums = ordered_sum(
        permute_pieces(jnp.concatenate([logit_part, square_part[:, None]], axis=1), kv_count),
        kv_count,
    )
    logit_sum = packed_sums[:, :-1]
    square_sum = packed_sums[:, -1]
    inv_rms = lax.rsqrt(square_sum / D + 1e-05)
    last_norm = (chosen * inv_rms[:, None] * final_gain).astype(jnp.bfloat16)
    local_max = jnp.max(inv_rms[:, None] * logit_sum, axis=-1)
    max_logit = tree_max(local_max, "blk", blocks)
    return (hidden, last_norm, max_logit)


def solution(mesh):
    placed = (
        P("blk", None, None),
        P("blk", None),
        P("blk"),
        P(),
        P(None, None, "kv"),
        P("kv", None),
        P(None, "kv"),
        P("blk", "kv"),
        P(),
        P(None, "kv"),
        P(None, None, "kv"),
        P("kv", None),
        P(),
        P("kv"),
        P("blk", "kv"),
    )
    return jax.shard_map(
        on_device,
        mesh=mesh,
        in_specs=placed,
        out_specs=(P("blk", "kv"), P(None, "kv"), P()),
        check_vma=False,
    )
```

```python
import functools
import math

import jax
import jax.numpy as jnp
from jax import lax
from jax.experimental import pallas as pl
from jax.experimental.pallas import tpu as pltpu
from jax.sharding import PartitionSpec as P

VHD = 88
D = 4096
QHEADS = 16
KVHEADS = 8
HD = 128


def layer_norm(inputs, gain):
    centre = jnp.mean(inputs, axis=-1, keepdims=True)
    centred = inputs - centre
    spread = jnp.mean(centred * centred, axis=-1, keepdims=True)
    return centred * lax.rsqrt(spread + 1e-06) * gain


def rotate(inputs, position):
    half_width = inputs.shape[-1] // 2
    inverse = 500000.0 ** (-jnp.arange(half_width, dtype=jnp.float32) * 2.0 / inputs.shape[-1])
    angles = position.astype(jnp.float32)[:, None] * inverse[None, :]
    cosine = jnp.cos(angles)[:, None, :]
    sine = jnp.sin(angles)[:, None, :]
    first = inputs[..., :half_width]
    second = inputs[..., half_width:]
    return jnp.concatenate(
        [first * cosine - second * sine, second * cosine + first * sine], axis=-1
    )


def request_info(row_index, req_lengths):
    ends_at = jnp.cumsum(req_lengths)
    starts_at = ends_at - req_lengths
    request_id = jnp.sum((row_index[:, None] >= ends_at[None, :]).astype(jnp.int32), axis=1)
    choose = request_id[:, None] == jnp.arange(req_lengths.shape[0], dtype=jnp.int32)[None, :]
    request_begin = jnp.sum(jnp.where(choose, starts_at[None, :], 0), axis=1)
    return (request_id, request_begin)


def flash_kernel(needed_ref, q_ref, k_ref, v_ref, qid_ref, qreq_ref, kid_ref, kreq_ref, o_ref,
                 max_ref, sum_ref, acc_ref, *, root):
    kb = pl.program_id(0)
    groups = q_ref.shape[0]

    @pl.when(kb == 0)
    def _():
        max_ref[...] = jnp.full(max_ref.shape, -1e30, jnp.float32)
        sum_ref[...] = jnp.zeros(sum_ref.shape, jnp.float32)
        acc_ref[...] = jnp.zeros(acc_ref.shape, jnp.float32)

    def step(j):
        allowed = (kid_ref[j] <= qid_ref[...]) & (kreq_ref[j] == qreq_ref[...])
        for g in range(groups):
            scores = lax.dot_general(
                q_ref[g], k_ref[j, :, g * HD : (g + 1) * HD], (((1,), (1,)), ((), ())),
                preferred_element_type=jnp.float32,
            ) / root
            scores = jnp.where(allowed, scores, -1e30)
            old_max = max_ref[g]
            new_max = jnp.maximum(old_max, jnp.max(scores, axis=1, keepdims=True))
            weights = jnp.where(allowed, jnp.exp(scores - new_max), 0.0)
            scale = jnp.exp(old_max - new_max)
            sum_ref[g] = sum_ref[g] * scale + jnp.sum(weights, axis=1, keepdims=True)
            acc_ref[g] = acc_ref[g] * scale + jnp.dot(
                weights.astype(jnp.bfloat16), v_ref[j, :, g * HD : (g + 1) * HD],
                preferred_element_type=jnp.float32,
            )
            max_ref[g] = new_max

    for j in range(k_ref.shape[0]):
        pl.when(needed_ref[kb * k_ref.shape[0] + j] != 0)(functools.partial(step, j))

    @pl.when(kb == pl.num_programs(0) - 1)
    def _():
        rows = o_ref.shape[0]
        per_group = q_ref.shape[1] // rows
        for g in range(groups):
            for head in range(per_group):
                part = slice(head * rows, (head + 1) * rows)
                col = (g * per_group + head) * HD
                o_ref[:, col : col + HD] = (acc_ref[g, part, :] / sum_ref[g, part, :]).astype(
                    o_ref.dtype
                )


def flash_attention(needed, grouped_q, gathered, q_ids, q_req, k_ids, k_req, groups, tok_rows, root):
    blocks = gathered.shape[0]
    group_rows = grouped_q.shape[1]
    width = groups * HD
    pair = 2 if blocks % 2 == 0 else 1
    grid_spec = pltpu.PrefetchScalarGridSpec(
        num_scalar_prefetch=1,
        grid=(blocks // pair,),
        in_specs=[
            pl.BlockSpec((groups, group_rows, HD), lambda kb, n: (0, 0, 0)),
            pl.BlockSpec((pair, tok_rows, width), lambda kb, n: (kb, 0, 0)),
            pl.BlockSpec((pair, tok_rows, width), lambda kb, n: (kb, 0, 1)),
            pl.BlockSpec((group_rows, 1), lambda kb, n: (0, 0)),
            pl.BlockSpec((group_rows, 1), lambda kb, n: (0, 0)),
            pl.BlockSpec((pair, 1, tok_rows), lambda kb, n: (kb, 0, 0)),
            pl.BlockSpec((pair, 1, tok_rows), lambda kb, n: (kb, 0, 0)),
        ],
        out_specs=pl.BlockSpec((tok_rows, groups * group_rows // tok_rows * HD), lambda kb, n: (0, 0)),
        scratch_shapes=[
            pltpu.VMEM((groups, group_rows, 1), jnp.float32),
            pltpu.VMEM((groups, group_rows, 1), jnp.float32),
            pltpu.VMEM((groups, group_rows, HD), jnp.float32),
        ],
    )
    flops = 4 * groups * blocks * group_rows * tok_rows * HD
    return pl.pallas_call(
        functools.partial(flash_kernel, root=root),
        grid_spec=grid_spec,
        out_shape=jax.ShapeDtypeStruct((tok_rows, groups * group_rows // tok_rows * HD), jnp.bfloat16),
        compiler_params=pltpu.CompilerParams(dimension_semantics=("arbitrary",)),
        cost_estimate=pl.CostEstimate(
            flops=flops,
            transcendentals=groups * blocks * group_rows * tok_rows,
            bytes_accessed=2 * groups * blocks * tok_rows * HD * 2 + 4 * groups * group_rows * HD,
        ),
    )(needed, grouped_q, gathered, gathered, q_ids, q_req, k_ids, k_req)


def gather_by_permutes(local, count):
    me = lax.axis_index("kv")
    pieces = [local]
    for shift in range(1, count):
        pieces.append(
            lax.ppermute(local, "kv", perm=[(i, (i + shift) % count) for i in range(count)])
        )
    stacked = jnp.stack(pieces)
    order = (me - jnp.arange(count, dtype=jnp.int32)) % count
    ordered = jnp.take(stacked, order, axis=0)
    return jnp.concatenate([ordered[j] for j in range(count)], axis=1)


def permute_pieces(local, count):
    pieces = [local]
    for shift in range(1, count):
        pieces.append(
            lax.ppermute(local, "kv", perm=[(i, (i + shift) % count) for i in range(count)])
        )
    return pieces


def ordered_sum(pieces, count):
    me = lax.axis_index("kv")
    stacked = jnp.stack([piece.astype(jnp.float32) for piece in pieces])
    order = (me - jnp.arange(count, dtype=jnp.int32)) % count
    return jnp.sum(jnp.take(stacked, order, axis=0), axis=0)


def tree_max(values, axis, count):
    if count & (count - 1):
        return lax.pmax(values, axis)
    step = 1
    while step < count:
        other = lax.ppermute(values, axis, perm=[(i, i ^ step) for i in range(count)])
        values = jnp.maximum(values, other)
        step *= 2
    return values


def on_device(
    patches,
    merged_grid,
    picture_start,
    vis_gain,
    vis_qkv,
    vis_out,
    merge_weight,
    text_embed,
    dec_gain,
    w_query,
    w_keyval,
    w_out,
    req_lengths,
    final_gain,
    table,
):
    pictures, patch_max, vis_width = patches.shape
    merged_max = patch_max // 4
    vis_cols = vis_qkv.shape[2]
    vis_heads = vis_cols // VHD
    tok_rows, feat_dev = text_embed.shape
    kv_count = D // text_embed.shape[1]
    text_rows = gather_by_permutes(text_embed, kv_count)
    inputs = patches.astype(jnp.float32)
    normed = layer_norm(inputs, vis_gain).astype(jnp.bfloat16)
    packed = jnp.einsum(
        "pnd,dce->pnce", normed, vis_qkv, preferred_element_type=jnp.float32
    ).astype(jnp.bfloat16)
    packed = packed.reshape(pictures, patch_max, 3, vis_heads, VHD)
    scores = jnp.einsum(
        "pqhd,pkhd->phqk", packed[:, :, 0], packed[:, :, 1], preferred_element_type=jnp.float32
    ) / math.sqrt(VHD)
    cell_count = merged_grid[:, 0] * merged_grid[:, 1]
    valid_cols = jnp.arange(patch_max, dtype=jnp.int32)[None, :] < 4 * cell_count[:, None]
    scores = jnp.where(valid_cols[:, None, None, :], scores, -1e30)
    weights = jnp.exp(scores - jnp.max(scores, axis=-1, keepdims=True))
    weight_sum = jnp.sum(weights, axis=-1)
    mixed_rows = jnp.einsum(
        "phqk,pkhd->pqhd",
        weights.astype(jnp.bfloat16),
        packed[:, :, 2],
        preferred_element_type=jnp.float32,
    )
    mixed_rows = (
        (mixed_rows / jnp.transpose(weight_sum, (0, 2, 1))[..., None])
        .astype(jnp.bfloat16)
        .reshape(pictures, patch_max, vis_cols)
    )
    head_part = jnp.einsum("pnc,cd->pnd", mixed_rows, vis_out, preferred_element_type=jnp.float32)
    head_pooled = jnp.mean(head_part.reshape(pictures, merged_max, 4, vis_width), axis=2)
    head_total = lax.psum(head_pooled.astype(jnp.bfloat16), "kv").astype(jnp.float32)
    input_pooled = jnp.mean(inputs.reshape(pictures, merged_max, 4, vis_width), axis=2)
    pooled = (input_pooled + head_total).astype(jnp.bfloat16)
    merged = jnp.einsum(
        "pmd,de->pme", pooled, merge_weight, preferred_element_type=jnp.float32
    ).astype(jnp.bfloat16)
    me_kv = lax.axis_index("kv")
    out_source, merged = lax.optimization_barrier((w_out, merged))
    weight_pieces = [lax.dynamic_slice_in_dim(out_source, me_kv * feat_dev, feat_dev, 1)]
    for shift in range(1, kv_count):
        payload = lax.dynamic_slice_in_dim(
            out_source, ((me_kv + shift) % kv_count) * feat_dev, feat_dev, 1
        )
        weight_pieces.append(
            lax.ppermute(
                payload, "kv", perm=[(i, (i + shift) % kv_count) for i in range(kv_count)]
            )
        )
    block_base = lax.axis_index("blk") * tok_rows
    slot_index = jnp.arange(merged_max, dtype=jnp.int32)
    target = picture_start[:, None] + slot_index[None, :] - block_base
    target = jnp.where(slot_index[None, :] < cell_count[:, None], target, -1).reshape(-1)
    local_rows = jnp.arange(tok_rows, dtype=jnp.int32)
    one_hot = local_rows[:, None] == target[None, :]
    placed = jnp.dot(
        one_hot.astype(jnp.bfloat16),
        merged.reshape(pictures * merged_max, feat_dev),
        preferred_element_type=jnp.float32,
    )
    is_vision = jnp.any(one_hot, axis=1)
    seq_in = jnp.where(is_vision[:, None], placed.astype(jnp.bfloat16), text_embed)
    merged_rows = lax.all_gather(
        merged.reshape(pictures * merged_max, feat_dev), "kv", axis=1, tiled=True
    )
    placed_rows = jnp.dot(one_hot.astype(jnp.bfloat16), merged_rows, preferred_element_type=jnp.float32)
    full_rows = jnp.where(is_vision[:, None], placed_rows.astype(jnp.bfloat16), text_rows)
    full_float = full_rows.astype(jnp.float32)
    dec_normed = (
        full_float
        * lax.rsqrt(jnp.mean(full_float * full_float, axis=-1, keepdims=True) + 1e-05)
        * dec_gain
    ).astype(jnp.bfloat16)
    per_group = QHEADS // KVHEADS
    kv_heads = w_keyval.shape[2] // HD
    row_ids = block_base + local_rows
    request_id, request_begin = request_info(row_ids, req_lengths)
    position = row_ids - request_begin
    query_proj = jnp.dot(dec_normed, w_query, preferred_element_type=jnp.float32).reshape(
        tok_rows, kv_heads * per_group, HD
    )
    query_proj = (
        rotate(query_proj, position)
        .astype(jnp.bfloat16)
        .reshape(tok_rows, kv_heads * per_group * HD)
    )
    key_value = jnp.einsum("td,dce->tce", dec_normed, w_keyval, preferred_element_type=jnp.float32)
    key_rows = (
        rotate(key_value[:, 0].reshape(tok_rows, kv_heads, HD), position)
        .astype(jnp.bfloat16)
        .reshape(tok_rows, kv_heads * HD)
    )
    value_rows = key_value[:, 1].astype(jnp.bfloat16)
    query_req, query_begin = request_info(row_ids, req_lengths)
    root = math.sqrt(HD)
    reqs = req_lengths.shape[0]
    ends_at = jnp.cumsum(req_lengths)
    last_ids = ends_at - 1
    picker = (local_rows[None, :] == (last_ids - block_base)[:, None]).astype(jnp.bfloat16)
    query_last = jnp.dot(picker, query_proj, preferred_element_type=jnp.float32)
    seq_last = jnp.dot(picker, seq_in, preferred_element_type=jnp.float32)
    extras = jnp.concatenate([query_last, seq_last], axis=1).astype(jnp.bfloat16).reshape(-1)
    kv_width = key_rows.shape[1]
    ship_width = 2 * kv_width
    extra_rows = -(-extras.shape[0] // ship_width)
    extras = jnp.pad(extras, (0, extra_rows * ship_width - extras.shape[0]))
    shipped = jnp.concatenate([key_rows, value_rows], axis=1)
    shipped = jnp.concatenate([shipped, extras.reshape(extra_rows, ship_width)], axis=0)
    gathered = lax.all_gather(shipped, "blk", axis=0, tiled=False)
    gathered, weight_pieces = lax.optimization_barrier((gathered, weight_pieces))
    blocks = gathered.shape[0]
    q_cols = query_proj.shape[1]
    extras_all = gathered[:, tok_rows:].reshape(blocks, -1)[:, : reqs * (q_cols + feat_dev)]
    extras_all = jnp.sum(extras_all.astype(jnp.float32).reshape(blocks, reqs, -1), axis=0)
    query_last = extras_all[:, :q_cols].astype(jnp.bfloat16)
    seq_last = extras_all[:, q_cols:]
    block_index = lax.axis_index("blk")
    first_begin = query_begin[0]
    block_ids = jnp.arange(blocks, dtype=jnp.int32)
    needed = (
        (block_ids <= block_index) & (block_ids * tok_rows + tok_rows - 1 >= first_begin)
    ).astype(jnp.int32)
    group_rows = tok_rows * per_group
    grouped_q = jnp.transpose(
        query_proj.reshape(tok_rows, kv_heads, per_group, HD), (1, 2, 0, 3)
    ).reshape(kv_heads, group_rows, HD)
    q_ids = jnp.tile(row_ids, per_group)[:, None]
    q_req = jnp.tile(query_req, per_group)[:, None]
    all_ids = jnp.arange(blocks * tok_rows, dtype=jnp.int32)
    all_req, unused = request_info(all_ids, req_lengths)
    k_ids = all_ids.reshape(blocks, 1, tok_rows)
    k_req = all_req.reshape(blocks, 1, tok_rows)
    context = flash_attention(
        needed, grouped_q, gathered, q_ids, q_req, k_ids, k_req, kv_heads, tok_rows, root
    )
    all_ids = jnp.arange(blocks * tok_rows, dtype=jnp.int32)
    last_begin = ends_at - req_lengths
    last_allowed = (all_ids[None, :] >= last_begin[:, None]) & (all_ids[None, :] <= last_ids[:, None])
    last_allowed = last_allowed[:, None, :]
    last_parts = []
    for g in range(kv_heads):
        keys_g = gathered[:, :tok_rows, g * HD : (g + 1) * HD].reshape(blocks * tok_rows, HD)
        values_g = gathered[:, :tok_rows, kv_width + g * HD : kv_width + (g + 1) * HD].reshape(
            blocks * tok_rows, HD
        )
        last_q = query_last[:, g * per_group * HD : (g + 1) * per_group * HD].reshape(
            reqs, per_group, HD
        )
        last_scores = (
            jnp.einsum("tqd,kd->tqk", last_q, keys_g, preferred_element_type=jnp.float32) / root
        )
        last_scores = jnp.where(last_allowed, last_scores, -1e30)
        last_max = jnp.max(last_scores, axis=-1)
        last_weights = jnp.where(last_allowed, jnp.exp(last_scores - last_max[..., None]), 0.0)
        last_sum = jnp.sum(last_weights, axis=-1)
        last_mix = jnp.einsum(
            "tqk,kd->tqd",
            last_weights.astype(jnp.bfloat16),
            values_g,
            preferred_element_type=jnp.float32,
        )
        last_parts.append((last_mix / last_sum[..., None]).reshape(reqs, per_group * HD))
    last_context = jnp.concatenate(last_parts, axis=1).astype(jnp.bfloat16)
    out_rows = jnp.concatenate([context, last_context], axis=0)
    context_all = lax.all_gather(out_rows, "kv", axis=0, tiled=False)
    head_sum = None
    for shift, piece in enumerate(weight_pieces):
        source = lax.dynamic_index_in_dim(
            context_all, (me_kv - shift) % kv_count, 0, keepdims=False
        )
        part = jnp.dot(source, piece, preferred_element_type=jnp.float32)
        part = part.astype(jnp.bfloat16).astype(jnp.float32)
        head_sum = part if head_sum is None else head_sum + part
    hidden = (seq_in.astype(jnp.float32) + head_sum[:tok_rows]).astype(jnp.bfloat16)
    chosen = (seq_last + head_sum[tok_rows:]).astype(jnp.bfloat16).astype(jnp.float32)
    square_part = jnp.sum(chosen * chosen, axis=-1)
    scaled = (chosen * final_gain).astype(jnp.bfloat16)
    logit_part = lax.dot_general(
        scaled, table, (((1,), (1,)), ((), ())), preferred_element_type=jnp.float32
    )
    packed_sums = ordered_sum(
        permute_pieces(jnp.concatenate([logit_part, square_part[:, None]], axis=1), kv_count),
        kv_count,
    )
    logit_sum = packed_sums[:, :-1]
    square_sum = packed_sums[:, -1]
    inv_rms = lax.rsqrt(square_sum / D + 1e-05)
    last_norm = (chosen * inv_rms[:, None] * final_gain).astype(jnp.bfloat16)
    local_max = jnp.max(inv_rms[:, None] * logit_sum, axis=-1)
    max_logit = tree_max(local_max, "blk", blocks)
    return (hidden, last_norm, max_logit)


def solution(mesh):
    placed = (
        P("blk", None, None),
        P("blk", None),
        P("blk"),
        P(),
        P(None, None, "kv"),
        P("kv", None),
        P(None, "kv"),
        P("blk", "kv"),
        P(),
        P(None, "kv"),
        P(None, None, "kv"),
        P("kv", None),
        P(),
        P("kv"),
        P("blk", "kv"),
    )
    return jax.shard_map(
        on_device,
        mesh=mesh,
        in_specs=placed,
        out_specs=(P("blk", "kv"), P(None, "kv"), P()),
        check_vma=False,
    )
```
